256 devices in a mesh: lat: 8 (over y_hi, x), lon: 32 (over y_lo, z, core).
Axes of the slice: x: 4, y: 4 (y_hi: 2, y_lo: 2; y = y_hi * 2 + y_lo), z: 8, core: 2. Of those that a mesh axis runs over, the one named last changes fastest.
Arguments:
- thickness: float32 [8, 256, 4096], P(None, 'lat', 'lon'), may hold values from 0.5 to 1.5
- winds: float32 [2, 8, 256, 4096], P(None, None, 'lat', 'lon'), may hold values from -2.5 to 2.5
- tracer_mass: float32 [8, 8, 256, 4096], P(None, None, 'lat', 'lon'), may hold values from -6 to 6
Outputs:
- thickness_out: float32 [8, 256, 4096], P(None, 'lat', 'lon')
- winds_out: float32 [2, 8, 256, 4096], P(None, None, 'lat', 'lon')
- tracer_out: float32 [8, 8, 256, 4096], P(None, None, 'lat', 'lon')
The draws below stay inside these ranges and needn't reach their ends.
All inputs are finite; a program needn't handle non-finite values.
Results may differ from the reference program's by a relative error of at most 0.0003.
Values sent between devices are 32-bit elements; how exact they have to be, the bound alone decides.
No kernel may reach another device: no remote copies, remote signals or barrier semaphores. Data moves between devices by JAX's collectives and lax.ppermute only.
A program may use at most 64 MiB of HBM per device.

```python
import math
import jax
import jax.numpy as jnp
from jax import lax

LEV = 8
NTR = 8
SUBSTEPS = 2
NLAT = 256
NLON = 4096


def shard_levels(rng, dims, shards, least, high):
    def one(axis_at, shards_of):
        heights = jax.random.uniform(jax.random.fold_in(jax.random.fold_in(rng, 6), axis_at), (shards_of,), jnp.float32, least / len(shards), high / len(shards))
        return jnp.repeat(jnp.exp(heights), dims[axis_at] // shards_of).reshape((-1,) + (1,) * (len(dims) - axis_at - 1))

    factor_of = one(*shards[0])
    for cut in shards[1:]:
        factor_of = factor_of * one(*cut)
    return factor_of


def noise(stream_key, extent, spread, reach, split=(), held_as=jnp.bfloat16):
    drawn = jax.random.normal(stream_key, extent, jnp.float32) * spread
    if len(split) > 0:
        drawn = shard_levels(stream_key, extent, split, -0.22, 0.18) * drawn
    return jnp.clip(drawn, min=-reach, max=reach).astype(held_as)


def setup_inputs(seed: int = 0) -> dict:
    key_of = jax.random.split(jax.random.key(seed), 4)
    return {
        "thickness": jnp.clip(0.5 + 1.0 * jax.random.uniform(key_of[0], (LEV, NLAT, NLON), jnp.float32) ** shard_levels(key_of[0], (LEV, NLAT, NLON), ((1, 8), (2, 32)), -0.2, 0.2), 0.5, 1.5),
        "winds": noise(key_of[1], (2, LEV, NLAT, NLON), 0.5, 2.5, ((2, 8), (3, 32)), jnp.float32),
        "tracer_mass": noise(key_of[2], (NTR, LEV, NLAT, NLON), 1.0, 6.0, ((2, 8), (3, 32)), jnp.float32),
    }


COUR = 0.25
GRAV = 1.0
FCOR = 1.0


def geopot(thick):
    return GRAV * jnp.flip(jnp.cumsum(jnp.flip(thick, 0), 0), 0)


def upwind(face_speed, behind, centre, forward, beyond):
    return face_speed * jnp.where(face_speed >= 0.0, 5.0 * centre + 2.0 * forward - behind, 5.0 * forward + 2.0 * centre - beyond) / 6.0


def advance(padded, potential, row_start, spacing):
    height = padded.shape[-2]
    columns = padded.shape[-1]
    row_index = (jnp.arange(height) + row_start).astype(jnp.float32)
    center_lat = (row_index[2:height - 2] + 0.5) * spacing - 0.5 * math.pi
    face_lat = (row_index[1:height - 2] + 1.0) * spacing - 0.5 * math.pi
    center_cos = jnp.cos(center_lat)[:, None]
    face_cos = jnp.abs(jnp.cos(face_lat))[:, None]
    coriolis = FCOR * jnp.sin(center_lat)[:, None] * jnp.where(center_cos >= 0.0, 1.0, -1.0)
    band_rows = padded[..., 2:height - 2, :]
    zonal_wind = band_rows[1]
    face_speed = COUR * 0.5 * (zonal_wind[..., 1:columns - 2] + zonal_wind[..., 2:columns - 1])
    zonal_flux = upwind(face_speed, band_rows[..., 0:columns - 3], band_rows[..., 1:columns - 2], band_rows[..., 2:columns - 1], band_rows[..., 3:columns])
    zonal_div = zonal_flux[..., 1:] - zonal_flux[..., :-1]
    column_strip = padded[..., 2:columns - 2]
    merid_wind = column_strip[2]
    merid_speed = COUR * 0.5 * (merid_wind[..., 1:height - 2, :] + merid_wind[..., 2:height - 1, :]) * face_cos
    merid_flux = upwind(merid_speed, column_strip[..., 0:height - 3, :], column_strip[..., 1:height - 2, :], column_strip[..., 2:height - 1, :], column_strip[..., 3:height, :])
    merid_div = (merid_flux[..., 1:, :] - merid_flux[..., :-1, :]) / jnp.abs(center_cos)
    center = padded[..., 2:height - 2, 2:columns - 2]
    advected = center - zonal_div - merid_div
    push_x = COUR * 0.5 * (potential[..., 2:height - 2, 3:columns - 1] - potential[..., 2:height - 2, 1:columns - 3])
    push_y = COUR * 0.5 * (potential[..., 3:height - 1, 2:columns - 2] - potential[..., 1:height - 3, 2:columns - 2])
    east_wind = advected[1] - push_x + COUR * coriolis * center[2]
    north_wind = advected[2] - push_y - COUR * coriolis * center[1]
    return jnp.concatenate([advected[0:1], east_wind[None], north_wind[None], advected[3:]], 0)


def global_pad(field, sign_vector, margin):
    half = field.shape[-1] // 2
    south_rows = jnp.roll(jnp.flip(field[..., 0:margin, :], -2), -half, -1) * sign_vector
    north_rows = jnp.roll(jnp.flip(field[..., field.shape[-2] - margin:, :], -2), -half, -1) * sign_vector
    tall = jnp.concatenate([south_rows, field, north_rows], -2)
    return jnp.concatenate([tall[..., -margin:], tall, tall[..., :margin]], -1)


def reference(thickness, winds, tracer_mass):
    fields = jnp.concatenate([thickness[None], winds, tracer_mass], 0)
    count = fields.shape[0]
    spacing = math.pi / fields.shape[2]
    sign_vector = jnp.where(jnp.arange(count) == 2, -1.0, 1.0).astype(jnp.float32)[:, None, None]
    for substep in range(SUBSTEPS):
        potential = geopot(fields[0])

        def one_level(level):
            layer = lax.dynamic_index_in_dim(fields, level, 1, keepdims=False)
            level_pot = lax.dynamic_index_in_dim(potential, level, 0, keepdims=False)
            return advance(global_pad(layer, sign_vector, 2), global_pad(level_pot, jnp.float32(1.0), 2), -2, spacing)

        fields = jnp.moveaxis(lax.map(one_level, jnp.arange(LEV, dtype=jnp.int32)), 0, 1)
    return fields[0], fields[1:3], fields[3:]
```

```python
import math

import jax
import jax.numpy as jnp
from jax import lax
from jax.experimental import pallas as pl
from jax.experimental.pallas import tpu as pltpu
from jax.sharding import PartitionSpec as P

SUBSTEPS = 2
COUR = 0.25
GRAV = 1.0
FCOR = 1.0

HALO = 2 * SUBSTEPS
STRIP = 4 * HALO


def _lroll(x, k):
    n = x.shape[-1]
    return pltpu.roll(x, k % n, x.ndim - 1)


def _rroll(x, k):
    n = x.shape[-2]
    return pltpu.roll(x, k % n, x.ndim - 2)


def _upwind(speed, pos, behind, centre, forward, beyond):
    return (
        speed
        * jnp.where(pos, 5.0 * centre + 2.0 * forward - behind, 5.0 * forward + 2.0 * centre - beyond)
        / 6.0
    )


def _substep(load, store, nf, pot, fcos, acos, cor):
    u = load(1)
    v = load(2)
    fs = COUR * 0.5 * (u + _lroll(u, -1))
    ms = COUR * 0.5 * (v + _rroll(v, -1)) * fcos
    fpos = fs >= 0.0
    mpos = ms >= 0.0
    for f in range(nf):
        x = u if f == 1 else (v if f == 2 else load(f))
        zf = _upwind(fs, fpos, _lroll(x, 1), x, _lroll(x, -1), _lroll(x, -2))
        mf = _upwind(ms, mpos, _rroll(x, 1), x, _rroll(x, -1), _rroll(x, -2))
        new = x - (zf - _lroll(zf, 1)) - (mf - _rroll(mf, 1)) / acos
        if f == 1:
            new = new - COUR * 0.5 * (_lroll(pot, -1) - _lroll(pot, 1)) + COUR * cor * v
        elif f == 2:
            new = new - COUR * 0.5 * (_rroll(pot, -1) - _rroll(pot, 1)) - COUR * cor * u
        store(f, new)


def _suffix_packed(h, group, ngroups):
    s = h
    k = 1
    while k < ngroups:
        s = s + jnp.where(group + k < ngroups, _lroll(s, -STRIP * k), 0.0)
        k *= 2
    return GRAV * s


def _fix_edges(x, g, lev, lane):
    w = x.shape[-1]
    base = STRIP * lev
    lo = _lroll(g, -(base + HALO))
    hi = _lroll(g, (w - 2) - (base + 2 * HALO + 2))
    return jnp.where(lane < 2, lo, jnp.where(lane >= w - 2, hi, x))


def _kernel(s_ref, g_ref, fcos_ref, acos_ref, cor_ref, thk_ref, wind_ref, trc_ref, s1_ref, g1_ref, p_ref):
    nf, nlev, rows, w = s_ref.shape
    fcos = fcos_ref[...]
    acos = acos_ref[...]
    cor = cor_ref[...]
    lane = lax.broadcasted_iota(jnp.int32, (rows, w), 1)
    group = lane // STRIP
    kk = lane % STRIP

    def set_g1(f, x):
        g1_ref[f] = x

    def potential(src):
        acc = None
        for lev in reversed(range(nlev)):
            acc = src[0, lev] if acc is None else acc + src[0, lev]
            p_ref[lev] = GRAV * acc

    _substep(lambda f: g_ref[f], set_g1, nf, _suffix_packed(g_ref[0], group, nlev), fcos, acos, cor)
    potential(s_ref)
    for lev in range(nlev):

        def store1(f, x, lev=lev):
            s1_ref[f, lev] = _fix_edges(x, g1_ref[f], lev, lane)

        _substep(lambda f, lev=lev: s_ref[f, lev], store1, nf, p_ref[lev], fcos, acos, cor)
    lo_mask = (kk >= HALO) & (kk < 2 * HALO)
    hi_mask = (kk >= 2 * HALO) & (kk < 3 * HALO)
    for f in range(nf):
        g = g1_ref[f]
        for lev in range(nlev):
            m = s1_ref[f, lev]
            base = STRIP * lev
            g = jnp.where((group == lev) & lo_mask, _lroll(m, base + HALO), g)
            g = jnp.where((group == lev) & hi_mask, _lroll(m, base + 2 * HALO - (w - HALO)), g)
        g1_ref[f] = g
    _substep(lambda f: g1_ref[f], set_g1, nf, _suffix_packed(g1_ref[0], group, nlev), fcos, acos, cor)
    potential(s1_ref)
    inner = rows - 2 * HALO
    for lev in range(nlev):

        def store2(f, x, lev=lev):
            x = _fix_edges(x, g1_ref[f], lev, lane)
            x = _rroll(x, -HALO)[:inner]
            if f == 0:
                thk_ref[lev] = x
            elif f < 3:
                wind_ref[f - 1, lev] = x
            else:
                trc_ref[f - 3, lev] = x

        _substep(lambda f, lev=lev: s1_ref[f, lev], store2, nf, p_ref[lev], fcos, acos, cor)


def _shift_pairs(n, d, closed):
    return [(i, (i + d) % n) for i in range(n) if closed or 0 <= i + d < n]


def shards(thickness, winds, tracer_mass):
    fields = jnp.concatenate([thickness[None], winds, tracer_mass], 0)
    nf, nlev, rows, w = fields.shape
    nlat = lax.axis_size("lat")
    nlon = lax.axis_size("lon")
    band = lax.axis_index("lat")
    spacing = math.pi / (rows * nlat)

    top = fields[:, :, rows - HALO :]
    bottom = fields[:, :, :HALO]
    from_south = lax.ppermute(top, "lat", _shift_pairs(nlat, 1, False))
    from_north = lax.ppermute(bottom, "lat", _shift_pairs(nlat, -1, False))
    half = nlon // 2
    pole_pairs = []
    for b in (0, nlat - 1):
        for s in range(nlon):
            pole_pairs.append((b * nlon + s, b * nlon + (s + half) % nlon))
    pole_out = jnp.where(band == 0, bottom, top)
    pole_in = lax.ppermute(pole_out, ("lat", "lon"), pole_pairs)
    sign = jnp.where(jnp.arange(nf) == 2, -1.0, 1.0).astype(jnp.float32)[:, None, None, None]
    mirrored = jnp.flip(pole_in, 2) * sign
    south = jnp.where(band == 0, mirrored, from_south)
    north = jnp.where(band == nlat - 1, mirrored, from_north)
    padded = jnp.concatenate([south, fields, north], 2)

    west_cols = padded[..., :HALO]
    east_cols = padded[..., w - HALO :]
    from_west = lax.ppermute(east_cols, "lon", _shift_pairs(nlon, 1, True))
    from_east = lax.ppermute(west_cols, "lon", _shift_pairs(nlon, -1, True))
    strip = jnp.concatenate([from_west, west_cols, east_cols, from_east], -1)
    tall = rows + 2 * HALO
    packed = jnp.transpose(strip, (0, 2, 1, 3)).reshape(nf, tall, nlev * STRIP)

    row_index = (jnp.arange(tall) + (band * rows - HALO)).astype(jnp.float32)
    center_lat = (row_index + 0.5) * spacing - 0.5 * math.pi
    face_lat = (row_index + 1.0) * spacing - 0.5 * math.pi
    center_cos = jnp.cos(center_lat)
    fcos = jnp.broadcast_to(jnp.abs(jnp.cos(face_lat))[:, None], (tall, w))
    acos = jnp.broadcast_to(jnp.abs(center_cos)[:, None], (tall, w))
    cor = jnp.broadcast_to(
        (FCOR * jnp.sin(center_lat) * jnp.where(center_cos >= 0.0, 1.0, -1.0))[:, None], (tall, w)
    )

    vmem = pl.BlockSpec(memory_space=pltpu.VMEM)
    return pl.pallas_call(
        _kernel,
        out_shape=(
            jax.ShapeDtypeStruct(thickness.shape, jnp.float32),
            jax.ShapeDtypeStruct(winds.shape, jnp.float32),
            jax.ShapeDtypeStruct(tracer_mass.shape, jnp.float32),
        ),
        in_specs=[vmem] * 5,
        out_specs=(vmem, vmem, vmem),
        scratch_shapes=[
            pltpu.VMEM(padded.shape, jnp.float32),
            pltpu.VMEM(packed.shape, jnp.float32),
            pltpu.VMEM((nlev, tall, w), jnp.float32),
        ],
    )(padded, packed, fcos, acos, cor)


def solution(mesh):
    return jax.shard_map(
        shards,
        mesh=mesh,
        in_specs=(P(None, "lat", "lon"), P(None, None, "lat", "lon"), P(None, None, "lat", "lon")),
        out_specs=(P(None, "lat", "lon"), P(None, None, "lat", "lon"), P(None, None, "lat", "lon")),
        check_vma=False,
    )
```

```python
import math

import jax
import jax.numpy as jnp
from jax import lax
from jax.experimental import pallas as pl
from jax.experimental.pallas import tpu as pltpu
from jax.sharding import PartitionSpec as P

SUBSTEPS = 2
COUR = 0.25
GRAV = 1.0
FCOR = 1.0

HALO = 2 * SUBSTEPS
STRIP = 4 * HALO


def _lroll(x, k):
    n = x.shape[-1]
    return pltpu.roll(x, k % n, x.ndim - 1)


def _rroll(x, k):
    n = x.shape[-2]
    return pltpu.roll(x, k % n, x.ndim - 2)


def _upwind(speed, pos, behind, centre, forward, beyond):
    return speed * jnp.where(pos, 5.0 * centre + 2.0 * forward - behind, 5.0 * forward + 2.0 * centre - beyond)


def _substep(load, store, nf, pot, rv):
    fcos, inv_acos, cor = rv
    u = load(1)
    v = load(2)
    fs = (COUR * 0.5 / 6.0) * (u + _lroll(u, -1))
    ms = (COUR * 0.5 / 6.0) * (v + _rroll(v, -1)) * fcos
    fpos = fs >= 0.0
    mpos = ms >= 0.0
    for f in range(nf):
        x = u if f == 1 else (v if f == 2 else load(f))
        zf = _upwind(fs, fpos, _lroll(x, 1), x, _lroll(x, -1), _lroll(x, -2))
        mf = _upwind(ms, mpos, _rroll(x, 1), x, _rroll(x, -1), _rroll(x, -2))
        new = x - (zf - _lroll(zf, 1)) - (mf - _rroll(mf, 1)) * inv_acos
        if f == 1:
            new = new - COUR * 0.5 * (_lroll(pot, -1) - _lroll(pot, 1)) + cor * v
        elif f == 2:
            new = new - COUR * 0.5 * (_rroll(pot, -1) - _rroll(pot, 1)) - cor * u
        store(f, new)


def _suffix_packed(h, group, ngroups):
    s = h
    k = 1
    while k < ngroups:
        s = s + jnp.where(group + k < ngroups, _lroll(s, -STRIP * k), 0.0)
        k *= 2
    return GRAV * s


def _fix_edges(x, g, lev, lane):
    w = x.shape[-1]
    base = STRIP * lev
    lo = _lroll(g, -(base + HALO))
    hi = _lroll(g, (w - 2) - (base + 2 * HALO + 2))
    return jnp.where(lane < 2, lo, jnp.where(lane >= w - 2, hi, x))


def _lanes(rows, w):
    lane = lax.broadcasted_iota(jnp.int32, (rows, w), 1)
    return lane, lane // STRIP, lane % STRIP


def _pack_edges(get, nlev, rows, w, init):
    lane, group, kk = _lanes(rows, w)
    lo_mask = (kk >= HALO) & (kk < 2 * HALO)
    hi_mask = (kk >= 2 * HALO) & (kk < 3 * HALO)
    g = init
    for lev in range(nlev):
        m = get(lev)
        base = STRIP * lev
        g = jnp.where((group == lev) & lo_mask, _lroll(m, base + HALO), g)
        g = jnp.where((group == lev) & hi_mask, _lroll(m, base + 2 * HALO - (w - HALO)), g)
    return g


def _potential(src, p_ref, nlev):
    acc = None
    for lev in reversed(range(nlev)):
        acc = src[0, lev] if acc is None else acc + src[0, lev]
        p_ref[lev] = GRAV * acc


def _edge_kernel(s_ref, e_ref):
    nf, nlev, rows, w = s_ref.shape
    for f in range(nf):
        e_ref[f] = _pack_edges(lambda lev: s_ref[f, lev], nlev, rows, w, jnp.zeros((rows, w), jnp.float32))


def _main1_kernel(s_ref, rv_ref, o_ref, p_ref):
    nf, nlev, rows, w = s_ref.shape
    rv = (rv_ref[0], rv_ref[1], rv_ref[2])
    _potential(s_ref, p_ref, nlev)
    for lev in range(nlev):

        def store(f, x, lev=lev):
            o_ref[f, lev] = x

        _substep(lambda f, lev=lev: s_ref[f, lev], store, nf, p_ref[lev], rv)


def _final_kernel(s1_ref, e_ref, ew_ref, ee_ref, rv_ref, thk_ref, wind_ref, trc_ref, s_ref, g_ref, p_ref):
    nf, nlev, rows, w = s1_ref.shape
    rv = (rv_ref[0], rv_ref[1], rv_ref[2])
    lane, group, kk = _lanes(rows, w)

    def set_g(f, x):
        g_ref[f] = x

    for f in range(nf):
        g_ref[f] = jnp.where(
            kk < HALO, _lroll(ew_ref[f], -2 * HALO), jnp.where(kk >= 3 * HALO, _lroll(ee_ref[f], 2 * HALO), e_ref[f])
        )
    _substep(lambda f: g_ref[f], set_g, nf, _suffix_packed(g_ref[0], group, nlev), rv)
    for f in range(nf):
        g = g_ref[f]
        for lev in range(nlev):
            s_ref[f, lev] = _fix_edges(s1_ref[f, lev], g, lev, lane)
    for f in range(nf):
        g_ref[f] = _pack_edges(lambda lev: s_ref[f, lev], nlev, rows, w, g_ref[f])
    _substep(lambda f: g_ref[f], set_g, nf, _suffix_packed(g_ref[0], group, nlev), rv)
    _potential(s_ref, p_ref, nlev)
    inner = rows - 2 * HALO
    for lev in range(nlev):

        def store2(f, x, lev=lev):
            x = _fix_edges(x, g_ref[f], lev, lane)
            x = _rroll(x, -HALO)[:inner]
            if f == 0:
                thk_ref[lev] = x
            elif f < 3:
                wind_ref[f - 1, lev] = x
            else:
                trc_ref[f - 3, lev] = x

        _substep(lambda f, lev=lev: s_ref[f, lev], store2, nf, p_ref[lev], rv)


def _shift_pairs(n, d, closed):
    return [(i, (i + d) % n) for i in range(n) if closed or 0 <= i + d < n]


def _vmem_call(kernel, out_shape, n_in, scratch, flops, nbytes):
    vmem = pl.BlockSpec(memory_space=pltpu.VMEM)
    return pl.pallas_call(
        kernel,
        out_shape=out_shape,
        in_specs=[vmem] * n_in,
        out_specs=tuple(vmem for _ in out_shape) if isinstance(out_shape, tuple) else vmem,
        scratch_shapes=scratch,
        cost_estimate=pl.CostEstimate(flops=flops, bytes_accessed=nbytes, transcendentals=0),
    )


def shards(thickness, winds, tracer_mass):
    fields = jnp.concatenate([thickness[None], winds, tracer_mass], 0)
    nf, nlev, rows, w = fields.shape
    nlat = lax.axis_size("lat")
    nlon = lax.axis_size("lon")
    band = lax.axis_index("lat")
    spacing = math.pi / (rows * nlat)
    tall = rows + 2 * HALO

    row_index = (jnp.arange(tall) + (band * rows - HALO)).astype(jnp.float32)
    center_lat = (row_index + 0.5) * spacing - 0.5 * math.pi
    face_lat = (row_index + 1.0) * spacing - 0.5 * math.pi
    center_cos = jnp.cos(center_lat)
    rowvec = jnp.stack(
        [
            jnp.abs(jnp.cos(face_lat)),
            1.0 / jnp.abs(center_cos),
            COUR * FCOR * jnp.sin(center_lat) * jnp.where(center_cos >= 0.0, 1.0, -1.0),
        ]
    )
    rowvec = jnp.broadcast_to(rowvec[:, :, None], (3, tall, w))

    top = fields[:, :, rows - HALO :]
    bottom = fields[:, :, :HALO]
    from_south = lax.ppermute(top, "lat", _shift_pairs(nlat, 1, False))
    from_north = lax.ppermute(bottom, "lat", _shift_pairs(nlat, -1, False))
    half = nlon // 2
    pole_pairs = []
    for b in (0, nlat - 1):
        for s in range(nlon):
            pole_pairs.append((b * nlon + s, b * nlon + (s + half) % nlon))
    pole_out = jnp.where(band == 0, bottom, top)
    pole_in = lax.ppermute(pole_out, ("lat", "lon"), pole_pairs)
    sign = jnp.where(jnp.arange(nf) == 2, -1.0, 1.0).astype(jnp.float32)[:, None, None, None]
    mirrored = jnp.flip(pole_in, 2) * sign
    south = jnp.where(band == 0, mirrored, from_south)
    north = jnp.where(band == nlat - 1, mirrored, from_north)
    padded = jnp.concatenate([south, fields, north], 2)

    slab = nf * tall * w * 4
    edges = _vmem_call(_edge_kernel, jax.ShapeDtypeStruct((nf, tall, w), jnp.float32), 1, [], 0, slab * (nlev + 1))(
        padded
    )
    from_west = lax.ppermute(edges, "lon", _shift_pairs(nlon, 1, True))
    from_east = lax.ppermute(edges, "lon", _shift_pairs(nlon, -1, True))

    step_flops = 60 * nf * nlev * tall * w
    main1 = _vmem_call(
        _main1_kernel,
        jax.ShapeDtypeStruct(padded.shape, jnp.float32),
        2,
        [pltpu.VMEM((nlev, tall, w), jnp.float32)],
        step_flops,
        2 * slab * nlev,
    )(padded, rowvec)

    return _vmem_call(
        _final_kernel,
        (
            jax.ShapeDtypeStruct(thickness.shape, jnp.float32),
            jax.ShapeDtypeStruct(winds.shape, jnp.float32),
            jax.ShapeDtypeStruct(tracer_mass.shape, jnp.float32),
        ),
        5,
        [
            pltpu.VMEM(padded.shape, jnp.float32),
            pltpu.VMEM(edges.shape, jnp.float32),
            pltpu.VMEM((nlev, tall, w), jnp.float32),
        ],
        step_flops + 3 * step_flops // nlev,
        2 * slab * nlev,
    )(main1, edges, from_west, from_east, rowvec)


def solution(mesh):
    return jax.shard_map(
        shards,
        mesh=mesh,
        in_specs=(P(None, "lat", "lon"), P(None, None, "lat", "lon"), P(None, None, "lat", "lon")),
        out_specs=(P(None, "lat", "lon"), P(None, None, "lat", "lon"), P(None, None, "lat", "lon")),
        check_vma=False,
    )
```

```python
import math

import jax
import jax.numpy as jnp
from jax import lax
from jax.experimental import pallas as pl
from jax.experimental.pallas import tpu as pltpu
from jax.sharding import PartitionSpec as P

SUBSTEPS = 2
COUR = 0.25
GRAV = 1.0
FCOR = 1.0

HALO = 2 * SUBSTEPS
STRIP = 4 * HALO
MARGIN = 8


def _lroll(x, k):
    n = x.shape[-1]
    return pltpu.roll(x, k % n, x.ndim - 1)


def _face(pos, behind, centre, forward, beyond):
    p = jnp.where(pos, centre, forward)
    q = jnp.where(pos, forward, centre)
    r = jnp.where(pos, behind, beyond)
    return 5.0 * p + 2.0 * q - r


def _substep(load, store, nf, pot, rv, mf_ref):
    fcos, inv_acos, cor = rv
    u = load(1, 0)
    v = load(2, 0)
    n = u.shape[0]
    fs = (COUR * 0.5 / 6.0) * (u + _lroll(u, -1))
    ms = (COUR * 0.5 / 6.0) * (v + load(2, 1)) * fcos
    fpos = fs >= 0.0
    mpos = ms >= 0.0
    for f in range(nf):
        x = u if f == 1 else (v if f == 2 else load(f, 0))
        zf = fs * _face(fpos, _lroll(x, 1), x, _lroll(x, -1), _lroll(x, -2))
        mf = ms * _face(mpos, load(f, -1), x, load(f, 1), load(f, 2))
        mf_ref[f, pl.ds(MARGIN, n)] = mf
        new = x - (zf - _lroll(zf, 1)) - (mf - mf_ref[f, pl.ds(MARGIN - 1, n)]) * inv_acos
        if f == 1:
            p0 = pot(0)
            new = new - COUR * 0.5 * (_lroll(p0, -1) - _lroll(p0, 1)) + cor * v
        elif f == 2:
            new = new - COUR * 0.5 * (pot(1) - pot(-1)) - cor * u
        store(f, new)


def _suffix_packed(h, group, ngroups):
    s = h
    k = 1
    while k < ngroups:
        s = s + jnp.where(group + k < ngroups, _lroll(s, -STRIP * k), 0.0)
        k *= 2
    return GRAV * s


def _fix_edges(x, g, lev, lane):
    w = x.shape[-1]
    base = STRIP * lev
    lo = _lroll(g, -(base + HALO))
    hi = _lroll(g, (w - 2) - (base + 2 * HALO + 2))
    return jnp.where(lane < 2, lo, jnp.where(lane >= w - 2, hi, x))


def _lanes(rows, w):
    lane = lax.broadcasted_iota(jnp.int32, (rows, w), 1)
    return lane, lane // STRIP, lane % STRIP


def _pack_edges(get, nlev, rows, w, init):
    lane, group, kk = _lanes(rows, w)
    lo_mask = (kk >= HALO) & (kk < 2 * HALO)
    hi_mask = (kk >= 2 * HALO) & (kk < 3 * HALO)
    g = init
    for lev in range(nlev):
        m = get(lev)
        base = STRIP * lev
        g = jnp.where((group == lev) & lo_mask, _lroll(m, base + HALO), g)
        g = jnp.where((group == lev) & hi_mask, _lroll(m, base + 2 * HALO - (w - HALO)), g)
    return g


def _potential(thick, p_ref, nlev, n):
    acc = None
    for lev in reversed(range(nlev)):
        acc = thick(lev) if acc is None else acc + thick(lev)
        p_ref[lev, pl.ds(MARGIN, n)] = GRAV * acc


def _edge_kernel(s_ref, e_ref):
    nf, nlev, _, w = s_ref.shape
    rows = e_ref.shape[1]
    for f in range(nf):
        e_ref[f] = _pack_edges(lambda lev: s_ref[f, lev], nlev, rows, w, jnp.zeros((rows, w), jnp.float32))


def _main1_kernel(s_ref, rv_ref, o_ref, p_ref, mf_ref, sp_ref):
    nf, nlev, rows, w = s_ref.shape
    rv = (rv_ref[0], rv_ref[1], rv_ref[2])
    win = pl.ds(MARGIN, rows)
    _potential(lambda lev: s_ref[0, lev], p_ref, nlev, rows)
    for lev in range(nlev):
        sp = sp_ref.at[lev % 2]
        for f in range(nf):
            sp[f, win] = s_ref[f, lev]

        def store(f, x, lev=lev):
            o_ref[f, lev, win] = x

        _substep(
            lambda f, d, sp=sp: sp[f, pl.ds(MARGIN + d, rows)],
            store,
            nf,
            lambda d, lev=lev: p_ref[lev, pl.ds(MARGIN + d, rows)],
            rv,
            mf_ref,
        )


def _final_kernel(
    s1_ref, e_ref, ew_ref, ee_ref, rv_ref, thk_ref, wind_ref, trc_ref, s_ref, g0_ref, g1_ref, g2_ref, p_ref, pg_ref, mf_ref, o2_ref
):
    nf, nlev, _, w = s1_ref.shape
    rows = rv_ref.shape[1]
    inner = rows - 2 * HALO
    rv1 = (rv_ref[0], rv_ref[1], rv_ref[2])
    lane, group, kk = _lanes(rows, w)
    win = pl.ds(MARGIN, rows)

    for f in range(nf):
        g0_ref[f, win] = jnp.where(
            kk < HALO, _lroll(ew_ref[f], -2 * HALO), jnp.where(kk >= 3 * HALO, _lroll(ee_ref[f], 2 * HALO), e_ref[f])
        )
    pg_ref[win] = _suffix_packed(g0_ref[0, win], group, nlev)

    def set_g1(f, x):
        g1_ref[f, win] = x

    _substep(
        lambda f, d: g0_ref[f, pl.ds(MARGIN + d, rows)],
        set_g1,
        nf,
        lambda d: pg_ref[pl.ds(MARGIN + d, rows)],
        rv1,
        mf_ref,
    )
    for f in range(nf):
        g = g1_ref[f, win]
        for lev in range(nlev):
            s_ref[f, lev, win] = _fix_edges(s1_ref[f, lev, win], g, lev, lane)
    for f in range(nf):
        g1_ref[f, win] = _pack_edges(lambda lev: s_ref[f, lev, win], nlev, rows, w, g1_ref[f, win])
    pg_ref[win] = _suffix_packed(g1_ref[0, win], group, nlev)

    def set_g2(f, x):
        g2_ref[f, win] = x

    _substep(
        lambda f, d: g1_ref[f, pl.ds(MARGIN + d, rows)],
        set_g2,
        nf,
        lambda d: pg_ref[pl.ds(MARGIN + d, rows)],
        rv1,
        mf_ref,
    )
    _potential(lambda lev: s_ref[0, lev, win], p_ref, nlev, rows)
    inner_rows = pl.ds(MARGIN + HALO, inner)
    for lev in range(nlev):

        def store2(f, x, lev=lev):
            o2_ref[f, win] = _fix_edges(x, g2_ref[f, win], lev, lane)
            x = o2_ref[f, inner_rows]
            if f == 0:
                thk_ref[lev] = x
            elif f < 3:
                wind_ref[f - 1, lev] = x
            else:
                trc_ref[f - 3, lev] = x

        _substep(
            lambda f, d, lev=lev: s_ref[f, lev, pl.ds(MARGIN + d, rows)],
            store2,
            nf,
            lambda d, lev=lev: p_ref[lev, pl.ds(MARGIN + d, rows)],
            rv1,
            mf_ref,
        )


def _shift_pairs(n, d, closed):
    return [(i, (i + d) % n) for i in range(n) if closed or 0 <= i + d < n]


def _vmem_call(kernel, out_shape, n_in, scratch, flops, nbytes):
    vmem = pl.BlockSpec(memory_space=pltpu.VMEM)
    return pl.pallas_call(
        kernel,
        out_shape=out_shape,
        in_specs=[vmem] * n_in,
        out_specs=tuple(vmem for _ in out_shape) if isinstance(out_shape, tuple) else vmem,
        scratch_shapes=scratch,
        cost_estimate=pl.CostEstimate(flops=flops, bytes_accessed=nbytes, transcendentals=0),
    )


def shards(thickness, winds, tracer_mass):
    fields = jnp.concatenate([thickness[None], winds, tracer_mass], 0)
    nf, nlev, rows, w = fields.shape
    nlat = lax.axis_size("lat")
    nlon = lax.axis_size("lon")
    band = lax.axis_index("lat")
    spacing = math.pi / (rows * nlat)
    tall = rows + 2 * HALO

    row_index = (jnp.arange(tall) + (band * rows - HALO)).astype(jnp.float32)
    center_lat = (row_index + 0.5) * spacing - 0.5 * math.pi
    face_lat = (row_index + 1.0) * spacing - 0.5 * math.pi
    center_cos = jnp.cos(center_lat)
    rowvec = jnp.stack(
        [
            jnp.abs(jnp.cos(face_lat)),
            1.0 / jnp.abs(center_cos),
            COUR * FCOR * jnp.sin(center_lat) * jnp.where(center_cos >= 0.0, 1.0, -1.0),
        ]
    )
    rowvec = jnp.broadcast_to(rowvec[:, :, None], (3, tall, w))

    top = fields[:, :, rows - HALO :]
    bottom = fields[:, :, :HALO]
    from_south = lax.ppermute(top, "lat", _shift_pairs(nlat, 1, False))
    from_north = lax.ppermute(bottom, "lat", _shift_pairs(nlat, -1, False))
    half = nlon // 2
    pole_pairs = []
    for b in (0, nlat - 1):
        for s in range(nlon):
            pole_pairs.append((b * nlon + s, b * nlon + (s + half) % nlon))
    pole_out = jnp.where(band == 0, bottom, top)
    pole_in = lax.ppermute(pole_out, ("lat", "lon"), pole_pairs)
    sign = jnp.where(jnp.arange(nf) == 2, -1.0, 1.0).astype(jnp.float32)[:, None, None, None]
    mirrored = jnp.flip(pole_in, 2) * sign
    south = jnp.where(band == 0, mirrored, from_south)
    north = jnp.where(band == nlat - 1, mirrored, from_north)
    padded = jnp.concatenate([south, fields, north], 2)

    slab = nf * tall * w * 4
    edges = _vmem_call(_edge_kernel, jax.ShapeDtypeStruct((nf, tall, w), jnp.float32), 1, [], 0, 2 * slab * nlev)(
        padded
    )
    from_west = lax.ppermute(edges, "lon", _shift_pairs(nlon, 1, True))
    from_east = lax.ppermute(edges, "lon", _shift_pairs(nlon, -1, True))

    step_flops = 60 * nf * nlev * tall * w
    deep = tall + 2 * MARGIN
    main1 = _vmem_call(
        _main1_kernel,
        jax.ShapeDtypeStruct((nf, nlev, deep, w), jnp.float32),
        2,
        [
            pltpu.VMEM((nlev, deep, w), jnp.float32),
            pltpu.VMEM((nf, deep, w), jnp.float32),
            pltpu.VMEM((2, nf, deep, w), jnp.float32),
        ],
        step_flops,
        2 * slab * nlev,
    )(padded, rowvec)

    return _vmem_call(
        _final_kernel,
        (
            jax.ShapeDtypeStruct(thickness.shape, jnp.float32),
            jax.ShapeDtypeStruct(winds.shape, jnp.float32),
            jax.ShapeDtypeStruct(tracer_mass.shape, jnp.float32),
        ),
        5,
        [
            pltpu.VMEM((nf, nlev, deep, w), jnp.float32),
            pltpu.VMEM((nf, tall + 2 * MARGIN, w), jnp.float32),
            pltpu.VMEM((nf, tall + 2 * MARGIN, w), jnp.float32),
            pltpu.VMEM((nf, tall + 2 * MARGIN, w), jnp.float32),
            pltpu.VMEM((nlev, tall + 2 * MARGIN, w), jnp.float32),
            pltpu.VMEM((tall + 2 * MARGIN, w), jnp.float32),
            pltpu.VMEM((nf, tall + 2 * MARGIN, w), jnp.float32),
            pltpu.VMEM((nf, tall + 2 * MARGIN, w), jnp.float32),
        ],
        step_flops + 3 * step_flops // nlev,
        2 * slab * nlev,
    )(main1, edges, from_west, from_east, rowvec)


def solution(mesh):
    return jax.shard_map(
        shards,
        mesh=mesh,
        in_specs=(P(None, "lat", "lon"), P(None, None, "lat", "lon"), P(None, None, "lat", "lon")),
        out_specs=(P(None, "lat", "lon"), P(None, None, "lat", "lon"), P(None, None, "lat", "lon")),
        check_vma=False,
    )
```

```python
import math

import jax
import jax.numpy as jnp
from jax import lax
from jax.experimental import pallas as pl
from jax.experimental.pallas import tpu as pltpu
from jax.sharding import PartitionSpec as P

SUBSTEPS = 2
COUR = 0.25
GRAV = 1.0
FCOR = 1.0

HALO = 2 * SUBSTEPS
STRIP = 4 * HALO
MARGIN = 8


def _lroll(x, k):
    n = x.shape[-1]
    return pltpu.roll(x, k % n, x.ndim - 1)


def _face(pos, behind, centre, forward, beyond):
    p = jnp.where(pos, centre, forward)
    q = jnp.where(pos, forward, centre)
    r = jnp.where(pos, behind, beyond)
    return 5.0 * p + 2.0 * q - r


def _substep(load, store, nf, pot, rv, mf_ref):
    fcos, inv_acos, cor = rv
    u = load(1, 0)
    v = load(2, 0)
    n = u.shape[0]
    fs = (COUR * 0.5 / 6.0) * (u + _lroll(u, -1))
    ms = (COUR * 0.5 / 6.0) * (v + load(2, 1)) * fcos
    fpos = fs >= 0.0
    mpos = ms >= 0.0
    for f in range(nf):
        x = u if f == 1 else (v if f == 2 else load(f, 0))
        zf = fs * _face(fpos, _lroll(x, 1), x, _lroll(x, -1), _lroll(x, -2))
        mf = ms * _face(mpos, load(f, -1), x, load(f, 1), load(f, 2))
        mf_ref[f, pl.ds(MARGIN, n)] = mf
        new = x - (zf - _lroll(zf, 1)) - (mf - mf_ref[f, pl.ds(MARGIN - 1, n)]) * inv_acos
        if f == 1:
            p0 = pot(0)
            new = new - COUR * 0.5 * (_lroll(p0, -1) - _lroll(p0, 1)) + cor * v
        elif f == 2:
            new = new - COUR * 0.5 * (pot(1) - pot(-1)) - cor * u
        store(f, new)


def _suffix_packed(h, group, ngroups):
    s = h
    k = 1
    while k < ngroups:
        s = s + jnp.where(group + k < ngroups, _lroll(s, -STRIP * k), 0.0)
        k *= 2
    return GRAV * s


def _fix_edges(x, g, lev, lane):
    w = x.shape[-1]
    base = STRIP * lev
    lo = _lroll(g, -(base + HALO))
    hi = _lroll(g, (w - 2) - (base + 2 * HALO + 2))
    return jnp.where(lane < 2, lo, jnp.where(lane >= w - 2, hi, x))


def _lanes(rows, w):
    lane = lax.broadcasted_iota(jnp.int32, (rows, w), 1)
    return lane, lane // STRIP, lane % STRIP


def _pack_edges(get, nlev, rows, w, init):
    lane, group, kk = _lanes(rows, w)
    lo_mask = (kk >= HALO) & (kk < 2 * HALO)
    hi_mask = (kk >= 2 * HALO) & (kk < 3 * HALO)
    g = init
    for lev in range(nlev):
        m = get(lev)
        base = STRIP * lev
        g = jnp.where((group == lev) & lo_mask, _lroll(m, base + HALO), g)
        g = jnp.where((group == lev) & hi_mask, _lroll(m, base + 2 * HALO - (w - HALO)), g)
    return g


def _potential(thick, p_ref, nlev, n):
    acc = None
    for lev in reversed(range(nlev)):
        acc = thick(lev) if acc is None else acc + thick(lev)
        p_ref[lev, pl.ds(MARGIN, n)] = GRAV * acc


def _edge_inner_kernel(thk_ref, wind_ref, trc_ref, e_ref):
    nlev, rows, w = thk_ref.shape
    zeros = jnp.zeros((rows, w), jnp.float32)
    for f in range(e_ref.shape[0]):
        if f == 0:
            get = lambda lev: thk_ref[lev]
        elif f < 3:
            get = lambda lev, f=f: wind_ref[f - 1, lev]
        else:
            get = lambda lev, f=f: trc_ref[f - 3, lev]
        e_ref[f] = _pack_edges(get, nlev, rows, w, zeros)


def _edge_kernel(south_ref, inner_ref, north_ref, e_ref):
    nf, nlev, halo, w = south_ref.shape
    rows = inner_ref.shape[1]
    zeros = jnp.zeros((halo, w), jnp.float32)
    for f in range(nf):
        e_ref[f, pl.ds(0, halo)] = _pack_edges(lambda lev: south_ref[f, lev], nlev, halo, w, zeros)
        e_ref[f, pl.ds(halo, rows)] = inner_ref[f]
        e_ref[f, pl.ds(halo + rows, halo)] = _pack_edges(lambda lev: north_ref[f, lev], nlev, halo, w, zeros)


def _main1_kernel(s_ref, th_ref, rv_ref, o_ref, p_ref, mf_ref, sp_ref):
    nf, _, rows, w = s_ref.shape
    nlev = th_ref.shape[1]
    lev = pl.program_id(0)
    win = pl.ds(MARGIN, rows)

    @pl.when(lev == 0)
    def _():
        _potential(lambda l: th_ref[0, l], p_ref, nlev, rows)

    rv = (rv_ref[0], rv_ref[1], rv_ref[2])
    for f in range(nf):
        sp_ref[f, win] = s_ref[f, 0]

    def store(f, x):
        o_ref[f, 0, win] = x

    _substep(
        lambda f, d: sp_ref[f, pl.ds(MARGIN + d, rows)],
        store,
        nf,
        lambda d: p_ref[lev, pl.ds(MARGIN + d, rows)],
        rv,
        mf_ref,
    )


def _final_kernel(
    s1_ref, e_ref, ew_ref, ee_ref, rv_ref, thk_ref, wind_ref, trc_ref, s_ref, g0_ref, g1_ref, g2_ref, p_ref, pg_ref, mf_ref, o2_ref
):
    nf, nlev, _, w = s1_ref.shape
    rows = rv_ref.shape[1]
    inner = rows - 2 * HALO
    rv1 = (rv_ref[0], rv_ref[1], rv_ref[2])
    lane, group, kk = _lanes(rows, w)
    win = pl.ds(MARGIN, rows)

    for f in range(nf):
        g0_ref[f, win] = jnp.where(
            kk < HALO, _lroll(ew_ref[f], -2 * HALO), jnp.where(kk >= 3 * HALO, _lroll(ee_ref[f], 2 * HALO), e_ref[f])
        )
    pg_ref[win] = _suffix_packed(g0_ref[0, win], group, nlev)

    def set_g1(f, x):
        g1_ref[f, win] = x

    _substep(
        lambda f, d: g0_ref[f, pl.ds(MARGIN + d, rows)],
        set_g1,
        nf,
        lambda d: pg_ref[pl.ds(MARGIN + d, rows)],
        rv1,
        mf_ref,
    )
    for f in range(nf):
        g = g1_ref[f, win]
        for lev in range(nlev):
            s_ref[f, lev, win] = _fix_edges(s1_ref[f, lev, win], g, lev, lane)
    for f in range(nf):
        g1_ref[f, win] = _pack_edges(lambda lev: s_ref[f, lev, win], nlev, rows, w, g1_ref[f, win])
    pg_ref[win] = _suffix_packed(g1_ref[0, win], group, nlev)

    def set_g2(f, x):
        g2_ref[f, win] = x

    _substep(
        lambda f, d: g1_ref[f, pl.ds(MARGIN + d, rows)],
        set_g2,
        nf,
        lambda d: pg_ref[pl.ds(MARGIN + d, rows)],
        rv1,
        mf_ref,
    )
    _potential(lambda lev: s_ref[0, lev, win], p_ref, nlev, rows)
    inner_rows = pl.ds(MARGIN + HALO, inner)
    for lev in range(nlev):

        def store2(f, x, lev=lev):
            o2_ref[f, win] = _fix_edges(x, g2_ref[f, win], lev, lane)
            x = o2_ref[f, inner_rows]
            if f == 0:
                thk_ref[lev] = x
            elif f < 3:
                wind_ref[f - 1, lev] = x
            else:
                trc_ref[f - 3, lev] = x

        _substep(
            lambda f, d, lev=lev: s_ref[f, lev, pl.ds(MARGIN + d, rows)],
            store2,
            nf,
            lambda d, lev=lev: p_ref[lev, pl.ds(MARGIN + d, rows)],
            rv1,
            mf_ref,
        )


def _shift_pairs(n, d, closed):
    return [(i, (i + d) % n) for i in range(n) if closed or 0 <= i + d < n]


def _vmem_call(kernel, out_shape, n_in, scratch, flops, nbytes):
    vmem = pl.BlockSpec(memory_space=pltpu.VMEM)
    return pl.pallas_call(
        kernel,
        out_shape=out_shape,
        in_specs=[vmem] * n_in,
        out_specs=tuple(vmem for _ in out_shape) if isinstance(out_shape, tuple) else vmem,
        scratch_shapes=scratch,
        cost_estimate=pl.CostEstimate(flops=flops, bytes_accessed=nbytes, transcendentals=0),
    )


def shards(thickness, winds, tracer_mass):
    fields = jnp.concatenate([thickness[None], winds, tracer_mass], 0)
    nf, nlev, rows, w = fields.shape
    nlat = lax.axis_size("lat")
    nlon = lax.axis_size("lon")
    band = lax.axis_index("lat")
    spacing = math.pi / (rows * nlat)
    tall = rows + 2 * HALO

    row_index = (jnp.arange(tall) + (band * rows - HALO)).astype(jnp.float32)
    center_lat = (row_index + 0.5) * spacing - 0.5 * math.pi
    face_lat = (row_index + 1.0) * spacing - 0.5 * math.pi
    center_cos = jnp.cos(center_lat)
    rowvec = jnp.stack(
        [
            jnp.abs(jnp.cos(face_lat)),
            1.0 / jnp.abs(center_cos),
            COUR * FCOR * jnp.sin(center_lat) * jnp.where(center_cos >= 0.0, 1.0, -1.0),
        ]
    )
    rowvec = jnp.broadcast_to(rowvec[:, :, None], (3, tall, w))

    inner_edges = _vmem_call(
        _edge_inner_kernel, jax.ShapeDtypeStruct((nf, rows, w), jnp.float32), 3, [], 0, nf * nlev * rows * w * 4
    )(thickness, winds, tracer_mass)

    top = fields[:, :, rows - HALO :]
    bottom = fields[:, :, :HALO]
    from_south = lax.ppermute(top, "lat", _shift_pairs(nlat, 1, False))
    from_north = lax.ppermute(bottom, "lat", _shift_pairs(nlat, -1, False))
    half = nlon // 2
    pole_pairs = []
    for b in (0, nlat - 1):
        for s in range(nlon):
            pole_pairs.append((b * nlon + s, b * nlon + (s + half) % nlon))
    pole_out = jnp.where(band == 0, bottom, top)
    pole_in = lax.ppermute(pole_out, ("lat", "lon"), pole_pairs)
    sign = jnp.where(jnp.arange(nf) == 2, -1.0, 1.0).astype(jnp.float32)[:, None, None, None]
    mirrored = jnp.flip(pole_in, 2) * sign
    south = jnp.where(band == 0, mirrored, from_south)
    north = jnp.where(band == nlat - 1, mirrored, from_north)
    padded = jnp.concatenate([south, fields, north], 2)

    slab = nf * tall * w * 4
    edges = _vmem_call(
        _edge_kernel, jax.ShapeDtypeStruct((nf, tall, w), jnp.float32), 3, [], 0, 2 * slab
    )(south, inner_edges, north)
    from_west = lax.ppermute(edges, "lon", _shift_pairs(nlon, 1, True))
    from_east = lax.ppermute(edges, "lon", _shift_pairs(nlon, -1, True))

    step_flops = 60 * nf * nlev * tall * w
    deep = tall + 2 * MARGIN
    main1 = pl.pallas_call(
        _main1_kernel,
        out_shape=jax.ShapeDtypeStruct((nf, nlev, deep, w), jnp.float32),
        grid=(nlev,),
        in_specs=[
            pl.BlockSpec((nf, 1, tall, w), lambda l: (0, l, 0, 0)),
            pl.BlockSpec((1, nlev, tall, w), lambda l: (0, 0, 0, 0)),
            pl.BlockSpec((3, tall, w), lambda l: (0, 0, 0)),
        ],
        out_specs=pl.BlockSpec((nf, 1, deep, w), lambda l: (0, l, 0, 0)),
        scratch_shapes=[
            pltpu.VMEM((nlev, deep, w), jnp.float32),
            pltpu.VMEM((nf, deep, w), jnp.float32),
            pltpu.VMEM((nf, deep, w), jnp.float32),
        ],
        compiler_params=pltpu.CompilerParams(dimension_semantics=("arbitrary",)),
        cost_estimate=pl.CostEstimate(flops=step_flops, bytes_accessed=2 * slab * nlev, transcendentals=0),
    )(padded, padded, rowvec)

    return _vmem_call(
        _final_kernel,
        (
            jax.ShapeDtypeStruct(thickness.shape, jnp.float32),
            jax.ShapeDtypeStruct(winds.shape, jnp.float32),
            jax.ShapeDtypeStruct(tracer_mass.shape, jnp.float32),
        ),
        5,
        [
            pltpu.VMEM((nf, nlev, deep, w), jnp.float32),
            pltpu.VMEM((nf, tall + 2 * MARGIN, w), jnp.float32),
            pltpu.VMEM((nf, tall + 2 * MARGIN, w), jnp.float32),
            pltpu.VMEM((nf, tall + 2 * MARGIN, w), jnp.float32),
            pltpu.VMEM((nlev, tall + 2 * MARGIN, w), jnp.float32),
            pltpu.VMEM((tall + 2 * MARGIN, w), jnp.float32),
            pltpu.VMEM((nf, tall + 2 * MARGIN, w), jnp.float32),
            pltpu.VMEM((nf, tall + 2 * MARGIN, w), jnp.float32),
        ],
        step_flops + 3 * step_flops // nlev,
        2 * slab * nlev,
    )(main1, edges, from_west, from_east, rowvec)


def solution(mesh):
    return jax.shard_map(
        shards,
        mesh=mesh,
        in_specs=(P(None, "lat", "lon"), P(None, None, "lat", "lon"), P(None, None, "lat", "lon")),
        out_specs=(P(None, "lat", "lon"), P(None, None, "lat", "lon"), P(None, None, "lat", "lon")),
        check_vma=False,
    )
```

```python
import math

import jax
import jax.numpy as jnp
from jax import lax
from jax.experimental import pallas as pl
from jax.experimental.pallas import tpu as pltpu
from jax.sharding import PartitionSpec as P

SUBSTEPS = 2
COUR = 0.25
GRAV = 1.0
FCOR = 1.0

HALO = 2 * SUBSTEPS
STRIP = 4 * HALO
MARGIN = 8


def _lroll(x, k):
    n = x.shape[-1]
    return pltpu.roll(x, k % n, x.ndim - 1)


def _face(pos, behind, centre, forward, beyond):
    p = jnp.where(pos, centre, forward)
    q = jnp.where(pos, forward, centre)
    r = jnp.where(pos, behind, beyond)
    return 5.0 * p + 2.0 * q - r


def _substep(load, store, nf, pot, rv, mf_ref):
    fcos, inv_acos, cor = rv
    u = load(1, 0)
    v = load(2, 0)
    n = u.shape[0]
    fs = (COUR * 0.5 / 6.0) * (u + _lroll(u, -1))
    ms = (COUR * 0.5 / 6.0) * (v + load(2, 1)) * fcos
    fpos = fs >= 0.0
    mpos = ms >= 0.0
    for f in range(nf):
        x = u if f == 1 else (v if f == 2 else load(f, 0))
        zf = fs * _face(fpos, _lroll(x, 1), x, _lroll(x, -1), _lroll(x, -2))
        mf = ms * _face(mpos, load(f, -1), x, load(f, 1), load(f, 2))
        mf_ref[f, pl.ds(MARGIN, n)] = mf
        new = x - (zf - _lroll(zf, 1)) - (mf - mf_ref[f, pl.ds(MARGIN - 1, n)]) * inv_acos
        if f == 1:
            p0 = pot(0)
            new = new - COUR * 0.5 * (_lroll(p0, -1) - _lroll(p0, 1)) + cor * v
        elif f == 2:
            new = new - COUR * 0.5 * (pot(1) - pot(-1)) - cor * u
        store(f, new)


def _suffix_packed(h, group, ngroups):
    s = h
    k = 1
    while k < ngroups:
        s = s + jnp.where(group + k < ngroups, _lroll(s, -STRIP * k), 0.0)
        k *= 2
    return GRAV * s


def _fix_edges(x, g, lev, lane):
    w = x.shape[-1]
    base = STRIP * lev
    lo = _lroll(g, -(base + HALO))
    hi = _lroll(g, (w - 2) - (base + 2 * HALO + 2))
    return jnp.where(lane < 2, lo, jnp.where(lane >= w - 2, hi, x))


def _lanes(rows, w):
    lane = lax.broadcasted_iota(jnp.int32, (rows, w), 1)
    return lane, lane // STRIP, lane % STRIP


def _pack_edges(get, nlev, rows, w, init):
    lane, group, kk = _lanes(rows, w)
    lo_mask = (kk >= HALO) & (kk < 2 * HALO)
    hi_mask = (kk >= 2 * HALO) & (kk < 3 * HALO)
    g = init
    for lev in range(nlev):
        m = get(lev)
        base = STRIP * lev
        g = jnp.where((group == lev) & lo_mask, _lroll(m, base + HALO), g)
        g = jnp.where((group == lev) & hi_mask, _lroll(m, base + 2 * HALO - (w - HALO)), g)
    return g


def _potential(thick, p_ref, nlev, n):
    acc = None
    for lev in reversed(range(nlev)):
        acc = thick(lev) if acc is None else acc + thick(lev)
        p_ref[lev, pl.ds(MARGIN, n)] = GRAV * acc


def _edge_inner_kernel(thk_ref, wind_ref, trc_ref, e_ref):
    nlev, rows, w = thk_ref.shape
    zeros = jnp.zeros((rows, w), jnp.float32)
    for f in range(e_ref.shape[0]):
        if f == 0:
            get = lambda lev: thk_ref[lev]
        elif f < 3:
            get = lambda lev, f=f: wind_ref[f - 1, lev]
        else:
            get = lambda lev, f=f: trc_ref[f - 3, lev]
        e_ref[f] = _pack_edges(get, nlev, rows, w, zeros)


def _edge_kernel(south_ref, inner_ref, north_ref, e_ref):
    nf, nlev, halo, w = south_ref.shape
    rows = inner_ref.shape[1]
    zeros = jnp.zeros((halo, w), jnp.float32)
    for f in range(nf):
        e_ref[f, pl.ds(0, halo)] = _pack_edges(lambda lev: south_ref[f, lev], nlev, halo, w, zeros)
        e_ref[f, pl.ds(halo, rows)] = inner_ref[f]
        e_ref[f, pl.ds(halo + rows, halo)] = _pack_edges(lambda lev: north_ref[f, lev], nlev, halo, w, zeros)


def _main1_kernel(south_ref, thk_ref, wind_ref, trc_ref, north_ref, tall_ref, sall_ref, nall_ref, rv_ref, o_ref, p_ref, mf_ref, sp_ref):
    nf, _, halo, w = south_ref.shape
    nlev, rows = tall_ref.shape[0], tall_ref.shape[1]
    lev = pl.program_id(0)
    tall = rows + 2 * halo
    win = pl.ds(MARGIN, tall)
    top = pl.ds(MARGIN, halo)
    mid = pl.ds(MARGIN + halo, rows)
    bot = pl.ds(MARGIN + halo + rows, halo)

    @pl.when(lev == 0)
    def _():
        acc = None
        for l in reversed(range(nlev)):
            part = (sall_ref[0, l], tall_ref[l], nall_ref[0, l])
            acc = part if acc is None else tuple(x + y for x, y in zip(acc, part))
            p_ref[l, top] = GRAV * acc[0]
            p_ref[l, mid] = GRAV * acc[1]
            p_ref[l, bot] = GRAV * acc[2]

    rv = (rv_ref[0], rv_ref[1], rv_ref[2])
    for f in range(nf):
        sp_ref[f, top] = south_ref[f, 0]
        if f == 0:
            sp_ref[f, mid] = thk_ref[0]
        elif f < 3:
            sp_ref[f, mid] = wind_ref[f - 1, 0]
        else:
            sp_ref[f, mid] = trc_ref[f - 3, 0]
        sp_ref[f, bot] = north_ref[f, 0]

    def store(f, x):
        o_ref[f, 0, win] = x

    _substep(
        lambda f, d: sp_ref[f, pl.ds(MARGIN + d, tall)],
        store,
        nf,
        lambda d: p_ref[lev, pl.ds(MARGIN + d, tall)],
        rv,
        mf_ref,
    )


def _final_kernel(
    s1_ref, e_ref, ew_hbm, ee_hbm, rv_ref, thk_ref, wind_ref, trc_ref, s_ref, g0_ref, g1_ref, g2_ref, p_ref, pg_ref, mf_ref, o2_ref, nb_ref, sem
):
    copies = [pltpu.make_async_copy(src, nb_ref.at[i], sem.at[i]) for i, src in enumerate((ew_hbm, ee_hbm))]
    for c in copies:
        c.start()
    for c in copies:
        c.wait()
    ew_ref = nb_ref.at[0]
    ee_ref = nb_ref.at[1]
    nf, nlev, _, w = s1_ref.shape
    rows = rv_ref.shape[1]
    inner = rows - 2 * HALO
    rv1 = (rv_ref[0], rv_ref[1], rv_ref[2])
    lane, group, kk = _lanes(rows, w)
    win = pl.ds(MARGIN, rows)

    for f in range(nf):
        g0_ref[f, win] = jnp.where(
            kk < HALO, _lroll(ew_ref[f], -2 * HALO), jnp.where(kk >= 3 * HALO, _lroll(ee_ref[f], 2 * HALO), e_ref[f])
        )
    pg_ref[win] = _suffix_packed(g0_ref[0, win], group, nlev)

    def set_g1(f, x):
        g1_ref[f, win] = x

    _substep(
        lambda f, d: g0_ref[f, pl.ds(MARGIN + d, rows)],
        set_g1,
        nf,
        lambda d: pg_ref[pl.ds(MARGIN + d, rows)],
        rv1,
        mf_ref,
    )
    for f in range(nf):
        g = g1_ref[f, win]
        for lev in range(nlev):
            s_ref[f, lev, win] = _fix_edges(s1_ref[f, lev, win], g, lev, lane)
    for f in range(nf):
        g1_ref[f, win] = _pack_edges(lambda lev: s_ref[f, lev, win], nlev, rows, w, g1_ref[f, win])
    pg_ref[win] = _suffix_packed(g1_ref[0, win], group, nlev)

    def set_g2(f, x):
        g2_ref[f, win] = x

    _substep(
        lambda f, d: g1_ref[f, pl.ds(MARGIN + d, rows)],
        set_g2,
        nf,
        lambda d: pg_ref[pl.ds(MARGIN + d, rows)],
        rv1,
        mf_ref,
    )
    _potential(lambda lev: s_ref[0, lev, win], p_ref, nlev, rows)
    inner_rows = pl.ds(MARGIN + HALO, inner)
    for lev in range(nlev):

        def store2(f, x, lev=lev):
            o2_ref[f, win] = _fix_edges(x, g2_ref[f, win], lev, lane)
            x = o2_ref[f, inner_rows]
            if f == 0:
                thk_ref[lev] = x
            elif f < 3:
                wind_ref[f - 1, lev] = x
            else:
                trc_ref[f - 3, lev] = x

        _substep(
            lambda f, d, lev=lev: s_ref[f, lev, pl.ds(MARGIN + d, rows)],
            store2,
            nf,
            lambda d, lev=lev: p_ref[lev, pl.ds(MARGIN + d, rows)],
            rv1,
            mf_ref,
        )


def _shift_pairs(n, d, closed):
    return [(i, (i + d) % n) for i in range(n) if closed or 0 <= i + d < n]


def _vmem_call(kernel, out_shape, n_in, scratch, flops, nbytes):
    vmem = pl.BlockSpec(memory_space=pltpu.VMEM)
    return pl.pallas_call(
        kernel,
        out_shape=out_shape,
        in_specs=[vmem] * n_in,
        out_specs=tuple(vmem for _ in out_shape) if isinstance(out_shape, tuple) else vmem,
        scratch_shapes=scratch,
        cost_estimate=pl.CostEstimate(flops=flops, bytes_accessed=nbytes, transcendentals=0),
    )


def shards(thickness, winds, tracer_mass):
    fields = jnp.concatenate([thickness[None], winds, tracer_mass], 0)
    nf, nlev, rows, w = fields.shape
    nlat = lax.axis_size("lat")
    nlon = lax.axis_size("lon")
    band = lax.axis_index("lat")
    spacing = math.pi / (rows * nlat)
    tall = rows + 2 * HALO

    row_index = (jnp.arange(tall) + (band * rows - HALO)).astype(jnp.float32)
    center_lat = (row_index + 0.5) * spacing - 0.5 * math.pi
    face_lat = (row_index + 1.0) * spacing - 0.5 * math.pi
    center_cos = jnp.cos(center_lat)
    rowvec = jnp.stack(
        [
            jnp.abs(jnp.cos(face_lat)),
            1.0 / jnp.abs(center_cos),
            COUR * FCOR * jnp.sin(center_lat) * jnp.where(center_cos >= 0.0, 1.0, -1.0),
        ]
    )
    rowvec = jnp.broadcast_to(rowvec[:, :, None], (3, tall, w))

    inner_edges = _vmem_call(
        _edge_inner_kernel, jax.ShapeDtypeStruct((nf, rows, w), jnp.float32), 3, [], 0, nf * nlev * rows * w * 4
    )(thickness, winds, tracer_mass)

    top = fields[:, :, rows - HALO :]
    bottom = fields[:, :, :HALO]
    from_south = lax.ppermute(top, "lat", _shift_pairs(nlat, 1, False))
    from_north = lax.ppermute(bottom, "lat", _shift_pairs(nlat, -1, False))
    half = nlon // 2
    pole_pairs = []
    for b in (0, nlat - 1):
        for s in range(nlon):
            pole_pairs.append((b * nlon + s, b * nlon + (s + half) % nlon))
    pole_out = jnp.where(band == 0, bottom, top)
    pole_in = lax.ppermute(pole_out, ("lat", "lon"), pole_pairs)
    sign = jnp.where(jnp.arange(nf) == 2, -1.0, 1.0).astype(jnp.float32)[:, None, None, None]
    mirrored = jnp.flip(pole_in, 2) * sign
    south = jnp.where(band == 0, mirrored, from_south)
    north = jnp.where(band == nlat - 1, mirrored, from_north)

    slab = nf * tall * w * 4
    edges = _vmem_call(
        _edge_kernel, jax.ShapeDtypeStruct((nf, tall, w), jnp.float32), 3, [], 0, 2 * slab
    )(south, inner_edges, north)
    from_west = lax.ppermute(edges, "lon", _shift_pairs(nlon, 1, True))
    from_east = lax.ppermute(edges, "lon", _shift_pairs(nlon, -1, True))

    step_flops = 60 * nf * nlev * tall * w
    deep = tall + 2 * MARGIN
    main1 = pl.pallas_call(
        _main1_kernel,
        out_shape=jax.ShapeDtypeStruct((nf, nlev, deep, w), jnp.float32),
        grid=(nlev,),
        in_specs=[
            pl.BlockSpec((nf, 1, HALO, w), lambda l: (0, l, 0, 0)),
            pl.BlockSpec((1, rows, w), lambda l: (l, 0, 0)),
            pl.BlockSpec((2, 1, rows, w), lambda l: (0, l, 0, 0)),
            pl.BlockSpec((nf - 3, 1, rows, w), lambda l: (0, l, 0, 0)),
            pl.BlockSpec((nf, 1, HALO, w), lambda l: (0, l, 0, 0)),
            pl.BlockSpec((nlev, rows, w), lambda l: (0, 0, 0)),
            pl.BlockSpec((1, nlev, HALO, w), lambda l: (0, 0, 0, 0)),
            pl.BlockSpec((1, nlev, HALO, w), lambda l: (0, 0, 0, 0)),
            pl.BlockSpec((3, tall, w), lambda l: (0, 0, 0)),
        ],
        out_specs=pl.BlockSpec((nf, 1, deep, w), lambda l: (0, l, 0, 0)),
        scratch_shapes=[
            pltpu.VMEM((nlev, deep, w), jnp.float32),
            pltpu.VMEM((nf, deep, w), jnp.float32),
            pltpu.VMEM((nf, deep, w), jnp.float32),
        ],
        compiler_params=pltpu.CompilerParams(dimension_semantics=("arbitrary",)),
        cost_estimate=pl.CostEstimate(flops=step_flops, bytes_accessed=2 * slab * nlev, transcendentals=0),
    )(south, thickness, winds, tracer_mass, north, thickness, south, north, rowvec)

    vmem = pl.BlockSpec(memory_space=pltpu.VMEM)
    anywhere = pl.BlockSpec(memory_space=pl.ANY)
    return pl.pallas_call(
        _final_kernel,
        out_shape=(
            jax.ShapeDtypeStruct(thickness.shape, jnp.float32),
            jax.ShapeDtypeStruct(winds.shape, jnp.float32),
            jax.ShapeDtypeStruct(tracer_mass.shape, jnp.float32),
        ),
        in_specs=[vmem, vmem, anywhere, anywhere, vmem],
        out_specs=(vmem, vmem, vmem),
        scratch_shapes=[
            pltpu.VMEM((nf, nlev, deep, w), jnp.float32),
            pltpu.VMEM((nf, deep, w), jnp.float32),
            pltpu.VMEM((nf, deep, w), jnp.float32),
            pltpu.VMEM((nf, deep, w), jnp.float32),
            pltpu.VMEM((nlev, deep, w), jnp.float32),
            pltpu.VMEM((deep, w), jnp.float32),
            pltpu.VMEM((nf, deep, w), jnp.float32),
            pltpu.VMEM((nf, deep, w), jnp.float32),
            pltpu.VMEM((2, nf, tall, w), jnp.float32),
            pltpu.SemaphoreType.DMA((2,)),
        ],
        cost_estimate=pl.CostEstimate(
            flops=step_flops + 3 * step_flops // nlev, bytes_accessed=2 * slab * nlev, transcendentals=0
        ),
    )(main1, edges, from_west, from_east, rowvec)


def solution(mesh):
    return jax.shard_map(
        shards,
        mesh=mesh,
        in_specs=(P(None, "lat", "lon"), P(None, None, "lat", "lon"), P(None, None, "lat", "lon")),
        out_specs=(P(None, "lat", "lon"), P(None, None, "lat", "lon"), P(None, None, "lat", "lon")),
        check_vma=False,
    )
```

```python
import math

import jax
import jax.numpy as jnp
from jax import lax
from jax.experimental import pallas as pl
from jax.experimental.pallas import tpu as pltpu
from jax.sharding import PartitionSpec as P

SUBSTEPS = 2
COUR = 0.25
GRAV = 1.0
FCOR = 1.0

HALO = 2 * SUBSTEPS
STRIP = 4 * HALO
MARGIN = 8


def _lroll(x, k):
    n = x.shape[-1]
    return pltpu.roll(x, k % n, x.ndim - 1)


def _face(pos, behind, centre, forward, beyond):
    p = jnp.where(pos, centre, forward)
    q = jnp.where(pos, forward, centre)
    r = jnp.where(pos, behind, beyond)
    return 5.0 * p + 2.0 * q - r


def _substep(load, store, nf, pot, rv, mf_ref):
    fcos, inv_acos, cor = rv
    u = load(1, 0)
    v = load(2, 0)
    n = u.shape[0]
    fs = (COUR * 0.5 / 6.0) * (u + _lroll(u, -1))
    ms = (COUR * 0.5 / 6.0) * (v + load(2, 1)) * fcos
    fpos = fs >= 0.0
    mpos = ms >= 0.0
    for f in range(nf):
        x = u if f == 1 else (v if f == 2 else load(f, 0))
        zf = fs * _face(fpos, _lroll(x, 1), x, _lroll(x, -1), _lroll(x, -2))
        mf = ms * _face(mpos, load(f, -1), x, load(f, 1), load(f, 2))
        mf_ref[f, pl.ds(MARGIN, n)] = mf
        new = x - (zf - _lroll(zf, 1)) - (mf - mf_ref[f, pl.ds(MARGIN - 1, n)]) * inv_acos
        if f == 1:
            p0 = pot(0)
            new = new - COUR * 0.5 * (_lroll(p0, -1) - _lroll(p0, 1)) + cor * v
        elif f == 2:
            new = new - COUR * 0.5 * (pot(1) - pot(-1)) - cor * u
        store(f, new)


def _suffix_packed(h, group, ngroups):
    s = h
    k = 1
    while k < ngroups:
        s = s + jnp.where(group + k < ngroups, _lroll(s, -STRIP * k), 0.0)
        k *= 2
    return GRAV * s


def _fix_edges(x, g, lev, lane):
    w = x.shape[-1]
    base = STRIP * lev
    lo = _lroll(g, -(base + HALO))
    hi = _lroll(g, (w - 2) - (base + 2 * HALO + 2))
    return jnp.where(lane < 2, lo, jnp.where(lane >= w - 2, hi, x))


def _lanes(rows, w):
    lane = lax.broadcasted_iota(jnp.int32, (rows, w), 1)
    return lane, lane // STRIP, lane % STRIP


def _pack_edges(get, nlev, rows, w, init):
    lane, group, kk = _lanes(rows, w)
    lo_mask = (kk >= HALO) & (kk < 2 * HALO)
    hi_mask = (kk >= 2 * HALO) & (kk < 3 * HALO)
    g = init
    for lev in range(nlev):
        m = get(lev)
        base = STRIP * lev
        g = jnp.where((group == lev) & lo_mask, _lroll(m, base + HALO), g)
        g = jnp.where((group == lev) & hi_mask, _lroll(m, base + 2 * HALO - (w - HALO)), g)
    return g


def _potential(thick, p_ref, nlev, n):
    acc = None
    for lev in reversed(range(nlev)):
        acc = thick(lev) if acc is None else acc + thick(lev)
        p_ref[lev, pl.ds(MARGIN, n)] = GRAV * acc


def _edge_inner_kernel(thk_ref, wind_ref, trc_ref, e_ref):
    nlev, rows, w = thk_ref.shape
    zeros = jnp.zeros((rows, w), jnp.float32)
    for f in range(e_ref.shape[0]):
        if f == 0:
            get = lambda lev: thk_ref[lev]
        elif f < 3:
            get = lambda lev, f=f: wind_ref[f - 1, lev]
        else:
            get = lambda lev, f=f: trc_ref[f - 3, lev]
        e_ref[f] = _pack_edges(get, nlev, rows, w, zeros)


def _edge_kernel(south_ref, inner_ref, north_ref, e_ref):
    nf, nlev, halo, w = south_ref.shape
    rows = inner_ref.shape[1]
    zeros = jnp.zeros((halo, w), jnp.float32)
    for f in range(nf):
        e_ref[f, pl.ds(0, halo)] = _pack_edges(lambda lev: south_ref[f, lev], nlev, halo, w, zeros)
        e_ref[f, pl.ds(halo, rows)] = inner_ref[f]
        e_ref[f, pl.ds(halo + rows, halo)] = _pack_edges(lambda lev: north_ref[f, lev], nlev, halo, w, zeros)


def _main1_kernel(south_ref, thk_ref, wind_ref, trc_ref, north_ref, tall_ref, sall_ref, nall_ref, rv_ref, o_ref, p_ref, mf_ref, sp_ref):
    nf, _, halo, w = south_ref.shape
    nlev, rows = tall_ref.shape[0], tall_ref.shape[1]
    lev = pl.program_id(0)
    tall = rows + 2 * halo
    win = pl.ds(MARGIN, tall)
    top = pl.ds(MARGIN, halo)
    mid = pl.ds(MARGIN + halo, rows)
    bot = pl.ds(MARGIN + halo + rows, halo)

    @pl.when(lev == 0)
    def _():
        acc = None
        for l in reversed(range(nlev)):
            part = (sall_ref[0, l], tall_ref[l], nall_ref[0, l])
            acc = part if acc is None else tuple(x + y for x, y in zip(acc, part))
            p_ref[l, top] = GRAV * acc[0]
            p_ref[l, mid] = GRAV * acc[1]
            p_ref[l, bot] = GRAV * acc[2]

    rv = (rv_ref[0], rv_ref[1], rv_ref[2])
    for f in range(nf):
        sp_ref[f, top] = south_ref[f, 0]
        if f == 0:
            sp_ref[f, mid] = thk_ref[0]
        elif f < 3:
            sp_ref[f, mid] = wind_ref[f - 1, 0]
        else:
            sp_ref[f, mid] = trc_ref[f - 3, 0]
        sp_ref[f, bot] = north_ref[f, 0]

    def store(f, x):
        o_ref[0, f] = x

    _substep(
        lambda f, d: sp_ref[f, pl.ds(MARGIN + d, tall)],
        store,
        nf,
        lambda d: p_ref[lev, pl.ds(MARGIN + d, tall)],
        rv,
        mf_ref,
    )


def _final_kernel(
    s1_hbm, e_ref, ew_hbm, ee_hbm, rv_ref, thk_hbm, wind_hbm, trc_hbm,
    s_ref, g0_ref, g1_ref, g2_ref, p_ref, pg_ref, mf_ref, o2_ref, nb_ref, sem, s1_ref, s1_sem, ob_ref, out_sem,
):
    nlev, nf, _, w = s1_hbm.shape
    s1_copies = [pltpu.make_async_copy(s1_hbm.at[lev], s1_ref.at[lev], s1_sem.at[lev]) for lev in range(nlev)]
    for c in s1_copies:
        c.start()
    copies = [pltpu.make_async_copy(src, nb_ref.at[i], sem.at[i]) for i, src in enumerate((ew_hbm, ee_hbm))]
    for c in copies:
        c.start()
    for c in copies:
        c.wait()
    ew_ref = nb_ref.at[0]
    ee_ref = nb_ref.at[1]
    rows = rv_ref.shape[1]
    inner = rows - 2 * HALO
    rv1 = (rv_ref[0], rv_ref[1], rv_ref[2])
    lane, group, kk = _lanes(rows, w)
    win = pl.ds(MARGIN, rows)

    for f in range(nf):
        g0_ref[f, win] = jnp.where(
            kk < HALO, _lroll(ew_ref[f], -2 * HALO), jnp.where(kk >= 3 * HALO, _lroll(ee_ref[f], 2 * HALO), e_ref[f])
        )
    pg_ref[win] = _suffix_packed(g0_ref[0, win], group, nlev)

    def set_g1(f, x):
        g1_ref[f, win] = x

    _substep(
        lambda f, d: g0_ref[f, pl.ds(MARGIN + d, rows)],
        set_g1,
        nf,
        lambda d: pg_ref[pl.ds(MARGIN + d, rows)],
        rv1,
        mf_ref,
    )
    for lev in range(nlev):
        s1_copies[lev].wait()
        for f in range(nf):
            s_ref[f, lev, win] = _fix_edges(s1_ref[lev, f], g1_ref[f, win], lev, lane)
    for f in range(nf):
        g1_ref[f, win] = _pack_edges(lambda lev: s_ref[f, lev, win], nlev, rows, w, g1_ref[f, win])
    pg_ref[win] = _suffix_packed(g1_ref[0, win], group, nlev)

    def set_g2(f, x):
        g2_ref[f, win] = x

    _substep(
        lambda f, d: g1_ref[f, pl.ds(MARGIN + d, rows)],
        set_g2,
        nf,
        lambda d: pg_ref[pl.ds(MARGIN + d, rows)],
        rv1,
        mf_ref,
    )
    _potential(lambda lev: s_ref[0, lev, win], p_ref, nlev, rows)
    inner_rows = pl.ds(MARGIN + HALO, inner)
    out_copies = []
    for lev in range(nlev):

        def store2(f, x, lev=lev):
            o2_ref[f, win] = _fix_edges(x, g2_ref[f, win], lev, lane)
            ob_ref[lev, f] = o2_ref[f, inner_rows]
            if f == 0:
                dst = thk_hbm.at[lev]
            elif f < 3:
                dst = wind_hbm.at[f - 1, lev]
            else:
                dst = trc_hbm.at[f - 3, lev]
            out_copies.append(pltpu.make_async_copy(ob_ref.at[lev, f], dst, out_sem.at[lev, f]))
            out_copies[-1].start()

        _substep(
            lambda f, d, lev=lev: s_ref[f, lev, pl.ds(MARGIN + d, rows)],
            store2,
            nf,
            lambda d, lev=lev: p_ref[lev, pl.ds(MARGIN + d, rows)],
            rv1,
            mf_ref,
        )
    for c in out_copies:
        c.wait()


def _shift_pairs(n, d, closed):
    return [(i, (i + d) % n) for i in range(n) if closed or 0 <= i + d < n]


def _vmem_call(kernel, out_shape, n_in, scratch, flops, nbytes):
    vmem = pl.BlockSpec(memory_space=pltpu.VMEM)
    return pl.pallas_call(
        kernel,
        out_shape=out_shape,
        in_specs=[vmem] * n_in,
        out_specs=tuple(vmem for _ in out_shape) if isinstance(out_shape, tuple) else vmem,
        scratch_shapes=scratch,
        cost_estimate=pl.CostEstimate(flops=flops, bytes_accessed=nbytes, transcendentals=0),
    )


def shards(thickness, winds, tracer_mass):
    fields = jnp.concatenate([thickness[None], winds, tracer_mass], 0)
    nf, nlev, rows, w = fields.shape
    nlat = lax.axis_size("lat")
    nlon = lax.axis_size("lon")
    band = lax.axis_index("lat")
    spacing = math.pi / (rows * nlat)
    tall = rows + 2 * HALO

    row_index = (jnp.arange(tall) + (band * rows - HALO)).astype(jnp.float32)
    center_lat = (row_index + 0.5) * spacing - 0.5 * math.pi
    face_lat = (row_index + 1.0) * spacing - 0.5 * math.pi
    center_cos = jnp.cos(center_lat)
    rowvec = jnp.stack(
        [
            jnp.abs(jnp.cos(face_lat)),
            1.0 / jnp.abs(center_cos),
            COUR * FCOR * jnp.sin(center_lat) * jnp.where(center_cos >= 0.0, 1.0, -1.0),
        ]
    )
    rowvec = jnp.broadcast_to(rowvec[:, :, None], (3, tall, w))

    inner_edges = _vmem_call(
        _edge_inner_kernel, jax.ShapeDtypeStruct((nf, rows, w), jnp.float32), 3, [], 0, nf * nlev * rows * w * 4
    )(thickness, winds, tracer_mass)

    top = fields[:, :, rows - HALO :]
    bottom = fields[:, :, :HALO]
    from_south = lax.ppermute(top, "lat", _shift_pairs(nlat, 1, False))
    from_north = lax.ppermute(bottom, "lat", _shift_pairs(nlat, -1, False))
    half = nlon // 2
    pole_pairs = []
    for b in (0, nlat - 1):
        for s in range(nlon):
            pole_pairs.append((b * nlon + s, b * nlon + (s + half) % nlon))
    pole_out = jnp.where(band == 0, bottom, top)
    pole_in = lax.ppermute(pole_out, ("lat", "lon"), pole_pairs)
    sign = jnp.where(jnp.arange(nf) == 2, -1.0, 1.0).astype(jnp.float32)[:, None, None, None]
    mirrored = jnp.flip(pole_in, 2) * sign
    south = jnp.where(band == 0, mirrored, from_south)
    north = jnp.where(band == nlat - 1, mirrored, from_north)

    slab = nf * tall * w * 4
    edges = _vmem_call(
        _edge_kernel, jax.ShapeDtypeStruct((nf, tall, w), jnp.float32), 3, [], 0, 2 * slab
    )(south, inner_edges, north)
    from_west = lax.ppermute(edges, "lon", _shift_pairs(nlon, 1, True))
    from_east = lax.ppermute(edges, "lon", _shift_pairs(nlon, -1, True))

    step_flops = 60 * nf * nlev * tall * w
    deep = tall + 2 * MARGIN
    main1 = pl.pallas_call(
        _main1_kernel,
        out_shape=jax.ShapeDtypeStruct((nlev, nf, tall, w), jnp.float32),
        grid=(nlev,),
        in_specs=[
            pl.BlockSpec((nf, 1, HALO, w), lambda l: (0, l, 0, 0)),
            pl.BlockSpec((1, rows, w), lambda l: (l, 0, 0)),
            pl.BlockSpec((2, 1, rows, w), lambda l: (0, l, 0, 0)),
            pl.BlockSpec((nf - 3, 1, rows, w), lambda l: (0, l, 0, 0)),
            pl.BlockSpec((nf, 1, HALO, w), lambda l: (0, l, 0, 0)),
            pl.BlockSpec((nlev, rows, w), lambda l: (0, 0, 0)),
            pl.BlockSpec((1, nlev, HALO, w), lambda l: (0, 0, 0, 0)),
            pl.BlockSpec((1, nlev, HALO, w), lambda l: (0, 0, 0, 0)),
            pl.BlockSpec((3, tall, w), lambda l: (0, 0, 0)),
        ],
        out_specs=pl.BlockSpec((1, nf, tall, w), lambda l: (l, 0, 0, 0)),
        scratch_shapes=[
            pltpu.VMEM((nlev, deep, w), jnp.float32),
            pltpu.VMEM((nf, deep, w), jnp.float32),
            pltpu.VMEM((nf, deep, w), jnp.float32),
        ],
        compiler_params=pltpu.CompilerParams(dimension_semantics=("arbitrary",)),
        cost_estimate=pl.CostEstimate(flops=step_flops, bytes_accessed=2 * slab * nlev, transcendentals=0),
    )(south, thickness, winds, tracer_mass, north, thickness, south, north, rowvec)

    vmem = pl.BlockSpec(memory_space=pltpu.VMEM)
    anywhere = pl.BlockSpec(memory_space=pl.ANY)
    return pl.pallas_call(
        _final_kernel,
        out_shape=(
            jax.ShapeDtypeStruct(thickness.shape, jnp.float32),
            jax.ShapeDtypeStruct(winds.shape, jnp.float32),
            jax.ShapeDtypeStruct(tracer_mass.shape, jnp.float32),
        ),
        in_specs=[anywhere, vmem, anywhere, anywhere, vmem],
        out_specs=(anywhere, anywhere, anywhere),
        scratch_shapes=[
            pltpu.VMEM((nf, nlev, deep, w), jnp.float32),
            pltpu.VMEM((nf, deep, w), jnp.float32),
            pltpu.VMEM((nf, deep, w), jnp.float32),
            pltpu.VMEM((nf, deep, w), jnp.float32),
            pltpu.VMEM((nlev, deep, w), jnp.float32),
            pltpu.VMEM((deep, w), jnp.float32),
            pltpu.VMEM((nf, deep, w), jnp.float32),
            pltpu.VMEM((nf, deep, w), jnp.float32),
            pltpu.VMEM((2, nf, tall, w), jnp.float32),
            pltpu.SemaphoreType.DMA((2,)),
            pltpu.VMEM((nlev, nf, tall, w), jnp.float32),
            pltpu.SemaphoreType.DMA((nlev,)),
            pltpu.VMEM((nlev, nf, rows, w), jnp.float32),
            pltpu.SemaphoreType.DMA((nlev, nf)),
        ],
        cost_estimate=pl.CostEstimate(
            flops=step_flops + 3 * step_flops // nlev, bytes_accessed=2 * slab * nlev, transcendentals=0
        ),
    )(main1, edges, from_west, from_east, rowvec)


def solution(mesh):
    return jax.shard_map(
        shards,
        mesh=mesh,
        in_specs=(P(None, "lat", "lon"), P(None, None, "lat", "lon"), P(None, None, "lat", "lon")),
        out_specs=(P(None, "lat", "lon"), P(None, None, "lat", "lon"), P(None, None, "lat", "lon")),
        check_vma=False,
    )
```

```python
import math

import jax
import jax.numpy as jnp
from jax import lax
from jax.experimental import pallas as pl
from jax.experimental.pallas import tpu as pltpu
from jax.sharding import PartitionSpec as P

SUBSTEPS = 2
COUR = 0.25
GRAV = 1.0
FCOR = 1.0

HALO = 2 * SUBSTEPS
GW = 6 * HALO
MARGIN = 8


def _lroll(x, k):
    n = x.shape[-1]
    return pltpu.roll(x, k % n, x.ndim - 1)


def _face(pos, behind, centre, forward, beyond):
    p = jnp.where(pos, centre, forward)
    q = jnp.where(pos, forward, centre)
    r = jnp.where(pos, behind, beyond)
    return 5.0 * p + 2.0 * q - r


def _substep(load, store, nf, pot, rv, mf_ref):
    fcos, inv_acos, cor = rv
    u = load(1, 0)
    v = load(2, 0)
    n = u.shape[0]
    fs = (COUR * 0.5 / 6.0) * (u + _lroll(u, -1))
    ms = (COUR * 0.5 / 6.0) * (v + load(2, 1)) * fcos
    fpos = fs >= 0.0
    mpos = ms >= 0.0
    for f in range(nf):
        x = u if f == 1 else (v if f == 2 else load(f, 0))
        zf = fs * _face(fpos, _lroll(x, 1), x, _lroll(x, -1), _lroll(x, -2))
        mf = ms * _face(mpos, load(f, -1), x, load(f, 1), load(f, 2))
        mf_ref[f, pl.ds(MARGIN, n)] = mf
        new = x - (zf - _lroll(zf, 1)) - (mf - mf_ref[f, pl.ds(MARGIN - 1, n)]) * inv_acos
        if f == 1:
            p0 = pot(0)
            new = new - COUR * 0.5 * (_lroll(p0, -1) - _lroll(p0, 1)) + cor * v
        elif f == 2:
            new = new - COUR * 0.5 * (pot(1) - pot(-1)) - cor * u
        store(f, new)


def _slab_of(lev, per):
    return lev // per, lev % per


def _lanes(rows, w):
    lane = lax.broadcasted_iota(jnp.int32, (rows, w), 1)
    return lane, lane // GW, lane % GW


def _pack_own(get, nlev, rows, w, slab, init):
    per = w // GW
    lane, group, kk = _lanes(rows, w)
    lo_mask = (kk >= HALO) & (kk < 3 * HALO)
    hi_mask = (kk >= 3 * HALO) & (kk < 5 * HALO)
    g = init
    for lev in range(slab * per, min(nlev, (slab + 1) * per)):
        m = get(lev)
        base = GW * (lev - slab * per)
        g = jnp.where((group == lev - slab * per) & lo_mask, _lroll(m, base + HALO), g)
        g = jnp.where((group == lev - slab * per) & hi_mask, _lroll(m, base + 3 * HALO - (w - 2 * HALO)), g)
    return g


def _packed_potential(h, nlev, w, pg_ref, n):
    per = w // GW
    nslab = len(h)
    _, group, _ = _lanes(n, w)
    below = None
    for s in reversed(range(nslab)):
        ng = min(per, nlev - s * per)
        acc = h[s]
        k = 1
        while k < ng:
            acc = acc + jnp.where(group + k < ng, _lroll(acc, -GW * k), 0.0)
            k *= 2
        if below is not None:
            spread = below
            for g in range(1, ng):
                spread = jnp.where(group == g, _lroll(below, GW * g), spread)
            acc = acc + spread
        pg_ref[s, pl.ds(MARGIN, n)] = GRAV * acc
        below = jnp.where(group == 0, acc, 0.0)


def _edge_inner_kernel(thk_ref, wind_ref, trc_ref, e_ref):
    nlev, rows, w = thk_ref.shape
    nslab, nf = e_ref.shape[0], e_ref.shape[1]
    zeros = jnp.zeros((rows, w), jnp.float32)
    for s in range(nslab):
        for f in range(nf):
            if f == 0:
                get = lambda lev: thk_ref[lev]
            elif f < 3:
                get = lambda lev, f=f: wind_ref[f - 1, lev]
            else:
                get = lambda lev, f=f: trc_ref[f - 3, lev]
            e_ref[s, f] = _pack_own(get, nlev, rows, w, s, zeros)


def _edge_kernel(south_ref, inner_ref, north_ref, e_ref):
    nf, nlev, halo, w = south_ref.shape
    nslab, rows = inner_ref.shape[0], inner_ref.shape[2]
    zeros = jnp.zeros((halo, w), jnp.float32)
    for s in range(nslab):
        for f in range(nf):
            e_ref[s, f, pl.ds(0, halo)] = _pack_own(lambda lev: south_ref[f, lev], nlev, halo, w, s, zeros)
            e_ref[s, f, pl.ds(halo, rows)] = inner_ref[s, f]
            e_ref[s, f, pl.ds(halo + rows, halo)] = _pack_own(lambda lev: north_ref[f, lev], nlev, halo, w, s, zeros)


def _main_kernel(
    south_ref, thk_ref, wind_ref, trc_ref, north_ref, tall_ref, sall_ref, nall_ref, rv_ref,
    thk_o, wind_o, trc_o, p_ref, mf_ref, sp_ref, s1_ref,
):
    nf, _, halo, w = south_ref.shape
    nlev, rows = tall_ref.shape[0], tall_ref.shape[1]
    i = pl.program_id(0)
    tall = rows + 2 * halo
    win = pl.ds(MARGIN, tall)
    top = pl.ds(MARGIN, halo)
    mid = pl.ds(MARGIN + halo, rows)
    bot = pl.ds(MARGIN + halo + rows, halo)
    rv = (rv_ref[0], rv_ref[1], rv_ref[2])

    @pl.when(i == 0)
    def _():
        acc = None
        for l in reversed(range(nlev)):
            part = (sall_ref[0, l], tall_ref[l], nall_ref[0, l])
            acc = part if acc is None else tuple(x + y for x, y in zip(acc, part))
            p_ref[l, top] = GRAV * acc[0]
            p_ref[l, mid] = GRAV * acc[1]
            p_ref[l, bot] = GRAV * acc[2]

    @pl.when(i < nlev)
    def _():
        lev = i
        for f in range(nf):
            sp_ref[f, top] = south_ref[f, 0]
            if f == 0:
                sp_ref[f, mid] = thk_ref[0]
            elif f < 3:
                sp_ref[f, mid] = wind_ref[f - 1, 0]
            else:
                sp_ref[f, mid] = trc_ref[f - 3, 0]
            sp_ref[f, bot] = north_ref[f, 0]

        def store(f, x):
            s1_ref[f, lev, win] = x

        _substep(
            lambda f, d: sp_ref[f, pl.ds(MARGIN + d, tall)],
            store,
            nf,
            lambda d: p_ref[lev, pl.ds(MARGIN + d, tall)],
            rv,
            mf_ref,
        )

    @pl.when(i == nlev)
    def _():
        acc = None
        for l in reversed(range(nlev)):
            acc = s1_ref[0, l, win] if acc is None else acc + s1_ref[0, l, win]
            p_ref[l, win] = GRAV * acc

    @pl.when(i >= nlev)
    def _():
        lev = i - nlev

        def store(f, x):
            x = x[halo : halo + rows]
            if f == 0:
                thk_o[0] = x
            elif f < 3:
                wind_o[f - 1, 0] = x
            else:
                trc_o[f - 3, 0] = x

        _substep(
            lambda f, d: s1_ref[f, lev, pl.ds(MARGIN + d, tall)],
            store,
            nf,
            lambda d: p_ref[lev, pl.ds(MARGIN + d, tall)],
            rv,
            mf_ref,
        )


def _final_kernel(
    e_ref, ew_ref, ee_ref, rv_ref, thk_i, wind_i, trc_i, thk_o, wind_o, trc_o, g0_ref, g1_ref, pg_ref, mf_ref
):
    nslab, nf, tall, w = e_ref.shape
    nlev, rows = thk_i.shape[0], thk_i.shape[1]
    per = w // GW
    rv = (rv_ref[0], rv_ref[1], rv_ref[2])
    lane, group, kk = _lanes(tall, w)
    win = pl.ds(MARGIN, tall)
    for s in range(nslab):
        for f in range(nf):
            g0_ref[s, f, win] = jnp.where(
                kk < HALO,
                _lroll(ew_ref[s, f], -4 * HALO),
                jnp.where(kk >= 5 * HALO, _lroll(ee_ref[s, f], 4 * HALO), e_ref[s, f]),
            )
    for src, dst in ((g0_ref, g1_ref), (g1_ref, g0_ref)):
        _packed_potential([src[s, 0, win] for s in range(nslab)], nlev, w, pg_ref, tall)
        for s in range(nslab):

            def store(f, x, s=s, dst=dst):
                dst[s, f, win] = x

            _substep(
                lambda f, d, s=s, src=src: src[s, f, pl.ds(MARGIN + d, tall)],
                store,
                nf,
                lambda d, s=s: pg_ref[s, pl.ds(MARGIN + d, tall)],
                rv,
                mf_ref,
            )
    lane_o = lane[:rows]
    inner = pl.ds(MARGIN + HALO, rows)
    for lev in range(nlev):
        s, g = _slab_of(lev, per)
        for f in range(nf):
            strip = g0_ref[s, f, inner]
            lo = _lroll(strip, -(GW * g + HALO))
            hi = _lroll(strip, (w - HALO) - (GW * g + 4 * HALO))
            if f == 0:
                src, dst = thk_i.at[lev], thk_o.at[lev]
            elif f < 3:
                src, dst = wind_i.at[f - 1, lev], wind_o.at[f - 1, lev]
            else:
                src, dst = trc_i.at[f - 3, lev], trc_o.at[f - 3, lev]
            dst[...] = jnp.where(lane_o < HALO, lo, jnp.where(lane_o >= w - HALO, hi, src[...]))


def _shift_pairs(n, d, closed):
    return [(i, (i + d) % n) for i in range(n) if closed or 0 <= i + d < n]


def _vmem_call(kernel, out_shape, n_in, scratch, flops, nbytes):
    vmem = pl.BlockSpec(memory_space=pltpu.VMEM)
    return pl.pallas_call(
        kernel,
        out_shape=out_shape,
        in_specs=[vmem] * n_in,
        out_specs=tuple(vmem for _ in out_shape) if isinstance(out_shape, tuple) else vmem,
        scratch_shapes=scratch,
        cost_estimate=pl.CostEstimate(flops=flops, bytes_accessed=nbytes, transcendentals=0),
    )


def shards(thickness, winds, tracer_mass):
    fields = jnp.concatenate([thickness[None], winds, tracer_mass], 0)
    nf, nlev, rows, w = fields.shape
    nlat = lax.axis_size("lat")
    nlon = lax.axis_size("lon")
    band = lax.axis_index("lat")
    spacing = math.pi / (rows * nlat)
    tall = rows + 2 * HALO
    deep = tall + 2 * MARGIN
    per = w // GW
    nslab = -(-nlev // per)

    row_index = (jnp.arange(tall) + (band * rows - HALO)).astype(jnp.float32)
    center_lat = (row_index + 0.5) * spacing - 0.5 * math.pi
    face_lat = (row_index + 1.0) * spacing - 0.5 * math.pi
    center_cos = jnp.cos(center_lat)
    rowvec = jnp.stack(
        [
            jnp.abs(jnp.cos(face_lat)),
            1.0 / jnp.abs(center_cos),
            COUR * FCOR * jnp.sin(center_lat) * jnp.where(center_cos >= 0.0, 1.0, -1.0),
        ]
    )
    rowvec = jnp.broadcast_to(rowvec[:, :, None], (3, tall, w))

    inner_edges = _vmem_call(
        _edge_inner_kernel, jax.ShapeDtypeStruct((nslab, nf, rows, w), jnp.float32), 3, [], 0, nf * nlev * rows * w * 4
    )(thickness, winds, tracer_mass)

    top = fields[:, :, rows - HALO :]
    bottom = fields[:, :, :HALO]
    from_south = lax.ppermute(top, "lat", _shift_pairs(nlat, 1, False))
    from_north = lax.ppermute(bottom, "lat", _shift_pairs(nlat, -1, False))
    half = nlon // 2
    pole_pairs = []
    for b in (0, nlat - 1):
        for s in range(nlon):
            pole_pairs.append((b * nlon + s, b * nlon + (s + half) % nlon))
    pole_out = jnp.where(band == 0, bottom, top)
    pole_in = lax.ppermute(pole_out, ("lat", "lon"), pole_pairs)
    sign = jnp.where(jnp.arange(nf) == 2, -1.0, 1.0).astype(jnp.float32)[:, None, None, None]
    mirrored = jnp.flip(pole_in, 2) * sign
    south = jnp.where(band == 0, mirrored, from_south)
    north = jnp.where(band == nlat - 1, mirrored, from_north)

    slab = nf * tall * w * 4
    edges = _vmem_call(
        _edge_kernel, jax.ShapeDtypeStruct((nslab, nf, tall, w), jnp.float32), 3, [], 0, 2 * slab * nslab
    )(south, inner_edges, north)
    from_west = lax.ppermute(edges, "lon", _shift_pairs(nlon, 1, True))
    from_east = lax.ppermute(edges, "lon", _shift_pairs(nlon, -1, True))

    step_flops = 60 * nf * nlev * tall * w
    first = lambda i: jnp.minimum(i, nlev - 1)
    second = lambda i: jnp.maximum(i - nlev, 0)
    raw = pl.pallas_call(
        _main_kernel,
        out_shape=(
            jax.ShapeDtypeStruct(thickness.shape, jnp.float32),
            jax.ShapeDtypeStruct(winds.shape, jnp.float32),
            jax.ShapeDtypeStruct(tracer_mass.shape, jnp.float32),
        ),
        grid=(2 * nlev,),
        in_specs=[
            pl.BlockSpec((nf, 1, HALO, w), lambda i: (0, first(i), 0, 0)),
            pl.BlockSpec((1, rows, w), lambda i: (first(i), 0, 0)),
            pl.BlockSpec((2, 1, rows, w), lambda i: (0, first(i), 0, 0)),
            pl.BlockSpec((nf - 3, 1, rows, w), lambda i: (0, first(i), 0, 0)),
            pl.BlockSpec((nf, 1, HALO, w), lambda i: (0, first(i), 0, 0)),
            pl.BlockSpec((nlev, rows, w), lambda i: (0, 0, 0)),
            pl.BlockSpec((1, nlev, HALO, w), lambda i: (0, 0, 0, 0)),
            pl.BlockSpec((1, nlev, HALO, w), lambda i: (0, 0, 0, 0)),
            pl.BlockSpec((3, tall, w), lambda i: (0, 0, 0)),
        ],
        out_specs=(
            pl.BlockSpec((1, rows, w), lambda i: (second(i), 0, 0)),
            pl.BlockSpec((2, 1, rows, w), lambda i: (0, second(i), 0, 0)),
            pl.BlockSpec((nf - 3, 1, rows, w), lambda i: (0, second(i), 0, 0)),
        ),
        scratch_shapes=[
            pltpu.VMEM((nlev, deep, w), jnp.float32),
            pltpu.VMEM((nf, deep, w), jnp.float32),
            pltpu.VMEM((nf, deep, w), jnp.float32),
            pltpu.VMEM((nf, nlev, deep, w), jnp.float32),
        ],
        compiler_params=pltpu.CompilerParams(dimension_semantics=("arbitrary",)),
        cost_estimate=pl.CostEstimate(flops=2 * step_flops, bytes_accessed=2 * slab * nlev, transcendentals=0),
    )(south, thickness, winds, tracer_mass, north, thickness, south, north, rowvec)

    return _vmem_call(
        _final_kernel,
        (
            jax.ShapeDtypeStruct(thickness.shape, jnp.float32),
            jax.ShapeDtypeStruct(winds.shape, jnp.float32),
            jax.ShapeDtypeStruct(tracer_mass.shape, jnp.float32),
        ),
        7,
        [
            pltpu.VMEM((nslab, nf, deep, w), jnp.float32),
            pltpu.VMEM((nslab, nf, deep, w), jnp.float32),
            pltpu.VMEM((nslab, deep, w), jnp.float32),
            pltpu.VMEM((nf, deep, w), jnp.float32),
        ],
        4 * step_flops // nlev,
        4 * slab * nslab,
    )(edges, from_west, from_east, rowvec, *raw)


def solution(mesh):
    return jax.shard_map(
        shards,
        mesh=mesh,
        in_specs=(P(None, "lat", "lon"), P(None, None, "lat", "lon"), P(None, None, "lat", "lon")),
        out_specs=(P(None, "lat", "lon"), P(None, None, "lat", "lon"), P(None, None, "lat", "lon")),
        check_vma=False,
    )
```

```python
import math

import jax
import jax.numpy as jnp
from jax import lax
from jax.experimental import pallas as pl
from jax.experimental.pallas import tpu as pltpu
from jax.sharding import PartitionSpec as P

SUBSTEPS = 2
COUR = 0.25
GRAV = 1.0
FCOR = 1.0

HALO = 2 * SUBSTEPS
GW = 6 * HALO
MARGIN = 8


def _lroll(x, k):
    n = x.shape[-1]
    return pltpu.roll(x, k % n, x.ndim - 1)


def _face(pos, behind, centre, forward, beyond):
    p = jnp.where(pos, centre, forward)
    q = jnp.where(pos, forward, centre)
    r = jnp.where(pos, behind, beyond)
    return 5.0 * p + 2.0 * q - r


def _substep(load, store, nf, pot, rv, mf_ref):
    fcos, inv_acos, cor = rv
    u = load(1, 0)
    v = load(2, 0)
    n = u.shape[0]
    fs = (COUR * 0.5 / 6.0) * (u + _lroll(u, -1))
    ms = (COUR * 0.5 / 6.0) * (v + load(2, 1)) * fcos
    fpos = fs >= 0.0
    mpos = ms >= 0.0
    for f in range(nf):
        x = u if f == 1 else (v if f == 2 else load(f, 0))
        zf = fs * _face(fpos, _lroll(x, 1), x, _lroll(x, -1), _lroll(x, -2))
        mf = ms * _face(mpos, load(f, -1), x, load(f, 1), load(f, 2))
        mf_ref[f, pl.ds(MARGIN, n)] = mf
        new = x - (zf - _lroll(zf, 1)) - (mf - mf_ref[f, pl.ds(MARGIN - 1, n)]) * inv_acos
        if f == 1:
            p0 = pot(0)
            new = new - COUR * 0.5 * (_lroll(p0, -1) - _lroll(p0, 1)) + cor * v
        elif f == 2:
            new = new - COUR * 0.5 * (pot(1) - pot(-1)) - cor * u
        store(f, new)


def _slab_of(lev, per):
    return lev // per, lev % per


def _lanes(rows, w):
    lane = lax.broadcasted_iota(jnp.int32, (rows, w), 1)
    return lane, lane // GW, lane % GW


def _pack_own(get, nlev, rows, w, slab, init):
    per = w // GW
    lane, group, kk = _lanes(rows, w)
    lo_mask = (kk >= HALO) & (kk < 3 * HALO)
    hi_mask = (kk >= 3 * HALO) & (kk < 5 * HALO)
    g = init
    for lev in range(slab * per, min(nlev, (slab + 1) * per)):
        m = get(lev)
        base = GW * (lev - slab * per)
        g = jnp.where((group == lev - slab * per) & lo_mask, _lroll(m, base + HALO), g)
        g = jnp.where((group == lev - slab * per) & hi_mask, _lroll(m, base + 3 * HALO - (w - 2 * HALO)), g)
    return g


def _packed_potential(h, nlev, w, pg_ref, n):
    per = w // GW
    nslab = len(h)
    _, group, _ = _lanes(n, w)
    below = None
    for s in reversed(range(nslab)):
        ng = min(per, nlev - s * per)
        acc = h[s]
        k = 1
        while k < ng:
            acc = acc + jnp.where(group + k < ng, _lroll(acc, -GW * k), 0.0)
            k *= 2
        if below is not None:
            spread = below
            for g in range(1, ng):
                spread = jnp.where(group == g, _lroll(below, GW * g), spread)
            acc = acc + spread
        pg_ref[s, pl.ds(MARGIN, n)] = GRAV * acc
        below = jnp.where(group == 0, acc, 0.0)


def _edge_inner_kernel(thk_ref, wind_ref, trc_ref, rvi_ref, e_ref, rv_ref):
    rv_ref[...] = rvi_ref[...]
    nlev, rows, w = thk_ref.shape
    nslab, nf = e_ref.shape[0], e_ref.shape[1]
    zeros = jnp.zeros((rows, w), jnp.float32)
    for s in range(nslab):
        for f in range(nf):
            if f == 0:
                get = lambda lev: thk_ref[lev]
            elif f < 3:
                get = lambda lev, f=f: wind_ref[f - 1, lev]
            else:
                get = lambda lev, f=f: trc_ref[f - 3, lev]
            e_ref[s, f] = _pack_own(get, nlev, rows, w, s, zeros)


def _edge_kernel(south_ref, inner_ref, north_ref, e_ref):
    nf, nlev, halo, w = south_ref.shape
    nslab, rows = inner_ref.shape[0], inner_ref.shape[2]
    zeros = jnp.zeros((halo, w), jnp.float32)
    for s in range(nslab):
        for f in range(nf):
            e_ref[s, f, pl.ds(0, halo)] = _pack_own(lambda lev: south_ref[f, lev], nlev, halo, w, s, zeros)
            e_ref[s, f, pl.ds(halo, rows)] = inner_ref[s, f]
            e_ref[s, f, pl.ds(halo + rows, halo)] = _pack_own(lambda lev: north_ref[f, lev], nlev, halo, w, s, zeros)


def _main_kernel(
    south_ref, thk_ref, wind_ref, trc_ref, north_ref, tall_ref, sall_ref, nall_ref, rv_ref,
    thk_o, wind_o, trc_o, p_ref, mf_ref, sp_ref, s1_ref,
):
    nf, _, halo, w = south_ref.shape
    nlev, rows = tall_ref.shape[0], tall_ref.shape[1]
    i = pl.program_id(0)
    tall = rows + 2 * halo
    win = pl.ds(MARGIN, tall)
    top = pl.ds(MARGIN, halo)
    mid = pl.ds(MARGIN + halo, rows)
    bot = pl.ds(MARGIN + halo + rows, halo)
    rv = (rv_ref[0], rv_ref[1], rv_ref[2])

    @pl.when(i == 0)
    def _():
        acc = None
        for l in reversed(range(nlev)):
            part = (sall_ref[0, l], tall_ref[l], nall_ref[0, l])
            acc = part if acc is None else tuple(x + y for x, y in zip(acc, part))
            p_ref[l, top] = GRAV * acc[0]
            p_ref[l, mid] = GRAV * acc[1]
            p_ref[l, bot] = GRAV * acc[2]

    @pl.when(i < nlev)
    def _():
        lev = i
        for f in range(nf):
            sp_ref[f, top] = south_ref[f, 0]
            if f == 0:
                sp_ref[f, mid] = thk_ref[0]
            elif f < 3:
                sp_ref[f, mid] = wind_ref[f - 1, 0]
            else:
                sp_ref[f, mid] = trc_ref[f - 3, 0]
            sp_ref[f, bot] = north_ref[f, 0]

        def store(f, x):
            s1_ref[f, lev, win] = x

        _substep(
            lambda f, d: sp_ref[f, pl.ds(MARGIN + d, tall)],
            store,
            nf,
            lambda d: p_ref[lev, pl.ds(MARGIN + d, tall)],
            rv,
            mf_ref,
        )

    @pl.when(i == nlev)
    def _():
        acc = None
        for l in reversed(range(nlev)):
            acc = s1_ref[0, l, win] if acc is None else acc + s1_ref[0, l, win]
            p_ref[l, win] = GRAV * acc

    @pl.when(i >= nlev)
    def _():
        lev = i - nlev

        def store(f, x):
            x = x[halo : halo + rows]
            if f == 0:
                thk_o[0] = x
            elif f < 3:
                wind_o[f - 1, 0] = x
            else:
                trc_o[f - 3, 0] = x

        _substep(
            lambda f, d: s1_ref[f, lev, pl.ds(MARGIN + d, tall)],
            store,
            nf,
            lambda d: p_ref[lev, pl.ds(MARGIN + d, tall)],
            rv,
            mf_ref,
        )


def _final_kernel(
    e_ref, ew_ref, ee_ref, rv_ref, thk_i, wind_i, trc_i, thk_o, wind_o, trc_o, g0_ref, g1_ref, pg_ref, mf_ref,
    buf_ref, in_sem, out_sem,
):
    nslab, nf, tall, w = e_ref.shape
    nlev, rows = thk_i.shape[0], thk_i.shape[1]

    def hbm(refs, f, lev):
        t, wd, tr = refs
        return t.at[lev] if f == 0 else (wd.at[f - 1, lev] if f < 3 else tr.at[f - 3, lev])

    ins = {}
    for lev in range(nlev):
        for f in range(nf):
            ins[lev, f] = pltpu.make_async_copy(hbm((thk_i, wind_i, trc_i), f, lev), buf_ref.at[lev, f], in_sem.at[lev, f])
            ins[lev, f].start()
    per = w // GW
    rv = (rv_ref[0], rv_ref[1], rv_ref[2])
    lane, group, kk = _lanes(tall, w)
    win = pl.ds(MARGIN, tall)
    for s in range(nslab):
        for f in range(nf):
            g0_ref[s, f, win] = jnp.where(
                kk < HALO,
                _lroll(ew_ref[s, f], -4 * HALO),
                jnp.where(kk >= 5 * HALO, _lroll(ee_ref[s, f], 4 * HALO), e_ref[s, f]),
            )
    for src, dst in ((g0_ref, g1_ref), (g1_ref, g0_ref)):
        _packed_potential([src[s, 0, win] for s in range(nslab)], nlev, w, pg_ref, tall)
        for s in range(nslab):

            def store(f, x, s=s, dst=dst):
                dst[s, f, win] = x

            _substep(
                lambda f, d, s=s, src=src: src[s, f, pl.ds(MARGIN + d, tall)],
                store,
                nf,
                lambda d, s=s: pg_ref[s, pl.ds(MARGIN + d, tall)],
                rv,
                mf_ref,
            )
    lane_o = lane[:rows]
    inner = pl.ds(MARGIN + HALO, rows)
    outs = []
    for lev in range(nlev):
        s, g = _slab_of(lev, per)
        for f in range(nf):
            strip = g0_ref[s, f, inner]
            lo = _lroll(strip, -(GW * g + HALO))
            hi = _lroll(strip, (w - HALO) - (GW * g + 4 * HALO))
            ins[lev, f].wait()
            buf_ref[lev, f] = jnp.where(lane_o < HALO, lo, jnp.where(lane_o >= w - HALO, hi, buf_ref[lev, f]))
            outs.append(pltpu.make_async_copy(buf_ref.at[lev, f], hbm((thk_o, wind_o, trc_o), f, lev), out_sem.at[lev, f]))
            outs[-1].start()
    for c in outs:
        c.wait()


def _shift_pairs(n, d, closed):
    return [(i, (i + d) % n) for i in range(n) if closed or 0 <= i + d < n]


def _vmem_call(kernel, out_shape, n_in, scratch, flops, nbytes):
    vmem = pl.BlockSpec(memory_space=pltpu.VMEM)
    return pl.pallas_call(
        kernel,
        out_shape=out_shape,
        in_specs=[vmem] * n_in,
        out_specs=tuple(vmem for _ in out_shape) if isinstance(out_shape, tuple) else vmem,
        scratch_shapes=scratch,
        cost_estimate=pl.CostEstimate(flops=flops, bytes_accessed=nbytes, transcendentals=0),
    )


def shards(thickness, winds, tracer_mass):
    fields = jnp.concatenate([thickness[None], winds, tracer_mass], 0)
    nf, nlev, rows, w = fields.shape
    nlat = lax.axis_size("lat")
    nlon = lax.axis_size("lon")
    band = lax.axis_index("lat")
    spacing = math.pi / (rows * nlat)
    tall = rows + 2 * HALO
    deep = tall + 2 * MARGIN
    per = w // GW
    nslab = -(-nlev // per)

    row_index = (jnp.arange(tall) + (band * rows - HALO)).astype(jnp.float32)
    center_lat = (row_index + 0.5) * spacing - 0.5 * math.pi
    face_lat = (row_index + 1.0) * spacing - 0.5 * math.pi
    center_cos = jnp.cos(center_lat)
    rowvec = jnp.stack(
        [
            jnp.abs(jnp.cos(face_lat)),
            1.0 / jnp.abs(center_cos),
            COUR * FCOR * jnp.sin(center_lat) * jnp.where(center_cos >= 0.0, 1.0, -1.0),
        ]
    )
    rowvec = jnp.broadcast_to(rowvec[:, :, None], (3, tall, w))

    inner_edges, rowvec = _vmem_call(
        _edge_inner_kernel,
        (jax.ShapeDtypeStruct((nslab, nf, rows, w), jnp.float32), jax.ShapeDtypeStruct(rowvec.shape, jnp.float32)),
        4,
        [],
        0,
        nf * nlev * rows * w * 4,
    )(thickness, winds, tracer_mass, rowvec)

    top = fields[:, :, rows - HALO :]
    bottom = fields[:, :, :HALO]
    from_south = lax.ppermute(top, "lat", _shift_pairs(nlat, 1, False))
    from_north = lax.ppermute(bottom, "lat", _shift_pairs(nlat, -1, False))
    half = nlon // 2
    pole_pairs = []
    for b in (0, nlat - 1):
        for s in range(nlon):
            pole_pairs.append((b * nlon + s, b * nlon + (s + half) % nlon))
    pole_out = jnp.where(band == 0, bottom, top)
    pole_in = lax.ppermute(pole_out, ("lat", "lon"), pole_pairs)
    sign = jnp.where(jnp.arange(nf) == 2, -1.0, 1.0).astype(jnp.float32)[:, None, None, None]
    mirrored = jnp.flip(pole_in, 2) * sign
    south = jnp.where(band == 0, mirrored, from_south)
    north = jnp.where(band == nlat - 1, mirrored, from_north)

    slab = nf * tall * w * 4
    edges = _vmem_call(
        _edge_kernel, jax.ShapeDtypeStruct((nslab, nf, tall, w), jnp.float32), 3, [], 0, 2 * slab * nslab
    )(south, inner_edges, north)
    from_west = lax.ppermute(edges, "lon", _shift_pairs(nlon, 1, True))
    from_east = lax.ppermute(edges, "lon", _shift_pairs(nlon, -1, True))

    step_flops = 60 * nf * nlev * tall * w
    first = lambda i: jnp.minimum(i, nlev - 1)
    second = lambda i: jnp.maximum(i - nlev, 0)
    raw = pl.pallas_call(
        _main_kernel,
        out_shape=(
            jax.ShapeDtypeStruct(thickness.shape, jnp.float32),
            jax.ShapeDtypeStruct(winds.shape, jnp.float32),
            jax.ShapeDtypeStruct(tracer_mass.shape, jnp.float32),
        ),
        grid=(2 * nlev,),
        in_specs=[
            pl.BlockSpec((nf, 1, HALO, w), lambda i: (0, first(i), 0, 0)),
            pl.BlockSpec((1, rows, w), lambda i: (first(i), 0, 0)),
            pl.BlockSpec((2, 1, rows, w), lambda i: (0, first(i), 0, 0)),
            pl.BlockSpec((nf - 3, 1, rows, w), lambda i: (0, first(i), 0, 0)),
            pl.BlockSpec((nf, 1, HALO, w), lambda i: (0, first(i), 0, 0)),
            pl.BlockSpec((nlev, rows, w), lambda i: (0, 0, 0)),
            pl.BlockSpec((1, nlev, HALO, w), lambda i: (0, 0, 0, 0)),
            pl.BlockSpec((1, nlev, HALO, w), lambda i: (0, 0, 0, 0)),
            pl.BlockSpec((3, tall, w), lambda i: (0, 0, 0)),
        ],
        out_specs=(
            pl.BlockSpec((1, rows, w), lambda i: (second(i), 0, 0)),
            pl.BlockSpec((2, 1, rows, w), lambda i: (0, second(i), 0, 0)),
            pl.BlockSpec((nf - 3, 1, rows, w), lambda i: (0, second(i), 0, 0)),
        ),
        scratch_shapes=[
            pltpu.VMEM((nlev, deep, w), jnp.float32),
            pltpu.VMEM((nf, deep, w), jnp.float32),
            pltpu.VMEM((nf, deep, w), jnp.float32),
            pltpu.VMEM((nf, nlev, deep, w), jnp.float32),
        ],
        compiler_params=pltpu.CompilerParams(dimension_semantics=("arbitrary",)),
        cost_estimate=pl.CostEstimate(flops=2 * step_flops, bytes_accessed=2 * slab * nlev, transcendentals=0),
    )(south, thickness, winds, tracer_mass, north, thickness, south, north, rowvec)

    vmem = pl.BlockSpec(memory_space=pltpu.VMEM)
    anywhere = pl.BlockSpec(memory_space=pl.ANY)
    return pl.pallas_call(
        _final_kernel,
        out_shape=(
            jax.ShapeDtypeStruct(thickness.shape, jnp.float32),
            jax.ShapeDtypeStruct(winds.shape, jnp.float32),
            jax.ShapeDtypeStruct(tracer_mass.shape, jnp.float32),
        ),
        in_specs=[vmem] * 4 + [anywhere] * 3,
        out_specs=(anywhere, anywhere, anywhere),
        input_output_aliases={4: 0, 5: 1, 6: 2},
        scratch_shapes=[
            pltpu.VMEM((nslab, nf, deep, w), jnp.float32),
            pltpu.VMEM((nslab, nf, deep, w), jnp.float32),
            pltpu.VMEM((nslab, deep, w), jnp.float32),
            pltpu.VMEM((nf, deep, w), jnp.float32),
            pltpu.VMEM((nlev, nf, rows, w), jnp.float32),
            pltpu.SemaphoreType.DMA((nlev, nf)),
            pltpu.SemaphoreType.DMA((nlev, nf)),
        ],
        cost_estimate=pl.CostEstimate(flops=4 * step_flops // nlev, bytes_accessed=4 * slab * nslab, transcendentals=0),
    )(edges, from_west, from_east, rowvec, *raw)


def solution(mesh):
    return jax.shard_map(
        shards,
        mesh=mesh,
        in_specs=(P(None, "lat", "lon"), P(None, None, "lat", "lon"), P(None, None, "lat", "lon")),
        out_specs=(P(None, "lat", "lon"), P(None, None, "lat", "lon"), P(None, None, "lat", "lon")),
        check_vma=False,
    )
```

```python
import math

import jax
import jax.numpy as jnp
from jax import lax
from jax.experimental import pallas as pl
from jax.experimental.pallas import tpu as pltpu
from jax.sharding import PartitionSpec as P

SUBSTEPS = 2
COUR = 0.25
GRAV = 1.0
FCOR = 1.0

HALO = 2 * SUBSTEPS
GW = 6 * HALO
MARGIN = 8


def _lroll(x, k):
    n = x.shape[-1]
    return pltpu.roll(x, k % n, x.ndim - 1)


def _face(pos, behind, centre, forward, beyond):
    p = jnp.where(pos, centre, forward)
    q = jnp.where(pos, forward, centre)
    r = jnp.where(pos, behind, beyond)
    return 5.0 * p + 2.0 * q - r


def _substep(load, store, nf, pot, rv, mf_ref):
    fcos, inv_acos, cor = rv
    u = load(1, 0)
    v = load(2, 0)
    n = u.shape[0]
    fs = (COUR * 0.5 / 6.0) * (u + _lroll(u, -1))
    ms = (COUR * 0.5 / 6.0) * (v + load(2, 1)) * fcos
    fpos = fs >= 0.0
    mpos = ms >= 0.0
    for f in range(nf):
        x = u if f == 1 else (v if f == 2 else load(f, 0))
        zf = fs * _face(fpos, _lroll(x, 1), x, _lroll(x, -1), _lroll(x, -2))
        mf = ms * _face(mpos, load(f, -1), x, load(f, 1), load(f, 2))
        mf_ref[f, pl.ds(MARGIN, n)] = mf
        new = x - (zf - _lroll(zf, 1)) - (mf - mf_ref[f, pl.ds(MARGIN - 1, n)]) * inv_acos
        if f == 1:
            p0 = pot(0)
            new = new - COUR * 0.5 * (_lroll(p0, -1) - _lroll(p0, 1)) + cor * v
        elif f == 2:
            new = new - COUR * 0.5 * (pot(1) - pot(-1)) - cor * u
        store(f, new)


def _slab_of(lev, per):
    return lev // per, lev % per


def _lanes(rows, w):
    lane = lax.broadcasted_iota(jnp.int32, (rows, w), 1)
    return lane, lane // GW, lane % GW


def _pack_own(get, nlev, rows, w, slab, init):
    per = w // GW
    lane, group, kk = _lanes(rows, w)
    lo_mask = (kk >= HALO) & (kk < 3 * HALO)
    hi_mask = (kk >= 3 * HALO) & (kk < 5 * HALO)
    g = init
    for lev in range(slab * per, min(nlev, (slab + 1) * per)):
        m = get(lev)
        base = GW * (lev - slab * per)
        g = jnp.where((group == lev - slab * per) & lo_mask, _lroll(m, base + HALO), g)
        g = jnp.where((group == lev - slab * per) & hi_mask, _lroll(m, base + 3 * HALO - (w - 2 * HALO)), g)
    return g


def _packed_potential(h, nlev, w, pg_ref, n):
    per = w // GW
    nslab = len(h)
    _, group, _ = _lanes(n, w)
    below = None
    for s in reversed(range(nslab)):
        ng = min(per, nlev - s * per)
        acc = h[s]
        k = 1
        while k < ng:
            acc = acc + jnp.where(group + k < ng, _lroll(acc, -GW * k), 0.0)
            k *= 2
        if below is not None:
            spread = below
            for g in range(1, ng):
                spread = jnp.where(group == g, _lroll(below, GW * g), spread)
            acc = acc + spread
        pg_ref[s, pl.ds(MARGIN, n)] = GRAV * acc
        below = jnp.where(group == 0, acc, 0.0)


def _edge_inner_kernel(thk_ref, wind_ref, trc_ref, e_ref):
    nlev, rows, w = thk_ref.shape
    nslab, nf = e_ref.shape[0], e_ref.shape[1]
    zeros = jnp.zeros((rows, w), jnp.float32)
    for s in range(nslab):
        for f in range(nf):
            if f == 0:
                get = lambda lev: thk_ref[lev]
            elif f < 3:
                get = lambda lev, f=f: wind_ref[f - 1, lev]
            else:
                get = lambda lev, f=f: trc_ref[f - 3, lev]
            e_ref[s, f] = _pack_own(get, nlev, rows, w, s, zeros)


def _edge_kernel(south_ref, inner_ref, north_ref, e_ref):
    nf, nlev, halo, w = south_ref.shape
    nslab, rows = inner_ref.shape[0], inner_ref.shape[2]
    zeros = jnp.zeros((halo, w), jnp.float32)
    for s in range(nslab):
        for f in range(nf):
            e_ref[s, f, pl.ds(0, halo)] = _pack_own(lambda lev: south_ref[f, lev], nlev, halo, w, s, zeros)
            e_ref[s, f, pl.ds(halo, rows)] = inner_ref[s, f]
            e_ref[s, f, pl.ds(halo + rows, halo)] = _pack_own(lambda lev: north_ref[f, lev], nlev, halo, w, s, zeros)


def _main_kernel(
    south_ref, thk_ref, wind_ref, trc_ref, north_ref, tall_ref, sall_ref, nall_ref, rv_ref,
    thk_o, wind_o, trc_o, p_ref, mf_ref, sp_ref, s1_ref,
):
    nf, _, halo, w = south_ref.shape
    nlev, rows = tall_ref.shape[0], tall_ref.shape[1]
    i = pl.program_id(0)
    tall = rows + 2 * halo
    win = pl.ds(MARGIN, tall)
    top = pl.ds(MARGIN, halo)
    mid = pl.ds(MARGIN + halo, rows)
    bot = pl.ds(MARGIN + halo + rows, halo)
    rv = (rv_ref[0], rv_ref[1], rv_ref[2])

    @pl.when(i == 0)
    def _():
        acc = None
        for l in reversed(range(nlev)):
            part = (sall_ref[0, l], tall_ref[l], nall_ref[0, l])
            acc = part if acc is None else tuple(x + y for x, y in zip(acc, part))
            p_ref[l, top] = GRAV * acc[0]
            p_ref[l, mid] = GRAV * acc[1]
            p_ref[l, bot] = GRAV * acc[2]

    @pl.when(i < nlev)
    def _():
        lev = i
        for f in range(nf):
            sp_ref[f, top] = south_ref[f, 0]
            if f == 0:
                sp_ref[f, mid] = thk_ref[0]
            elif f < 3:
                sp_ref[f, mid] = wind_ref[f - 1, 0]
            else:
                sp_ref[f, mid] = trc_ref[f - 3, 0]
            sp_ref[f, bot] = north_ref[f, 0]

        def store(f, x):
            s1_ref[f, lev, win] = x

        _substep(
            lambda f, d: sp_ref[f, pl.ds(MARGIN + d, tall)],
            store,
            nf,
            lambda d: p_ref[lev, pl.ds(MARGIN + d, tall)],
            rv,
            mf_ref,
        )

    @pl.when(i == nlev)
    def _():
        acc = None
        for l in reversed(range(nlev)):
            acc = s1_ref[0, l, win] if acc is None else acc + s1_ref[0, l, win]
            p_ref[l, win] = GRAV * acc

    @pl.when(i >= nlev)
    def _():
        lev = i - nlev

        def store(f, x):
            x = x[halo : halo + rows]
            if f == 0:
                thk_o[0] = x
            elif f < 3:
                wind_o[f - 1, 0] = x
            else:
                trc_o[f - 3, 0] = x

        _substep(
            lambda f, d: s1_ref[f, lev, pl.ds(MARGIN + d, tall)],
            store,
            nf,
            lambda d: p_ref[lev, pl.ds(MARGIN + d, tall)],
            rv,
            mf_ref,
        )


def _final_kernel(
    e_ref, ew_ref, ee_ref, rv_ref, thk_h, wind_h, trc_h, thk_oh, wind_oh, trc_oh, g0_ref, g1_ref, pg_ref, mf_ref,
    thk_i, wind_i, trc_i, sem,
):
    nslab, nf, tall, w = e_ref.shape
    nlev, rows = thk_i.shape[0], thk_i.shape[1]
    ins = [pltpu.make_async_copy(h, v, sem.at[k]) for k, (h, v) in enumerate(zip((thk_h, wind_h, trc_h), (thk_i, wind_i, trc_i)))]
    for c in ins:
        c.start()
    thk_o, wind_o, trc_o = thk_i, wind_i, trc_i
    per = w // GW
    rv = (rv_ref[0], rv_ref[1], rv_ref[2])
    lane, group, kk = _lanes(tall, w)
    win = pl.ds(MARGIN, tall)
    for s in range(nslab):
        for f in range(nf):
            g0_ref[s, f, win] = jnp.where(
                kk < HALO,
                _lroll(ew_ref[s, f], -4 * HALO),
                jnp.where(kk >= 5 * HALO, _lroll(ee_ref[s, f], 4 * HALO), e_ref[s, f]),
            )
    for src, dst in ((g0_ref, g1_ref), (g1_ref, g0_ref)):
        _packed_potential([src[s, 0, win] for s in range(nslab)], nlev, w, pg_ref, tall)
        for s in range(nslab):

            def store(f, x, s=s, dst=dst):
                dst[s, f, win] = x

            _substep(
                lambda f, d, s=s, src=src: src[s, f, pl.ds(MARGIN + d, tall)],
                store,
                nf,
                lambda d, s=s: pg_ref[s, pl.ds(MARGIN + d, tall)],
                rv,
                mf_ref,
            )
    lane_o = lane[:rows]
    inner = pl.ds(MARGIN + HALO, rows)
    for c in ins:
        c.wait()
    for lev in range(nlev):
        s, g = _slab_of(lev, per)
        for f in range(nf):
            strip = g0_ref[s, f, inner]
            lo = _lroll(strip, -(GW * g + HALO))
            hi = _lroll(strip, (w - HALO) - (GW * g + 4 * HALO))
            if f == 0:
                src, dst = thk_i.at[lev], thk_o.at[lev]
            elif f < 3:
                src, dst = wind_i.at[f - 1, lev], wind_o.at[f - 1, lev]
            else:
                src, dst = trc_i.at[f - 3, lev], trc_o.at[f - 3, lev]
            dst[...] = jnp.where(lane_o < HALO, lo, jnp.where(lane_o >= w - HALO, hi, src[...]))
    outs = [pltpu.make_async_copy(v, h, sem.at[3 + k]) for k, (v, h) in enumerate(zip((thk_i, wind_i, trc_i), (thk_oh, wind_oh, trc_oh)))]
    for c in outs:
        c.start()
    for c in outs:
        c.wait()


def _shift_pairs(n, d, closed):
    return [(i, (i + d) % n) for i in range(n) if closed or 0 <= i + d < n]


def _vmem_call(kernel, out_shape, n_in, scratch, flops, nbytes):
    vmem = pl.BlockSpec(memory_space=pltpu.VMEM)
    return pl.pallas_call(
        kernel,
        out_shape=out_shape,
        in_specs=[vmem] * n_in,
        out_specs=tuple(vmem for _ in out_shape) if isinstance(out_shape, tuple) else vmem,
        scratch_shapes=scratch,
        cost_estimate=pl.CostEstimate(flops=flops, bytes_accessed=nbytes, transcendentals=0),
    )


def shards(thickness, winds, tracer_mass):
    fields = jnp.concatenate([thickness[None], winds, tracer_mass], 0)
    nf, nlev, rows, w = fields.shape
    nlat = lax.axis_size("lat")
    nlon = lax.axis_size("lon")
    band = lax.axis_index("lat")
    spacing = math.pi / (rows * nlat)
    tall = rows + 2 * HALO
    deep = tall + 2 * MARGIN
    per = w // GW
    nslab = -(-nlev // per)

    row_index = (jnp.arange(tall) + (band * rows - HALO)).astype(jnp.float32)
    center_lat = (row_index + 0.5) * spacing - 0.5 * math.pi
    face_lat = (row_index + 1.0) * spacing - 0.5 * math.pi
    center_cos = jnp.cos(center_lat)
    rowvec = jnp.stack(
        [
            jnp.abs(jnp.cos(face_lat)),
            1.0 / jnp.abs(center_cos),
            COUR * FCOR * jnp.sin(center_lat) * jnp.where(center_cos >= 0.0, 1.0, -1.0),
        ]
    )
    rowvec = jnp.broadcast_to(rowvec[:, :, None], (3, tall, w))

    inner_edges = _vmem_call(
        _edge_inner_kernel, jax.ShapeDtypeStruct((nslab, nf, rows, w), jnp.float32), 3, [], 0, nf * nlev * rows * w * 4
    )(thickness, winds, tracer_mass)

    top = fields[:, :, rows - HALO :]
    bottom = fields[:, :, :HALO]
    from_south = lax.ppermute(top, "lat", _shift_pairs(nlat, 1, False))
    from_north = lax.ppermute(bottom, "lat", _shift_pairs(nlat, -1, False))
    half = nlon // 2
    pole_pairs = []
    for b in (0, nlat - 1):
        for s in range(nlon):
            pole_pairs.append((b * nlon + s, b * nlon + (s + half) % nlon))
    pole_out = jnp.where(band == 0, bottom, top)
    pole_in = lax.ppermute(pole_out, ("lat", "lon"), pole_pairs)
    sign = jnp.where(jnp.arange(nf) == 2, -1.0, 1.0).astype(jnp.float32)[:, None, None, None]
    mirrored = jnp.flip(pole_in, 2) * sign
    south = jnp.where(band == 0, mirrored, from_south)
    north = jnp.where(band == nlat - 1, mirrored, from_north)

    slab = nf * tall * w * 4
    edges = _vmem_call(
        _edge_kernel, jax.ShapeDtypeStruct((nslab, nf, tall, w), jnp.float32), 3, [], 0, 2 * slab * nslab
    )(south, inner_edges, north)
    from_west = lax.ppermute(edges, "lon", _shift_pairs(nlon, 1, True))
    from_east = lax.ppermute(edges, "lon", _shift_pairs(nlon, -1, True))

    step_flops = 60 * nf * nlev * tall * w
    first = lambda i: jnp.minimum(i, nlev - 1)
    second = lambda i: jnp.maximum(i - nlev, 0)
    raw = pl.pallas_call(
        _main_kernel,
        out_shape=(
            jax.ShapeDtypeStruct(thickness.shape, jnp.float32),
            jax.ShapeDtypeStruct(winds.shape, jnp.float32),
            jax.ShapeDtypeStruct(tracer_mass.shape, jnp.float32),
        ),
        grid=(2 * nlev,),
        in_specs=[
            pl.BlockSpec((nf, 1, HALO, w), lambda i: (0, first(i), 0, 0)),
            pl.BlockSpec((1, rows, w), lambda i: (first(i), 0, 0)),
            pl.BlockSpec((2, 1, rows, w), lambda i: (0, first(i), 0, 0)),
            pl.BlockSpec((nf - 3, 1, rows, w), lambda i: (0, first(i), 0, 0)),
            pl.BlockSpec((nf, 1, HALO, w), lambda i: (0, first(i), 0, 0)),
            pl.BlockSpec((nlev, rows, w), lambda i: (0, 0, 0)),
            pl.BlockSpec((1, nlev, HALO, w), lambda i: (0, 0, 0, 0)),
            pl.BlockSpec((1, nlev, HALO, w), lambda i: (0, 0, 0, 0)),
            pl.BlockSpec((3, tall, w), lambda i: (0, 0, 0)),
        ],
        out_specs=(
            pl.BlockSpec((1, rows, w), lambda i: (second(i), 0, 0)),
            pl.BlockSpec((2, 1, rows, w), lambda i: (0, second(i), 0, 0)),
            pl.BlockSpec((nf - 3, 1, rows, w), lambda i: (0, second(i), 0, 0)),
        ),
        scratch_shapes=[
            pltpu.VMEM((nlev, deep, w), jnp.float32),
            pltpu.VMEM((nf, deep, w), jnp.float32),
            pltpu.VMEM((nf, deep, w), jnp.float32),
            pltpu.VMEM((nf, nlev, deep, w), jnp.float32),
        ],
        compiler_params=pltpu.CompilerParams(dimension_semantics=("arbitrary",)),
        cost_estimate=pl.CostEstimate(flops=2 * step_flops, bytes_accessed=2 * slab * nlev, transcendentals=0),
    )(south, thickness, winds, tracer_mass, north, thickness, south, north, rowvec)

    vmem = pl.BlockSpec(memory_space=pltpu.VMEM)
    anywhere = pl.BlockSpec(memory_space=pl.ANY)
    return pl.pallas_call(
        _final_kernel,
        out_shape=(
            jax.ShapeDtypeStruct(thickness.shape, jnp.float32),
            jax.ShapeDtypeStruct(winds.shape, jnp.float32),
            jax.ShapeDtypeStruct(tracer_mass.shape, jnp.float32),
        ),
        in_specs=[vmem] * 4 + [anywhere] * 3,
        out_specs=(anywhere, anywhere, anywhere),
        input_output_aliases={4: 0, 5: 1, 6: 2},
        scratch_shapes=[
            pltpu.VMEM((nslab, nf, deep, w), jnp.float32),
            pltpu.VMEM((nslab, nf, deep, w), jnp.float32),
            pltpu.VMEM((nslab, deep, w), jnp.float32),
            pltpu.VMEM((nf, deep, w), jnp.float32),
            pltpu.VMEM(thickness.shape, jnp.float32),
            pltpu.VMEM(winds.shape, jnp.float32),
            pltpu.VMEM(tracer_mass.shape, jnp.float32),
            pltpu.SemaphoreType.DMA((6,)),
        ],
        cost_estimate=pl.CostEstimate(flops=4 * step_flops // nlev, bytes_accessed=4 * slab * nslab, transcendentals=0),
    )(edges, from_west, from_east, rowvec, *raw)


def solution(mesh):
    return jax.shard_map(
        shards,
        mesh=mesh,
        in_specs=(P(None, "lat", "lon"), P(None, None, "lat", "lon"), P(None, None, "lat", "lon")),
        out_specs=(P(None, "lat", "lon"), P(None, None, "lat", "lon"), P(None, None, "lat", "lon")),
        check_vma=False,
    )
```

```python
import math

import jax
import jax.numpy as jnp
from jax import lax
from jax.experimental import pallas as pl
from jax.experimental.pallas import tpu as pltpu
from jax.sharding import PartitionSpec as P

SUBSTEPS = 2
COUR = 0.25
GRAV = 1.0
FCOR = 1.0

HALO = 2 * SUBSTEPS
GW = 6 * HALO
MARGIN = 8


def _lroll(x, k):
    n = x.shape[-1]
    return pltpu.roll(x, k % n, x.ndim - 1)


def _face(pos, behind, centre, forward, beyond):
    p = jnp.where(pos, centre, forward)
    q = jnp.where(pos, forward, centre)
    r = jnp.where(pos, behind, beyond)
    return 5.0 * p + 2.0 * q - r


def _substep(load, store, nf, pot, rv, mf_ref):
    fcos, inv_acos, cor = rv
    u = load(1, 0)
    v = load(2, 0)
    n = u.shape[0]
    fs = (COUR * 0.5 / 6.0) * (u + _lroll(u, -1))
    ms = (COUR * 0.5 / 6.0) * (v + load(2, 1)) * fcos
    fpos = fs >= 0.0
    mpos = ms >= 0.0
    for f in range(nf):
        x = u if f == 1 else (v if f == 2 else load(f, 0))
        zf = fs * _face(fpos, _lroll(x, 1), x, _lroll(x, -1), _lroll(x, -2))
        mf = ms * _face(mpos, load(f, -1), x, load(f, 1), load(f, 2))
        mf_ref[f, pl.ds(MARGIN, n)] = mf
        new = x - (zf - _lroll(zf, 1)) - (mf - mf_ref[f, pl.ds(MARGIN - 1, n)]) * inv_acos
        if f == 1:
            p0 = pot(0)
            new = new - COUR * 0.5 * (_lroll(p0, -1) - _lroll(p0, 1)) + cor * v
        elif f == 2:
            new = new - COUR * 0.5 * (pot(1) - pot(-1)) - cor * u
        store(f, new)


def _slab_of(lev, per):
    return lev // per, lev % per


def _lanes(rows, w):
    lane = lax.broadcasted_iota(jnp.int32, (rows, w), 1)
    return lane, lane // GW, lane % GW


def _pack_own(get, nlev, rows, w, slab, init):
    per = w // GW
    lane, group, kk = _lanes(rows, w)
    lo_mask = (kk >= HALO) & (kk < 3 * HALO)
    hi_mask = (kk >= 3 * HALO) & (kk < 5 * HALO)
    g = init
    for lev in range(slab * per, min(nlev, (slab + 1) * per)):
        m = get(lev)
        base = GW * (lev - slab * per)
        g = jnp.where((group == lev - slab * per) & lo_mask, _lroll(m, base + HALO), g)
        g = jnp.where((group == lev - slab * per) & hi_mask, _lroll(m, base + 3 * HALO - (w - 2 * HALO)), g)
    return g


def _packed_potential(h, nlev, w, pg_ref, n):
    per = w // GW
    nslab = len(h)
    _, group, _ = _lanes(n, w)
    below = None
    for s in reversed(range(nslab)):
        ng = min(per, nlev - s * per)
        acc = h[s]
        k = 1
        while k < ng:
            acc = acc + jnp.where(group + k < ng, _lroll(acc, -GW * k), 0.0)
            k *= 2
        if below is not None:
            spread = below
            for g in range(1, ng):
                spread = jnp.where(group == g, _lroll(below, GW * g), spread)
            acc = acc + spread
        pg_ref[s, pl.ds(MARGIN, n)] = GRAV * acc
        below = jnp.where(group == 0, acc, 0.0)


def _edge_inner_kernel(thk_ref, wind_ref, trc_ref, e_ref):
    nlev, rows, w = thk_ref.shape
    nslab, nf = e_ref.shape[0], e_ref.shape[1]
    zeros = jnp.zeros((rows, w), jnp.float32)
    for s in range(nslab):
        for f in range(nf):
            if f == 0:
                get = lambda lev: thk_ref[lev]
            elif f < 3:
                get = lambda lev, f=f: wind_ref[f - 1, lev]
            else:
                get = lambda lev, f=f: trc_ref[f - 3, lev]
            e_ref[s, f] = _pack_own(get, nlev, rows, w, s, zeros)


def _edge_kernel(
    pole_at_ref, fs_ref, fn_ref, pole_ref, inner_ref, rvi_ref, e_ref, south_ref, north_ref, rv_ref
):
    nf, nlev, halo, w = fs_ref.shape
    nslab, rows = inner_ref.shape[0], inner_ref.shape[2]
    tall = rv_ref.shape[1]
    for k in range(rv_ref.shape[0]):
        rv_ref[k] = jnp.broadcast_to(rvi_ref[k], (tall, w))
    at_south = pole_at_ref[0] == 1
    at_north = pole_at_ref[1] == 1
    for f in range(nf):
        for lev in range(nlev):
            for k in range(halo):
                mirrored = pole_ref[f, lev, pl.ds(halo - 1 - k, 1)]
                if f == 2:
                    mirrored = -mirrored
                row = pl.ds(k, 1)
                south_ref[f, lev, row] = jnp.where(at_south, mirrored, fs_ref[f, lev, row])
                north_ref[f, lev, row] = jnp.where(at_north, mirrored, fn_ref[f, lev, row])
    zeros = jnp.zeros((halo, w), jnp.float32)
    for s in range(nslab):
        for f in range(nf):
            e_ref[s, f, pl.ds(0, halo)] = _pack_own(lambda lev: south_ref[f, lev], nlev, halo, w, s, zeros)
            e_ref[s, f, pl.ds(halo, rows)] = inner_ref[s, f]
            e_ref[s, f, pl.ds(halo + rows, halo)] = _pack_own(lambda lev: north_ref[f, lev], nlev, halo, w, s, zeros)


def _main_kernel(
    south_ref, thk_ref, wind_ref, trc_ref, north_ref, tall_ref, sall_ref, nall_ref, rv_ref,
    thk_o, wind_o, trc_o, p_ref, mf_ref, sp_ref, s1_ref,
):
    nf, _, halo, w = south_ref.shape
    nlev, rows = tall_ref.shape[0], tall_ref.shape[1]
    i = pl.program_id(0)
    tall = rows + 2 * halo
    win = pl.ds(MARGIN, tall)
    top = pl.ds(MARGIN, halo)
    mid = pl.ds(MARGIN + halo, rows)
    bot = pl.ds(MARGIN + halo + rows, halo)
    rv = (rv_ref[0], rv_ref[1], rv_ref[2])

    @pl.when(i == 0)
    def _():
        acc = None
        for l in reversed(range(nlev)):
            part = (sall_ref[0, l], tall_ref[l], nall_ref[0, l])
            acc = part if acc is None else tuple(x + y for x, y in zip(acc, part))
            p_ref[l, top] = GRAV * acc[0]
            p_ref[l, mid] = GRAV * acc[1]
            p_ref[l, bot] = GRAV * acc[2]

    @pl.when(i < nlev)
    def _():
        lev = i
        for f in range(nf):
            sp_ref[f, top] = south_ref[f, 0]
            if f == 0:
                sp_ref[f, mid] = thk_ref[0]
            elif f < 3:
                sp_ref[f, mid] = wind_ref[f - 1, 0]
            else:
                sp_ref[f, mid] = trc_ref[f - 3, 0]
            sp_ref[f, bot] = north_ref[f, 0]

        def store(f, x):
            s1_ref[f, lev, win] = x

        _substep(
            lambda f, d: sp_ref[f, pl.ds(MARGIN + d, tall)],
            store,
            nf,
            lambda d: p_ref[lev, pl.ds(MARGIN + d, tall)],
            rv,
            mf_ref,
        )

    @pl.when(i == nlev)
    def _():
        acc = None
        for l in reversed(range(nlev)):
            acc = s1_ref[0, l, win] if acc is None else acc + s1_ref[0, l, win]
            p_ref[l, win] = GRAV * acc

    @pl.when(i >= nlev)
    def _():
        lev = i - nlev

        def store(f, x):
            x = x[halo : halo + rows]
            if f == 0:
                thk_o[0] = x
            elif f < 3:
                wind_o[f - 1, 0] = x
            else:
                trc_o[f - 3, 0] = x

        _substep(
            lambda f, d: s1_ref[f, lev, pl.ds(MARGIN + d, tall)],
            store,
            nf,
            lambda d: p_ref[lev, pl.ds(MARGIN + d, tall)],
            rv,
            mf_ref,
        )


def _final_kernel(
    e_ref, ew_ref, ee_ref, rv_ref, thk_h, wind_h, trc_h, thk_oh, wind_oh, trc_oh, g0_ref, g1_ref, pg_ref, mf_ref,
    thk_i, wind_i, trc_i, sem,
):
    nslab, nf, tall, w = e_ref.shape
    nlev, rows = thk_i.shape[0], thk_i.shape[1]
    ins = [pltpu.make_async_copy(h, v, sem.at[k]) for k, (h, v) in enumerate(zip((thk_h, wind_h, trc_h), (thk_i, wind_i, trc_i)))]
    for c in ins:
        c.start()
    thk_o, wind_o, trc_o = thk_i, wind_i, trc_i
    per = w // GW
    rv = (rv_ref[0], rv_ref[1], rv_ref[2])
    lane, group, kk = _lanes(tall, w)
    win = pl.ds(MARGIN, tall)
    for s in range(nslab):
        for f in range(nf):
            g0_ref[s, f, win] = jnp.where(
                kk < HALO,
                _lroll(ew_ref[s, f], -4 * HALO),
                jnp.where(kk >= 5 * HALO, _lroll(ee_ref[s, f], 4 * HALO), e_ref[s, f]),
            )
    for src, dst in ((g0_ref, g1_ref), (g1_ref, g0_ref)):
        _packed_potential([src[s, 0, win] for s in range(nslab)], nlev, w, pg_ref, tall)
        for s in range(nslab):

            def store(f, x, s=s, dst=dst):
                dst[s, f, win] = x

            _substep(
                lambda f, d, s=s, src=src: src[s, f, pl.ds(MARGIN + d, tall)],
                store,
                nf,
                lambda d, s=s: pg_ref[s, pl.ds(MARGIN + d, tall)],
                rv,
                mf_ref,
            )
    lane_o = lane[:rows]
    inner = pl.ds(MARGIN + HALO, rows)
    for c in ins:
        c.wait()
    for lev in range(nlev):
        s, g = _slab_of(lev, per)
        for f in range(nf):
            strip = g0_ref[s, f, inner]
            lo = _lroll(strip, -(GW * g + HALO))
            hi = _lroll(strip, (w - HALO) - (GW * g + 4 * HALO))
            if f == 0:
                src, dst = thk_i.at[lev], thk_o.at[lev]
            elif f < 3:
                src, dst = wind_i.at[f - 1, lev], wind_o.at[f - 1, lev]
            else:
                src, dst = trc_i.at[f - 3, lev], trc_o.at[f - 3, lev]
            dst[...] = jnp.where(lane_o < HALO, lo, jnp.where(lane_o >= w - HALO, hi, src[...]))
    outs = [pltpu.make_async_copy(v, h, sem.at[3 + k]) for k, (v, h) in enumerate(zip((thk_i, wind_i, trc_i), (thk_oh, wind_oh, trc_oh)))]
    for c in outs:
        c.start()
    for c in outs:
        c.wait()


def _shift_pairs(n, d, closed):
    return [(i, (i + d) % n) for i in range(n) if closed or 0 <= i + d < n]


def _vmem_call(kernel, out_shape, n_in, scratch, flops, nbytes):
    vmem = pl.BlockSpec(memory_space=pltpu.VMEM)
    return pl.pallas_call(
        kernel,
        out_shape=out_shape,
        in_specs=[vmem] * n_in,
        out_specs=tuple(vmem for _ in out_shape) if isinstance(out_shape, tuple) else vmem,
        scratch_shapes=scratch,
        cost_estimate=pl.CostEstimate(flops=flops, bytes_accessed=nbytes, transcendentals=0),
    )


def shards(thickness, winds, tracer_mass):
    fields = jnp.concatenate([thickness[None], winds, tracer_mass], 0)
    nf, nlev, rows, w = fields.shape
    nlat = lax.axis_size("lat")
    nlon = lax.axis_size("lon")
    band = lax.axis_index("lat")
    spacing = math.pi / (rows * nlat)
    tall = rows + 2 * HALO
    deep = tall + 2 * MARGIN
    per = w // GW
    nslab = -(-nlev // per)

    row_index = (jnp.arange(tall) + (band * rows - HALO)).astype(jnp.float32)
    center_lat = (row_index + 0.5) * spacing - 0.5 * math.pi
    face_lat = (row_index + 1.0) * spacing - 0.5 * math.pi
    center_cos = jnp.cos(center_lat)
    rowvec = jnp.stack(
        [
            jnp.abs(jnp.cos(face_lat)),
            1.0 / jnp.abs(center_cos),
            COUR * FCOR * jnp.sin(center_lat) * jnp.where(center_cos >= 0.0, 1.0, -1.0),
        ]
    )
    rowvec = rowvec[:, :, None]

    inner_edges = _vmem_call(
        _edge_inner_kernel, jax.ShapeDtypeStruct((nslab, nf, rows, w), jnp.float32), 3, [], 0, nf * nlev * rows * w * 4
    )(thickness, winds, tracer_mass)

    top = fields[:, :, rows - HALO :]
    bottom = fields[:, :, :HALO]
    from_south = lax.ppermute(top, "lat", _shift_pairs(nlat, 1, False))
    from_north = lax.ppermute(bottom, "lat", _shift_pairs(nlat, -1, False))
    half = nlon // 2
    pole_pairs = []
    for b in (0, nlat - 1):
        for s in range(nlon):
            pole_pairs.append((b * nlon + s, b * nlon + (s + half) % nlon))
    pole_out = jnp.where(band == 0, bottom, top)
    pole_in = lax.ppermute(pole_out, ("lat", "lon"), pole_pairs)
    pole_at = jnp.stack([band == 0, band == nlat - 1]).astype(jnp.int32)

    slab = nf * tall * w * 4
    vmem = pl.BlockSpec(memory_space=pltpu.VMEM)
    edges, south, north, rowvec = pl.pallas_call(
        _edge_kernel,
        out_shape=(
            jax.ShapeDtypeStruct((nslab, nf, tall, w), jnp.float32),
            jax.ShapeDtypeStruct(top.shape, jnp.float32),
            jax.ShapeDtypeStruct(top.shape, jnp.float32),
            jax.ShapeDtypeStruct((3, tall, w), jnp.float32),
        ),
        in_specs=[pl.BlockSpec(memory_space=pltpu.SMEM)] + [vmem] * 5,
        out_specs=(vmem, vmem, vmem, vmem),
        cost_estimate=pl.CostEstimate(flops=0, bytes_accessed=2 * slab * nslab, transcendentals=0),
    )(pole_at, from_south, from_north, pole_in, inner_edges, rowvec)
    from_west = lax.ppermute(edges, "lon", _shift_pairs(nlon, 1, True))
    from_east = lax.ppermute(edges, "lon", _shift_pairs(nlon, -1, True))

    step_flops = 60 * nf * nlev * tall * w
    first = lambda i: jnp.minimum(i, nlev - 1)
    second = lambda i: jnp.maximum(i - nlev, 0)
    raw = pl.pallas_call(
        _main_kernel,
        out_shape=(
            jax.ShapeDtypeStruct(thickness.shape, jnp.float32),
            jax.ShapeDtypeStruct(winds.shape, jnp.float32),
            jax.ShapeDtypeStruct(tracer_mass.shape, jnp.float32),
        ),
        grid=(2 * nlev,),
        in_specs=[
            pl.BlockSpec((nf, 1, HALO, w), lambda i: (0, first(i), 0, 0)),
            pl.BlockSpec((1, rows, w), lambda i: (first(i), 0, 0)),
            pl.BlockSpec((2, 1, rows, w), lambda i: (0, first(i), 0, 0)),
            pl.BlockSpec((nf - 3, 1, rows, w), lambda i: (0, first(i), 0, 0)),
            pl.BlockSpec((nf, 1, HALO, w), lambda i: (0, first(i), 0, 0)),
            pl.BlockSpec((nlev, rows, w), lambda i: (0, 0, 0)),
            pl.BlockSpec((1, nlev, HALO, w), lambda i: (0, 0, 0, 0)),
            pl.BlockSpec((1, nlev, HALO, w), lambda i: (0, 0, 0, 0)),
            pl.BlockSpec((3, tall, w), lambda i: (0, 0, 0)),
        ],
        out_specs=(
            pl.BlockSpec((1, rows, w), lambda i: (second(i), 0, 0)),
            pl.BlockSpec((2, 1, rows, w), lambda i: (0, second(i), 0, 0)),
            pl.BlockSpec((nf - 3, 1, rows, w), lambda i: (0, second(i), 0, 0)),
        ),
        scratch_shapes=[
            pltpu.VMEM((nlev, deep, w), jnp.float32),
            pltpu.VMEM((nf, deep, w), jnp.float32),
            pltpu.VMEM((nf, deep, w), jnp.float32),
            pltpu.VMEM((nf, nlev, deep, w), jnp.float32),
        ],
        compiler_params=pltpu.CompilerParams(dimension_semantics=("arbitrary",)),
        cost_estimate=pl.CostEstimate(flops=2 * step_flops, bytes_accessed=2 * slab * nlev, transcendentals=0),
    )(south, thickness, winds, tracer_mass, north, thickness, south, north, rowvec)

    vmem = pl.BlockSpec(memory_space=pltpu.VMEM)
    anywhere = pl.BlockSpec(memory_space=pl.ANY)
    return pl.pallas_call(
        _final_kernel,
        out_shape=(
            jax.ShapeDtypeStruct(thickness.shape, jnp.float32),
            jax.ShapeDtypeStruct(winds.shape, jnp.float32),
            jax.ShapeDtypeStruct(tracer_mass.shape, jnp.float32),
        ),
        in_specs=[vmem] * 4 + [anywhere] * 3,
        out_specs=(anywhere, anywhere, anywhere),
        input_output_aliases={4: 0, 5: 1, 6: 2},
        scratch_shapes=[
            pltpu.VMEM((nslab, nf, deep, w), jnp.float32),
            pltpu.VMEM((nslab, nf, deep, w), jnp.float32),
            pltpu.VMEM((nslab, deep, w), jnp.float32),
            pltpu.VMEM((nf, deep, w), jnp.float32),
            pltpu.VMEM(thickness.shape, jnp.float32),
            pltpu.VMEM(winds.shape, jnp.float32),
            pltpu.VMEM(tracer_mass.shape, jnp.float32),
            pltpu.SemaphoreType.DMA((6,)),
        ],
        cost_estimate=pl.CostEstimate(flops=4 * step_flops // nlev, bytes_accessed=4 * slab * nslab, transcendentals=0),
    )(edges, from_west, from_east, rowvec, *raw)


def solution(mesh):
    return jax.shard_map(
        shards,
        mesh=mesh,
        in_specs=(P(None, "lat", "lon"), P(None, None, "lat", "lon"), P(None, None, "lat", "lon")),
        out_specs=(P(None, "lat", "lon"), P(None, None, "lat", "lon"), P(None, None, "lat", "lon")),
        check_vma=False,
    )
```

```python
import math

import jax
import jax.numpy as jnp
from jax import lax
from jax.experimental import pallas as pl
from jax.experimental.pallas import tpu as pltpu
from jax.sharding import PartitionSpec as P

SUBSTEPS = 2
COUR = 0.25
GRAV = 1.0
FCOR = 1.0

HALO = 2 * SUBSTEPS
GW = 6 * HALO
MARGIN = 8


def _lroll(x, k):
    n = x.shape[-1]
    return pltpu.roll(x, k % n, x.ndim - 1)


def _face(pos, behind, centre, forward, beyond):
    p = jnp.where(pos, centre, forward)
    q = jnp.where(pos, forward, centre)
    r = jnp.where(pos, behind, beyond)
    return 5.0 * p + 2.0 * q - r


def _substep(load, store, nf, pot, rv, mf_ref):
    fcos, inv_acos, cor = rv
    u = load(1, 0)
    v = load(2, 0)
    n = u.shape[0]
    fs = (COUR * 0.5 / 6.0) * (u + _lroll(u, -1))
    ms = (COUR * 0.5 / 6.0) * (v + load(2, 1)) * fcos
    fpos = fs >= 0.0
    mpos = ms >= 0.0
    for f in range(nf):
        x = u if f == 1 else (v if f == 2 else load(f, 0))
        zf = fs * _face(fpos, _lroll(x, 1), x, _lroll(x, -1), _lroll(x, -2))
        mf = ms * _face(mpos, load(f, -1), x, load(f, 1), load(f, 2))
        mf_ref[f, pl.ds(MARGIN, n)] = mf
        new = x - (zf - _lroll(zf, 1)) - (mf - mf_ref[f, pl.ds(MARGIN - 1, n)]) * inv_acos
        if f == 1:
            p0 = pot(0)
            new = new - COUR * 0.5 * (_lroll(p0, -1) - _lroll(p0, 1)) + cor * v
        elif f == 2:
            new = new - COUR * 0.5 * (pot(1) - pot(-1)) - cor * u
        store(f, new)


def _slab_of(lev, per):
    return lev // per, lev % per


def _lanes(rows, w):
    lane = lax.broadcasted_iota(jnp.int32, (rows, w), 1)
    return lane, lane // GW, lane % GW


def _pack_own(get, nlev, rows, w, slab, init):
    per = w // GW
    lane, group, kk = _lanes(rows, w)
    lo_mask = (kk >= HALO) & (kk < 3 * HALO)
    hi_mask = (kk >= 3 * HALO) & (kk < 5 * HALO)
    g = init
    for lev in range(slab * per, min(nlev, (slab + 1) * per)):
        m = get(lev)
        base = GW * (lev - slab * per)
        g = jnp.where((group == lev - slab * per) & lo_mask, _lroll(m, base + HALO), g)
        g = jnp.where((group == lev - slab * per) & hi_mask, _lroll(m, base + 3 * HALO - (w - 2 * HALO)), g)
    return g


def _packed_potential(h, nlev, w, pg_ref, n):
    per = w // GW
    nslab = len(h)
    _, group, _ = _lanes(n, w)
    below = None
    for s in reversed(range(nslab)):
        ng = min(per, nlev - s * per)
        acc = h[s]
        k = 1
        while k < ng:
            acc = acc + jnp.where(group + k < ng, _lroll(acc, -GW * k), 0.0)
            k *= 2
        if below is not None:
            spread = below
            for g in range(1, ng):
                spread = jnp.where(group == g, _lroll(below, GW * g), spread)
            acc = acc + spread
        pg_ref[s, pl.ds(MARGIN, n)] = GRAV * acc
        below = jnp.where(group == 0, acc, 0.0)


def _edge_inner_kernel(thk_ref, wind_ref, trc_ref, e_ref):
    nlev, rows, w = thk_ref.shape
    nslab, nf = e_ref.shape[0], e_ref.shape[1]
    zeros = jnp.zeros((rows, w), jnp.float32)
    for s in range(nslab):
        for f in range(nf):
            if f == 0:
                get = lambda lev: thk_ref[lev]
            elif f < 3:
                get = lambda lev, f=f: wind_ref[f - 1, lev]
            else:
                get = lambda lev, f=f: trc_ref[f - 3, lev]
            e_ref[s, f] = _pack_own(get, nlev, rows, w, s, zeros)


def _edge_kernel(
    pole_at_ref, fs_ref, fn_ref, pole_ref, inner_ref, rvi_ref, e_ref, south_ref, north_ref, rv_ref
):
    nf, nlev, halo, w = fs_ref.shape
    nslab, rows = inner_ref.shape[0], inner_ref.shape[2]
    tall = rv_ref.shape[1]
    for k in range(rv_ref.shape[0]):
        rv_ref[k] = jnp.broadcast_to(rvi_ref[k], (tall, w))
    at_south = pole_at_ref[0] == 1
    at_north = pole_at_ref[1] == 1
    for f in range(nf):
        for lev in range(nlev):
            for k in range(halo):
                mirrored = pole_ref[f, lev, pl.ds(halo - 1 - k, 1)]
                if f == 2:
                    mirrored = -mirrored
                row = pl.ds(k, 1)
                south_ref[f, lev, row] = jnp.where(at_south, mirrored, fs_ref[f, lev, row])
                north_ref[f, lev, row] = jnp.where(at_north, mirrored, fn_ref[f, lev, row])
    zeros = jnp.zeros((halo, w), jnp.float32)
    for s in range(nslab):
        for f in range(nf):
            e_ref[s, f, pl.ds(0, halo)] = _pack_own(lambda lev: south_ref[f, lev], nlev, halo, w, s, zeros)
            e_ref[s, f, pl.ds(halo, rows)] = inner_ref[s, f]
            e_ref[s, f, pl.ds(halo + rows, halo)] = _pack_own(lambda lev: north_ref[f, lev], nlev, halo, w, s, zeros)


def _main_kernel(
    south_ref, thk_ref, wind_ref, trc_ref, north_ref, tall_ref, sall_ref, nall_ref, rv_ref,
    thk_o, wind_o, trc_o, p_ref, mf_ref, sp_ref, s1_ref,
):
    nf, per, halo, w = south_ref.shape
    nlev, rows = tall_ref.shape[0], tall_ref.shape[1]
    nb = nlev // per
    i = pl.program_id(0)
    tall = rows + 2 * halo
    win = pl.ds(MARGIN, tall)
    top = pl.ds(MARGIN, halo)
    mid = pl.ds(MARGIN + halo, rows)
    bot = pl.ds(MARGIN + halo + rows, halo)
    rv = (rv_ref[0], rv_ref[1], rv_ref[2])

    @pl.when(i == 0)
    def _():
        acc = None
        for l in reversed(range(nlev)):
            part = (sall_ref[0, l], tall_ref[l], nall_ref[0, l])
            acc = part if acc is None else tuple(x + y for x, y in zip(acc, part))
            p_ref[l, top] = GRAV * acc[0]
            p_ref[l, mid] = GRAV * acc[1]
            p_ref[l, bot] = GRAV * acc[2]

    @pl.when(i < nb)
    def _():
        for j in range(per):
            lev = i * per + j
            sp = sp_ref.at[j]
            for f in range(nf):
                sp[f, top] = south_ref[f, j]
                if f == 0:
                    sp[f, mid] = thk_ref[j]
                elif f < 3:
                    sp[f, mid] = wind_ref[f - 1, j]
                else:
                    sp[f, mid] = trc_ref[f - 3, j]
                sp[f, bot] = north_ref[f, j]

            def store(f, x, lev=lev):
                s1_ref[f, lev, win] = x

            _substep(
                lambda f, d, sp=sp: sp[f, pl.ds(MARGIN + d, tall)],
                store,
                nf,
                lambda d, lev=lev: p_ref[lev, pl.ds(MARGIN + d, tall)],
                rv,
                mf_ref.at[j],
            )

    @pl.when(i == nb)
    def _():
        acc = None
        for l in reversed(range(nlev)):
            acc = s1_ref[0, l, win] if acc is None else acc + s1_ref[0, l, win]
            p_ref[l, win] = GRAV * acc

    @pl.when(i >= nb)
    def _():
        for j in range(per):
            lev = (i - nb) * per + j

            def store(f, x, j=j):
                x = x[halo : halo + rows]
                if f == 0:
                    thk_o[j] = x
                elif f < 3:
                    wind_o[f - 1, j] = x
                else:
                    trc_o[f - 3, j] = x

            _substep(
                lambda f, d, lev=lev: s1_ref[f, lev, pl.ds(MARGIN + d, tall)],
                store,
                nf,
                lambda d, lev=lev: p_ref[lev, pl.ds(MARGIN + d, tall)],
                rv,
                mf_ref.at[j],
            )


def _final_kernel(
    e_ref, ew_ref, ee_ref, rv_ref, thk_h, wind_h, trc_h, thk_oh, wind_oh, trc_oh, g0_ref, g1_ref, pg_ref, mf_ref,
    thk_i, wind_i, trc_i, sem,
):
    nslab, nf, tall, w = e_ref.shape
    nlev, rows = thk_i.shape[0], thk_i.shape[1]
    ins = [pltpu.make_async_copy(h, v, sem.at[k]) for k, (h, v) in enumerate(zip((thk_h, wind_h, trc_h), (thk_i, wind_i, trc_i)))]
    for c in ins:
        c.start()
    thk_o, wind_o, trc_o = thk_i, wind_i, trc_i
    per = w // GW
    rv = (rv_ref[0], rv_ref[1], rv_ref[2])
    lane, group, kk = _lanes(tall, w)
    win = pl.ds(MARGIN, tall)
    for s in range(nslab):
        for f in range(nf):
            g0_ref[s, f, win] = jnp.where(
                kk < HALO,
                _lroll(ew_ref[s, f], -4 * HALO),
                jnp.where(kk >= 5 * HALO, _lroll(ee_ref[s, f], 4 * HALO), e_ref[s, f]),
            )
    for src, dst in ((g0_ref, g1_ref), (g1_ref, g0_ref)):
        _packed_potential([src[s, 0, win] for s in range(nslab)], nlev, w, pg_ref, tall)
        for s in range(nslab):

            def store(f, x, s=s, dst=dst):
                dst[s, f, win] = x

            _substep(
                lambda f, d, s=s, src=src: src[s, f, pl.ds(MARGIN + d, tall)],
                store,
                nf,
                lambda d, s=s: pg_ref[s, pl.ds(MARGIN + d, tall)],
                rv,
                mf_ref,
            )
    lane_o = lane[:rows]
    inner = pl.ds(MARGIN + HALO, rows)
    for c in ins:
        c.wait()
    for lev in range(nlev):
        s, g = _slab_of(lev, per)
        for f in range(nf):
            strip = g0_ref[s, f, inner]
            lo = _lroll(strip, -(GW * g + HALO))
            hi = _lroll(strip, (w - HALO) - (GW * g + 4 * HALO))
            if f == 0:
                src, dst = thk_i.at[lev], thk_o.at[lev]
            elif f < 3:
                src, dst = wind_i.at[f - 1, lev], wind_o.at[f - 1, lev]
            else:
                src, dst = trc_i.at[f - 3, lev], trc_o.at[f - 3, lev]
            dst[...] = jnp.where(lane_o < HALO, lo, jnp.where(lane_o >= w - HALO, hi, src[...]))
    outs = [pltpu.make_async_copy(v, h, sem.at[3 + k]) for k, (v, h) in enumerate(zip((thk_i, wind_i, trc_i), (thk_oh, wind_oh, trc_oh)))]
    for c in outs:
        c.start()
    for c in outs:
        c.wait()


def _shift_pairs(n, d, closed):
    return [(i, (i + d) % n) for i in range(n) if closed or 0 <= i + d < n]


def _vmem_call(kernel, out_shape, n_in, scratch, flops, nbytes):
    vmem = pl.BlockSpec(memory_space=pltpu.VMEM)
    return pl.pallas_call(
        kernel,
        out_shape=out_shape,
        in_specs=[vmem] * n_in,
        out_specs=tuple(vmem for _ in out_shape) if isinstance(out_shape, tuple) else vmem,
        scratch_shapes=scratch,
        cost_estimate=pl.CostEstimate(flops=flops, bytes_accessed=nbytes, transcendentals=0),
    )


def shards(thickness, winds, tracer_mass):
    fields = jnp.concatenate([thickness[None], winds, tracer_mass], 0)
    nf, nlev, rows, w = fields.shape
    nlat = lax.axis_size("lat")
    nlon = lax.axis_size("lon")
    band = lax.axis_index("lat")
    spacing = math.pi / (rows * nlat)
    tall = rows + 2 * HALO
    deep = tall + 2 * MARGIN
    per = w // GW
    nslab = -(-nlev // per)

    row_index = (jnp.arange(tall) + (band * rows - HALO)).astype(jnp.float32)
    center_lat = (row_index + 0.5) * spacing - 0.5 * math.pi
    face_lat = (row_index + 1.0) * spacing - 0.5 * math.pi
    center_cos = jnp.cos(center_lat)
    rowvec = jnp.stack(
        [
            jnp.abs(jnp.cos(face_lat)),
            1.0 / jnp.abs(center_cos),
            COUR * FCOR * jnp.sin(center_lat) * jnp.where(center_cos >= 0.0, 1.0, -1.0),
        ]
    )
    rowvec = rowvec[:, :, None]

    inner_edges = _vmem_call(
        _edge_inner_kernel, jax.ShapeDtypeStruct((nslab, nf, rows, w), jnp.float32), 3, [], 0, nf * nlev * rows * w * 4
    )(thickness, winds, tracer_mass)

    top = fields[:, :, rows - HALO :]
    bottom = fields[:, :, :HALO]
    from_south = lax.ppermute(top, "lat", _shift_pairs(nlat, 1, False))
    from_north = lax.ppermute(bottom, "lat", _shift_pairs(nlat, -1, False))
    half = nlon // 2
    pole_pairs = []
    for b in (0, nlat - 1):
        for s in range(nlon):
            pole_pairs.append((b * nlon + s, b * nlon + (s + half) % nlon))
    pole_out = jnp.where(band == 0, bottom, top)
    pole_in = lax.ppermute(pole_out, ("lat", "lon"), pole_pairs)
    pole_at = jnp.stack([band == 0, band == nlat - 1]).astype(jnp.int32)

    slab = nf * tall * w * 4
    vmem = pl.BlockSpec(memory_space=pltpu.VMEM)
    edges, south, north, rowvec = pl.pallas_call(
        _edge_kernel,
        out_shape=(
            jax.ShapeDtypeStruct((nslab, nf, tall, w), jnp.float32),
            jax.ShapeDtypeStruct(top.shape, jnp.float32),
            jax.ShapeDtypeStruct(top.shape, jnp.float32),
            jax.ShapeDtypeStruct((3, tall, w), jnp.float32),
        ),
        in_specs=[pl.BlockSpec(memory_space=pltpu.SMEM)] + [vmem] * 5,
        out_specs=(vmem, vmem, vmem, vmem),
        cost_estimate=pl.CostEstimate(flops=0, bytes_accessed=2 * slab * nslab, transcendentals=0),
    )(pole_at, from_south, from_north, pole_in, inner_edges, rowvec)
    from_west = lax.ppermute(edges, "lon", _shift_pairs(nlon, 1, True))
    from_east = lax.ppermute(edges, "lon", _shift_pairs(nlon, -1, True))

    step_flops = 60 * nf * nlev * tall * w
    per = 2 if nlev % 2 == 0 else 1
    nb = nlev // per
    first = lambda i: jnp.minimum(i, nb - 1)
    second = lambda i: jnp.maximum(i - nb, 0)
    raw = pl.pallas_call(
        _main_kernel,
        out_shape=(
            jax.ShapeDtypeStruct(thickness.shape, jnp.float32),
            jax.ShapeDtypeStruct(winds.shape, jnp.float32),
            jax.ShapeDtypeStruct(tracer_mass.shape, jnp.float32),
        ),
        grid=(2 * nb,),
        in_specs=[
            pl.BlockSpec((nf, per, HALO, w), lambda i: (0, first(i), 0, 0)),
            pl.BlockSpec((per, rows, w), lambda i: (first(i), 0, 0)),
            pl.BlockSpec((2, per, rows, w), lambda i: (0, first(i), 0, 0)),
            pl.BlockSpec((nf - 3, per, rows, w), lambda i: (0, first(i), 0, 0)),
            pl.BlockSpec((nf, per, HALO, w), lambda i: (0, first(i), 0, 0)),
            pl.BlockSpec((nlev, rows, w), lambda i: (0, 0, 0)),
            pl.BlockSpec((1, nlev, HALO, w), lambda i: (0, 0, 0, 0)),
            pl.BlockSpec((1, nlev, HALO, w), lambda i: (0, 0, 0, 0)),
            pl.BlockSpec((3, tall, w), lambda i: (0, 0, 0)),
        ],
        out_specs=(
            pl.BlockSpec((per, rows, w), lambda i: (second(i), 0, 0)),
            pl.BlockSpec((2, per, rows, w), lambda i: (0, second(i), 0, 0)),
            pl.BlockSpec((nf - 3, per, rows, w), lambda i: (0, second(i), 0, 0)),
        ),
        scratch_shapes=[
            pltpu.VMEM((nlev, deep, w), jnp.float32),
            pltpu.VMEM((per, nf, deep, w), jnp.float32),
            pltpu.VMEM((per, nf, deep, w), jnp.float32),
            pltpu.VMEM((nf, nlev, deep, w), jnp.float32),
        ],
        compiler_params=pltpu.CompilerParams(dimension_semantics=("arbitrary",)),
        cost_estimate=pl.CostEstimate(flops=2 * step_flops, bytes_accessed=2 * slab * nlev, transcendentals=0),
    )(south, thickness, winds, tracer_mass, north, thickness, south, north, rowvec)

    vmem = pl.BlockSpec(memory_space=pltpu.VMEM)
    anywhere = pl.BlockSpec(memory_space=pl.ANY)
    return pl.pallas_call(
        _final_kernel,
        out_shape=(
            jax.ShapeDtypeStruct(thickness.shape, jnp.float32),
            jax.ShapeDtypeStruct(winds.shape, jnp.float32),
            jax.ShapeDtypeStruct(tracer_mass.shape, jnp.float32),
        ),
        in_specs=[vmem] * 4 + [anywhere] * 3,
        out_specs=(anywhere, anywhere, anywhere),
        input_output_aliases={4: 0, 5: 1, 6: 2},
        scratch_shapes=[
            pltpu.VMEM((nslab, nf, deep, w), jnp.float32),
            pltpu.VMEM((nslab, nf, deep, w), jnp.float32),
            pltpu.VMEM((nslab, deep, w), jnp.float32),
            pltpu.VMEM((nf, deep, w), jnp.float32),
            pltpu.VMEM(thickness.shape, jnp.float32),
            pltpu.VMEM(winds.shape, jnp.float32),
            pltpu.VMEM(tracer_mass.shape, jnp.float32),
            pltpu.SemaphoreType.DMA((6,)),
        ],
        cost_estimate=pl.CostEstimate(flops=4 * step_flops // nlev, bytes_accessed=4 * slab * nslab, transcendentals=0),
    )(edges, from_west, from_east, rowvec, *raw)


def solution(mesh):
    return jax.shard_map(
        shards,
        mesh=mesh,
        in_specs=(P(None, "lat", "lon"), P(None, None, "lat", "lon"), P(None, None, "lat", "lon")),
        out_specs=(P(None, "lat", "lon"), P(None, None, "lat", "lon"), P(None, None, "lat", "lon")),
        check_vma=False,
    )
```

```python
import math

import jax
import jax.numpy as jnp
from jax import lax
from jax.experimental import pallas as pl
from jax.experimental.pallas import tpu as pltpu
from jax.sharding import PartitionSpec as P

SUBSTEPS = 2
COUR = 0.25
GRAV = 1.0
FCOR = 1.0

HALO = 2 * SUBSTEPS
GW = 6 * HALO
MARGIN = 8


def _lroll(x, k):
    n = x.shape[-1]
    return pltpu.roll(x, k % n, x.ndim - 1)


def _face(pos, behind, centre, forward, beyond):
    p = jnp.where(pos, centre, forward)
    q = jnp.where(pos, forward, centre)
    r = jnp.where(pos, behind, beyond)
    return 5.0 * p + 2.0 * q - r


def _substep(load, store, nf, pot, rv, mf_ref):
    fcos, inv_acos, cor = rv
    u = load(1, 0)
    v = load(2, 0)
    n = u.shape[0]
    fs = (COUR * 0.5 / 6.0) * (u + _lroll(u, -1))
    ms = (COUR * 0.5 / 6.0) * (v + load(2, 1)) * fcos
    fpos = fs >= 0.0
    mpos = ms >= 0.0
    for f in range(nf):
        x = u if f == 1 else (v if f == 2 else load(f, 0))
        zf = fs * _face(fpos, _lroll(x, 1), x, _lroll(x, -1), _lroll(x, -2))
        mf = ms * _face(mpos, load(f, -1), x, load(f, 1), load(f, 2))
        mf_ref[f, pl.ds(MARGIN, n)] = mf
        new = x - (zf - _lroll(zf, 1)) - (mf - mf_ref[f, pl.ds(MARGIN - 1, n)]) * inv_acos
        if f == 1:
            p0 = pot(0)
            new = new - COUR * 0.5 * (_lroll(p0, -1) - _lroll(p0, 1)) + cor * v
        elif f == 2:
            new = new - COUR * 0.5 * (pot(1) - pot(-1)) - cor * u
        store(f, new)


def _slab_of(lev, per):
    return lev // per, lev % per


def _lanes(rows, w):
    lane = lax.broadcasted_iota(jnp.int32, (rows, w), 1)
    return lane, lane // GW, lane % GW


def _pack_own(get, nlev, rows, w, slab, init):
    per = w // GW
    lane, group, kk = _lanes(rows, w)
    lo_mask = (kk >= HALO) & (kk < 3 * HALO)
    hi_mask = (kk >= 3 * HALO) & (kk < 5 * HALO)
    g = init
    for lev in range(slab * per, min(nlev, (slab + 1) * per)):
        m = get(lev)
        base = GW * (lev - slab * per)
        g = jnp.where((group == lev - slab * per) & lo_mask, _lroll(m, base + HALO), g)
        g = jnp.where((group == lev - slab * per) & hi_mask, _lroll(m, base + 3 * HALO - (w - 2 * HALO)), g)
    return g


def _packed_potential(h, nlev, w, pg_ref, n):
    per = w // GW
    nslab = len(h)
    _, group, _ = _lanes(n, w)
    below = None
    for s in reversed(range(nslab)):
        ng = min(per, nlev - s * per)
        acc = h[s]
        k = 1
        while k < ng:
            acc = acc + jnp.where(group + k < ng, _lroll(acc, -GW * k), 0.0)
            k *= 2
        if below is not None:
            spread = below
            for g in range(1, ng):
                spread = jnp.where(group == g, _lroll(below, GW * g), spread)
            acc = acc + spread
        pg_ref[s, pl.ds(MARGIN, n)] = GRAV * acc
        below = jnp.where(group == 0, acc, 0.0)


def _edge_inner_kernel(thk_ref, wind_ref, trc_ref, e_ref):
    nlev, rows, w = thk_ref.shape
    nslab, nf = e_ref.shape[0], e_ref.shape[1]
    zeros = jnp.zeros((rows, w), jnp.float32)
    for s in range(nslab):
        for f in range(nf):
            if f == 0:
                get = lambda lev: thk_ref[lev]
            elif f < 3:
                get = lambda lev, f=f: wind_ref[f - 1, lev]
            else:
                get = lambda lev, f=f: trc_ref[f - 3, lev]
            e_ref[s, f] = _pack_own(get, nlev, rows, w, s, zeros)


def _edge_kernel(
    pole_at_ref, fs_ref, fn_ref, pole_ref, inner_ref, rvi_ref, e_ref, south_ref, north_ref, rv_ref
):
    nf, nlev, halo, w = fs_ref.shape
    nslab, rows = inner_ref.shape[0], inner_ref.shape[2]
    tall = rv_ref.shape[1]
    for k in range(rv_ref.shape[0]):
        rv_ref[k] = jnp.broadcast_to(rvi_ref[k], (tall, w))
    at_south = pole_at_ref[0] == 1
    at_north = pole_at_ref[1] == 1
    for f in range(nf):
        for lev in range(nlev):
            for k in range(halo):
                mirrored = pole_ref[f, lev, pl.ds(halo - 1 - k, 1)]
                if f == 2:
                    mirrored = -mirrored
                row = pl.ds(k, 1)
                south_ref[f, lev, row] = jnp.where(at_south, mirrored, fs_ref[f, lev, row])
                north_ref[f, lev, row] = jnp.where(at_north, mirrored, fn_ref[f, lev, row])
    zeros = jnp.zeros((halo, w), jnp.float32)
    for s in range(nslab):
        for f in range(nf):
            e_ref[s, f, pl.ds(0, halo)] = _pack_own(lambda lev: south_ref[f, lev], nlev, halo, w, s, zeros)
            e_ref[s, f, pl.ds(halo, rows)] = inner_ref[s, f]
            e_ref[s, f, pl.ds(halo + rows, halo)] = _pack_own(lambda lev: north_ref[f, lev], nlev, halo, w, s, zeros)


def _main_kernel(
    south_ref, thk_ref, wind_ref, trc_ref, north_ref, tall_ref, sall_ref, nall_ref, rv_ref,
    thk_o, wind_o, trc_o, p_ref, mf_ref, sp_ref, s1_ref,
):
    nf, _, halo, w = south_ref.shape
    nlev, rows = tall_ref.shape[0], tall_ref.shape[1]
    i = pl.program_id(0)
    tall = rows + 2 * halo
    win = pl.ds(MARGIN, tall)
    top = pl.ds(MARGIN, halo)
    mid = pl.ds(MARGIN + halo, rows)
    bot = pl.ds(MARGIN + halo + rows, halo)
    rv = (rv_ref[0], rv_ref[1], rv_ref[2])

    @pl.when(i == 0)
    def _():
        acc = None
        for l in reversed(range(nlev)):
            part = (sall_ref[0, l], tall_ref[l], nall_ref[0, l])
            acc = part if acc is None else tuple(x + y for x, y in zip(acc, part))
            p_ref[l, top] = GRAV * acc[0]
            p_ref[l, mid] = GRAV * acc[1]
            p_ref[l, bot] = GRAV * acc[2]

    @pl.when(i < nlev)
    def _():
        lev = i
        for f in range(nf):
            sp_ref[f, top] = south_ref[f, 0]
            if f == 0:
                sp_ref[f, mid] = thk_ref[0]
            elif f < 3:
                sp_ref[f, mid] = wind_ref[f - 1, 0]
            else:
                sp_ref[f, mid] = trc_ref[f - 3, 0]
            sp_ref[f, bot] = north_ref[f, 0]

        def store(f, x):
            s1_ref[f, lev, win] = x

        _substep(
            lambda f, d: sp_ref[f, pl.ds(MARGIN + d, tall)],
            store,
            nf,
            lambda d: p_ref[lev, pl.ds(MARGIN + d, tall)],
            rv,
            mf_ref,
        )

    @pl.when(i == nlev)
    def _():
        acc = None
        for l in reversed(range(nlev)):
            acc = s1_ref[0, l, win] if acc is None else acc + s1_ref[0, l, win]
            p_ref[l, win] = GRAV * acc

    @pl.when(i >= nlev)
    def _():
        lev = i - nlev

        def store(f, x):
            sp_ref[f, win] = x
            x = sp_ref[f, mid]
            if f == 0:
                thk_o[0] = x
            elif f < 3:
                wind_o[f - 1, 0] = x
            else:
                trc_o[f - 3, 0] = x

        _substep(
            lambda f, d: s1_ref[f, lev, pl.ds(MARGIN + d, tall)],
            store,
            nf,
            lambda d: p_ref[lev, pl.ds(MARGIN + d, tall)],
            rv,
            mf_ref,
        )


def _final_kernel(
    e_ref, ew_ref, ee_ref, rv_ref, thk_h, wind_h, trc_h, thk_oh, wind_oh, trc_oh, g0_ref, g1_ref, pg_ref, mf_ref,
    thk_i, wind_i, trc_i, sem,
):
    nslab, nf, tall, w = e_ref.shape
    nlev, rows = thk_i.shape[0], thk_i.shape[1]
    ins = [pltpu.make_async_copy(h, v, sem.at[k]) for k, (h, v) in enumerate(zip((thk_h, wind_h, trc_h), (thk_i, wind_i, trc_i)))]
    for c in ins:
        c.start()
    thk_o, wind_o, trc_o = thk_i, wind_i, trc_i
    per = w // GW
    rv = (rv_ref[0], rv_ref[1], rv_ref[2])
    lane, group, kk = _lanes(tall, w)
    win = pl.ds(MARGIN, tall)
    for s in range(nslab):
        for f in range(nf):
            g0_ref[s, f, win] = jnp.where(
                kk < HALO,
                _lroll(ew_ref[s, f], -4 * HALO),
                jnp.where(kk >= 5 * HALO, _lroll(ee_ref[s, f], 4 * HALO), e_ref[s, f]),
            )
    for src, dst in ((g0_ref, g1_ref), (g1_ref, g0_ref)):
        _packed_potential([src[s, 0, win] for s in range(nslab)], nlev, w, pg_ref, tall)
        for s in range(nslab):

            def store(f, x, s=s, dst=dst):
                dst[s, f, win] = x

            _substep(
                lambda f, d, s=s, src=src: src[s, f, pl.ds(MARGIN + d, tall)],
                store,
                nf,
                lambda d, s=s: pg_ref[s, pl.ds(MARGIN + d, tall)],
                rv,
                mf_ref,
            )
    lane_o = lane[:rows]
    inner = pl.ds(MARGIN + HALO, rows)
    for c in ins:
        c.wait()
    for lev in range(nlev):
        s, g = _slab_of(lev, per)
        for f in range(nf):
            strip = g0_ref[s, f, inner]
            lo = _lroll(strip, -(GW * g + HALO))
            hi = _lroll(strip, (w - HALO) - (GW * g + 4 * HALO))
            if f == 0:
                src, dst = thk_i.at[lev], thk_o.at[lev]
            elif f < 3:
                src, dst = wind_i.at[f - 1, lev], wind_o.at[f - 1, lev]
            else:
                src, dst = trc_i.at[f - 3, lev], trc_o.at[f - 3, lev]
            dst[...] = jnp.where(lane_o < HALO, lo, jnp.where(lane_o >= w - HALO, hi, src[...]))
    outs = [pltpu.make_async_copy(v, h, sem.at[3 + k]) for k, (v, h) in enumerate(zip((thk_i, wind_i, trc_i), (thk_oh, wind_oh, trc_oh)))]
    for c in outs:
        c.start()
    for c in outs:
        c.wait()


def _shift_pairs(n, d, closed):
    return [(i, (i + d) % n) for i in range(n) if closed or 0 <= i + d < n]


def _vmem_call(kernel, out_shape, n_in, scratch, flops, nbytes):
    vmem = pl.BlockSpec(memory_space=pltpu.VMEM)
    return pl.pallas_call(
        kernel,
        out_shape=out_shape,
        in_specs=[vmem] * n_in,
        out_specs=tuple(vmem for _ in out_shape) if isinstance(out_shape, tuple) else vmem,
        scratch_shapes=scratch,
        cost_estimate=pl.CostEstimate(flops=flops, bytes_accessed=nbytes, transcendentals=0),
    )


def shards(thickness, winds, tracer_mass):
    fields = jnp.concatenate([thickness[None], winds, tracer_mass], 0)
    nf, nlev, rows, w = fields.shape
    nlat = lax.axis_size("lat")
    nlon = lax.axis_size("lon")
    band = lax.axis_index("lat")
    spacing = math.pi / (rows * nlat)
    tall = rows + 2 * HALO
    deep = tall + 2 * MARGIN
    per = w // GW
    nslab = -(-nlev // per)

    row_index = (jnp.arange(tall) + (band * rows - HALO)).astype(jnp.float32)
    center_lat = (row_index + 0.5) * spacing - 0.5 * math.pi
    face_lat = (row_index + 1.0) * spacing - 0.5 * math.pi
    center_cos = jnp.cos(center_lat)
    rowvec = jnp.stack(
        [
            jnp.abs(jnp.cos(face_lat)),
            1.0 / jnp.abs(center_cos),
            COUR * FCOR * jnp.sin(center_lat) * jnp.where(center_cos >= 0.0, 1.0, -1.0),
        ]
    )
    rowvec = rowvec[:, :, None]

    inner_edges = _vmem_call(
        _edge_inner_kernel, jax.ShapeDtypeStruct((nslab, nf, rows, w), jnp.float32), 3, [], 0, nf * nlev * rows * w * 4
    )(thickness, winds, tracer_mass)

    top = fields[:, :, rows - HALO :]
    bottom = fields[:, :, :HALO]
    from_south = lax.ppermute(top, "lat", _shift_pairs(nlat, 1, False))
    from_north = lax.ppermute(bottom, "lat", _shift_pairs(nlat, -1, False))
    half = nlon // 2
    pole_pairs = []
    for b in (0, nlat - 1):
        for s in range(nlon):
            pole_pairs.append((b * nlon + s, b * nlon + (s + half) % nlon))
    pole_out = jnp.where(band == 0, bottom, top)
    pole_in = lax.ppermute(pole_out, ("lat", "lon"), pole_pairs)
    pole_at = jnp.stack([band == 0, band == nlat - 1]).astype(jnp.int32)

    slab = nf * tall * w * 4
    vmem = pl.BlockSpec(memory_space=pltpu.VMEM)
    edges, south, north, rowvec = pl.pallas_call(
        _edge_kernel,
        out_shape=(
            jax.ShapeDtypeStruct((nslab, nf, tall, w), jnp.float32),
            jax.ShapeDtypeStruct(top.shape, jnp.float32),
            jax.ShapeDtypeStruct(top.shape, jnp.float32),
            jax.ShapeDtypeStruct((3, tall, w), jnp.float32),
        ),
        in_specs=[pl.BlockSpec(memory_space=pltpu.SMEM)] + [vmem] * 5,
        out_specs=(vmem, vmem, vmem, vmem),
        cost_estimate=pl.CostEstimate(flops=0, bytes_accessed=2 * slab * nslab, transcendentals=0),
    )(pole_at, from_south, from_north, pole_in, inner_edges, rowvec)
    from_west = lax.ppermute(edges, "lon", _shift_pairs(nlon, 1, True))
    from_east = lax.ppermute(edges, "lon", _shift_pairs(nlon, -1, True))

    step_flops = 60 * nf * nlev * tall * w
    first = lambda i: jnp.minimum(i, nlev - 1)
    second = lambda i: jnp.maximum(i - nlev, 0)
    raw = pl.pallas_call(
        _main_kernel,
        out_shape=(
            jax.ShapeDtypeStruct(thickness.shape, jnp.float32),
            jax.ShapeDtypeStruct(winds.shape, jnp.float32),
            jax.ShapeDtypeStruct(tracer_mass.shape, jnp.float32),
        ),
        grid=(2 * nlev,),
        in_specs=[
            pl.BlockSpec((nf, 1, HALO, w), lambda i: (0, first(i), 0, 0)),
            pl.BlockSpec((1, rows, w), lambda i: (first(i), 0, 0)),
            pl.BlockSpec((2, 1, rows, w), lambda i: (0, first(i), 0, 0)),
            pl.BlockSpec((nf - 3, 1, rows, w), lambda i: (0, first(i), 0, 0)),
            pl.BlockSpec((nf, 1, HALO, w), lambda i: (0, first(i), 0, 0)),
            pl.BlockSpec((nlev, rows, w), lambda i: (0, 0, 0)),
            pl.BlockSpec((1, nlev, HALO, w), lambda i: (0, 0, 0, 0)),
            pl.BlockSpec((1, nlev, HALO, w), lambda i: (0, 0, 0, 0)),
            pl.BlockSpec((3, tall, w), lambda i: (0, 0, 0)),
        ],
        out_specs=(
            pl.BlockSpec((1, rows, w), lambda i: (second(i), 0, 0)),
            pl.BlockSpec((2, 1, rows, w), lambda i: (0, second(i), 0, 0)),
            pl.BlockSpec((nf - 3, 1, rows, w), lambda i: (0, second(i), 0, 0)),
        ),
        scratch_shapes=[
            pltpu.VMEM((nlev, deep, w), jnp.float32),
            pltpu.VMEM((nf, deep, w), jnp.float32),
            pltpu.VMEM((nf, deep, w), jnp.float32),
            pltpu.VMEM((nf, nlev, deep, w), jnp.float32),
        ],
        compiler_params=pltpu.CompilerParams(dimension_semantics=("arbitrary",)),
        cost_estimate=pl.CostEstimate(flops=2 * step_flops, bytes_accessed=2 * slab * nlev, transcendentals=0),
    )(south, thickness, winds, tracer_mass, north, thickness, south, north, rowvec)

    vmem = pl.BlockSpec(memory_space=pltpu.VMEM)
    anywhere = pl.BlockSpec(memory_space=pl.ANY)
    return pl.pallas_call(
        _final_kernel,
        out_shape=(
            jax.ShapeDtypeStruct(thickness.shape, jnp.float32),
            jax.ShapeDtypeStruct(winds.shape, jnp.float32),
            jax.ShapeDtypeStruct(tracer_mass.shape, jnp.float32),
        ),
        in_specs=[vmem] * 4 + [anywhere] * 3,
        out_specs=(anywhere, anywhere, anywhere),
        input_output_aliases={4: 0, 5: 1, 6: 2},
        scratch_shapes=[
            pltpu.VMEM((nslab, nf, deep, w), jnp.float32),
            pltpu.VMEM((nslab, nf, deep, w), jnp.float32),
            pltpu.VMEM((nslab, deep, w), jnp.float32),
            pltpu.VMEM((nf, deep, w), jnp.float32),
            pltpu.VMEM(thickness.shape, jnp.float32),
            pltpu.VMEM(winds.shape, jnp.float32),
            pltpu.VMEM(tracer_mass.shape, jnp.float32),
            pltpu.SemaphoreType.DMA((6,)),
        ],
        cost_estimate=pl.CostEstimate(flops=4 * step_flops // nlev, bytes_accessed=4 * slab * nslab, transcendentals=0),
    )(edges, from_west, from_east, rowvec, *raw)


def solution(mesh):
    return jax.shard_map(
        shards,
        mesh=mesh,
        in_specs=(P(None, "lat", "lon"), P(None, None, "lat", "lon"), P(None, None, "lat", "lon")),
        out_specs=(P(None, "lat", "lon"), P(None, None, "lat", "lon"), P(None, None, "lat", "lon")),
        check_vma=False,
    )
```

```python
import math

import jax
import jax.numpy as jnp
from jax import lax
from jax.experimental import pallas as pl
from jax.experimental.pallas import tpu as pltpu
from jax.sharding import PartitionSpec as P

SUBSTEPS = 2
COUR = 0.25
GRAV = 1.0
FCOR = 1.0

HALO = 2 * SUBSTEPS
GW = 6 * HALO
MARGIN = 8


def _lroll(x, k):
    n = x.shape[-1]
    return pltpu.roll(x, k % n, x.ndim - 1)


def _face(pos, behind, centre, forward, beyond):
    p = jnp.where(pos, centre, forward)
    q = jnp.where(pos, forward, centre)
    r = jnp.where(pos, behind, beyond)
    return 5.0 * p + 2.0 * q - r


def _substep(load, store, nf, pot, rv, mf_ref):
    fcos, inv_acos, cor = rv
    u = load(1, 0)
    v = load(2, 0)
    n = u.shape[0]
    fs = (COUR * 0.5 / 6.0) * (u + _lroll(u, -1))
    ms = (COUR * 0.5 / 6.0) * (v + load(2, 1)) * fcos
    fpos = fs >= 0.0
    mpos = ms >= 0.0
    for f in range(nf):
        x = u if f == 1 else (v if f == 2 else load(f, 0))
        zf = fs * _face(fpos, _lroll(x, 1), x, _lroll(x, -1), _lroll(x, -2))
        mf = ms * _face(mpos, load(f, -1), x, load(f, 1), load(f, 2))
        mf_ref[f, pl.ds(MARGIN, n)] = mf
        new = x - (zf - _lroll(zf, 1)) - (mf - mf_ref[f, pl.ds(MARGIN - 1, n)]) * inv_acos
        if f == 1:
            p0 = pot(0)
            new = new - COUR * 0.5 * (_lroll(p0, -1) - _lroll(p0, 1)) + cor * v
        elif f == 2:
            new = new - COUR * 0.5 * (pot(1) - pot(-1)) - cor * u
        store(f, new)


def _slab_of(lev, per):
    return lev // per, lev % per


def _lanes(rows, w):
    lane = lax.broadcasted_iota(jnp.int32, (rows, w), 1)
    return lane, lane // GW, lane % GW


def _pack_own(get, nlev, rows, w, slab, init):
    per = w // GW
    lane, group, kk = _lanes(rows, w)
    lo_mask = (kk >= HALO) & (kk < 3 * HALO)
    hi_mask = (kk >= 3 * HALO) & (kk < 5 * HALO)
    g = init
    for lev in range(slab * per, min(nlev, (slab + 1) * per)):
        m = get(lev)
        base = GW * (lev - slab * per)
        g = jnp.where((group == lev - slab * per) & lo_mask, _lroll(m, base + HALO), g)
        g = jnp.where((group == lev - slab * per) & hi_mask, _lroll(m, base + 3 * HALO - (w - 2 * HALO)), g)
    return g


def _packed_potential(h, nlev, w, pg_ref, n):
    per = w // GW
    nslab = len(h)
    _, group, _ = _lanes(n, w)
    below = None
    for s in reversed(range(nslab)):
        ng = min(per, nlev - s * per)
        acc = h[s]
        k = 1
        while k < ng:
            acc = acc + jnp.where(group + k < ng, _lroll(acc, -GW * k), 0.0)
            k *= 2
        if below is not None:
            spread = below
            for g in range(1, ng):
                spread = jnp.where(group == g, _lroll(below, GW * g), spread)
            acc = acc + spread
        pg_ref[s, pl.ds(MARGIN, n)] = GRAV * acc
        below = jnp.where(group == 0, acc, 0.0)


def _edge_inner_kernel(thk_ref, wind_ref, trc_ref, e_ref):
    nlev, rows, w = thk_ref.shape
    nslab, nf = e_ref.shape[0], e_ref.shape[1]
    zeros = jnp.zeros((rows, w), jnp.float32)
    for s in range(nslab):
        for f in range(nf):
            if f == 0:
                get = lambda lev: thk_ref[lev]
            elif f < 3:
                get = lambda lev, f=f: wind_ref[f - 1, lev]
            else:
                get = lambda lev, f=f: trc_ref[f - 3, lev]
            e_ref[s, f] = _pack_own(get, nlev, rows, w, s, zeros)


def _edge_kernel(fs_ref, fn_ref, pole_ref, inner_ref, rvi_ref, e_ref, south_ref, north_ref, rv_ref):
    nf, nlev, halo, w = fs_ref.shape
    nslab, rows = inner_ref.shape[0], inner_ref.shape[2]
    tall = rv_ref.shape[1]
    for k in range(rv_ref.shape[0]):
        rv_ref[k] = jnp.broadcast_to(rvi_ref[k], (tall, w))
    band = lax.axis_index("lat")
    at_south = band == 0
    at_north = band == lax.axis_size("lat") - 1
    for f in range(nf):
        for lev in range(nlev):
            for k in range(halo):
                mirrored = pole_ref[f, lev, pl.ds(halo - 1 - k, 1)]
                if f == 2:
                    mirrored = -mirrored
                row = pl.ds(k, 1)
                south_ref[f, lev, row] = jnp.where(at_south, mirrored, fs_ref[f, lev, row])
                north_ref[f, lev, row] = jnp.where(at_north, mirrored, fn_ref[f, lev, row])
    zeros = jnp.zeros((halo, w), jnp.float32)
    for s in range(nslab):
        for f in range(nf):
            e_ref[s, f, pl.ds(0, halo)] = _pack_own(lambda lev: south_ref[f, lev], nlev, halo, w, s, zeros)
            e_ref[s, f, pl.ds(halo, rows)] = inner_ref[s, f]
            e_ref[s, f, pl.ds(halo + rows, halo)] = _pack_own(lambda lev: north_ref[f, lev], nlev, halo, w, s, zeros)


def _main_kernel(
    south_ref, thk_ref, wind_ref, trc_ref, north_ref, tall_ref, sall_ref, nall_ref, rv_ref,
    thk_o, wind_o, trc_o, p_ref, mf_ref, sp_ref, s1_ref,
):
    nf, _, halo, w = south_ref.shape
    nlev, rows = tall_ref.shape[0], tall_ref.shape[1]
    i = pl.program_id(0)
    tall = rows + 2 * halo
    win = pl.ds(MARGIN, tall)
    top = pl.ds(MARGIN, halo)
    mid = pl.ds(MARGIN + halo, rows)
    bot = pl.ds(MARGIN + halo + rows, halo)
    rv = (rv_ref[0], rv_ref[1], rv_ref[2])

    @pl.when(i == 0)
    def _():
        acc = None
        for l in reversed(range(nlev)):
            part = (sall_ref[0, l], tall_ref[l], nall_ref[0, l])
            acc = part if acc is None else tuple(x + y for x, y in zip(acc, part))
            p_ref[l, top] = GRAV * acc[0]
            p_ref[l, mid] = GRAV * acc[1]
            p_ref[l, bot] = GRAV * acc[2]

    @pl.when(i < nlev)
    def _():
        lev = i
        for f in range(nf):
            sp_ref[f, top] = south_ref[f, 0]
            if f == 0:
                sp_ref[f, mid] = thk_ref[0]
            elif f < 3:
                sp_ref[f, mid] = wind_ref[f - 1, 0]
            else:
                sp_ref[f, mid] = trc_ref[f - 3, 0]
            sp_ref[f, bot] = north_ref[f, 0]

        def store(f, x):
            s1_ref[f, lev, win] = x

        _substep(
            lambda f, d: sp_ref[f, pl.ds(MARGIN + d, tall)],
            store,
            nf,
            lambda d: p_ref[lev, pl.ds(MARGIN + d, tall)],
            rv,
            mf_ref,
        )

    @pl.when(i == nlev)
    def _():
        acc = None
        for l in reversed(range(nlev)):
            acc = s1_ref[0, l, win] if acc is None else acc + s1_ref[0, l, win]
            p_ref[l, win] = GRAV * acc

    @pl.when(i >= nlev)
    def _():
        lev = i - nlev

        def store(f, x):
            x = x[halo : halo + rows]
            if f == 0:
                thk_o[0] = x
            elif f < 3:
                wind_o[f - 1, 0] = x
            else:
                trc_o[f - 3, 0] = x

        _substep(
            lambda f, d: s1_ref[f, lev, pl.ds(MARGIN + d, tall)],
            store,
            nf,
            lambda d: p_ref[lev, pl.ds(MARGIN + d, tall)],
            rv,
            mf_ref,
        )


def _final_kernel(
    e_ref, ew_ref, ee_ref, rv_ref, thk_h, wind_h, trc_h, thk_oh, wind_oh, trc_oh, g0_ref, g1_ref, pg_ref, mf_ref,
    thk_i, wind_i, trc_i, sem,
):
    nslab, nf, tall, w = e_ref.shape
    nlev, rows = thk_i.shape[0], thk_i.shape[1]
    ins = [pltpu.make_async_copy(h, v, sem.at[k]) for k, (h, v) in enumerate(zip((thk_h, wind_h, trc_h), (thk_i, wind_i, trc_i)))]
    for c in ins:
        c.start()
    thk_o, wind_o, trc_o = thk_i, wind_i, trc_i
    per = w // GW
    rv = (rv_ref[0], rv_ref[1], rv_ref[2])
    lane, group, kk = _lanes(tall, w)
    win = pl.ds(MARGIN, tall)
    for s in range(nslab):
        for f in range(nf):
            g0_ref[s, f, win] = jnp.where(
                kk < HALO,
                _lroll(ew_ref[s, f], -4 * HALO),
                jnp.where(kk >= 5 * HALO, _lroll(ee_ref[s, f], 4 * HALO), e_ref[s, f]),
            )
    for src, dst in ((g0_ref, g1_ref), (g1_ref, g0_ref)):
        _packed_potential([src[s, 0, win] for s in range(nslab)], nlev, w, pg_ref, tall)
        for s in range(nslab):

            def store(f, x, s=s, dst=dst):
                dst[s, f, win] = x

            _substep(
                lambda f, d, s=s, src=src: src[s, f, pl.ds(MARGIN + d, tall)],
                store,
                nf,
                lambda d, s=s: pg_ref[s, pl.ds(MARGIN + d, tall)],
                rv,
                mf_ref,
            )
    lane_o = lane[:rows]
    inner = pl.ds(MARGIN + HALO, rows)
    for c in ins:
        c.wait()
    for lev in range(nlev):
        s, g = _slab_of(lev, per)
        for f in range(nf):
            strip = g0_ref[s, f, inner]
            lo = _lroll(strip, -(GW * g + HALO))
            hi = _lroll(strip, (w - HALO) - (GW * g + 4 * HALO))
            if f == 0:
                src, dst = thk_i.at[lev], thk_o.at[lev]
            elif f < 3:
                src, dst = wind_i.at[f - 1, lev], wind_o.at[f - 1, lev]
            else:
                src, dst = trc_i.at[f - 3, lev], trc_o.at[f - 3, lev]
            dst[...] = jnp.where(lane_o < HALO, lo, jnp.where(lane_o >= w - HALO, hi, src[...]))
    outs = [pltpu.make_async_copy(v, h, sem.at[3 + k]) for k, (v, h) in enumerate(zip((thk_i, wind_i, trc_i), (thk_oh, wind_oh, trc_oh)))]
    for c in outs:
        c.start()
    for c in outs:
        c.wait()


def _shift_pairs(n, d, closed):
    return [(i, (i + d) % n) for i in range(n) if closed or 0 <= i + d < n]


def _vmem_call(kernel, out_shape, n_in, scratch, flops, nbytes):
    vmem = pl.BlockSpec(memory_space=pltpu.VMEM)
    return pl.pallas_call(
        kernel,
        out_shape=out_shape,
        in_specs=[vmem] * n_in,
        out_specs=tuple(vmem for _ in out_shape) if isinstance(out_shape, tuple) else vmem,
        scratch_shapes=scratch,
        cost_estimate=pl.CostEstimate(flops=flops, bytes_accessed=nbytes, transcendentals=0),
    )


def shards(thickness, winds, tracer_mass):
    fields = jnp.concatenate([thickness[None], winds, tracer_mass], 0)
    nf, nlev, rows, w = fields.shape
    nlat = lax.axis_size("lat")
    nlon = lax.axis_size("lon")
    band = lax.axis_index("lat")
    spacing = math.pi / (rows * nlat)
    tall = rows + 2 * HALO
    deep = tall + 2 * MARGIN
    per = w // GW
    nslab = -(-nlev // per)

    row_index = (jnp.arange(tall) + (band * rows - HALO)).astype(jnp.float32)
    center_lat = (row_index + 0.5) * spacing - 0.5 * math.pi
    face_lat = (row_index + 1.0) * spacing - 0.5 * math.pi
    center_cos = jnp.cos(center_lat)
    rowvec = jnp.stack(
        [
            jnp.abs(jnp.cos(face_lat)),
            1.0 / jnp.abs(center_cos),
            COUR * FCOR * jnp.sin(center_lat) * jnp.where(center_cos >= 0.0, 1.0, -1.0),
        ]
    )
    rowvec = rowvec[:, :, None]

    inner_edges = _vmem_call(
        _edge_inner_kernel, jax.ShapeDtypeStruct((nslab, nf, rows, w), jnp.float32), 3, [], 0, nf * nlev * rows * w * 4
    )(thickness, winds, tracer_mass)

    top = fields[:, :, rows - HALO :]
    bottom = fields[:, :, :HALO]
    from_south = lax.ppermute(top, "lat", _shift_pairs(nlat, 1, False))
    from_north = lax.ppermute(bottom, "lat", _shift_pairs(nlat, -1, False))
    half = nlon // 2
    pole_pairs = []
    for b in (0, nlat - 1):
        for s in range(nlon):
            pole_pairs.append((b * nlon + s, b * nlon + (s + half) % nlon))
    pole_out = jnp.where(band == 0, bottom, top)
    pole_in = lax.ppermute(pole_out, ("lat", "lon"), pole_pairs)
    slab = nf * tall * w * 4
    vmem = pl.BlockSpec(memory_space=pltpu.VMEM)
    edges, south, north, rowvec = pl.pallas_call(
        _edge_kernel,
        out_shape=(
            jax.ShapeDtypeStruct((nslab, nf, tall, w), jnp.float32),
            jax.ShapeDtypeStruct(top.shape, jnp.float32),
            jax.ShapeDtypeStruct(top.shape, jnp.float32),
            jax.ShapeDtypeStruct((3, tall, w), jnp.float32),
        ),
        in_specs=[vmem] * 5,
        out_specs=(vmem, vmem, vmem, vmem),
        cost_estimate=pl.CostEstimate(flops=0, bytes_accessed=2 * slab * nslab, transcendentals=0),
    )(from_south, from_north, pole_in, inner_edges, rowvec)
    from_west = lax.ppermute(edges, "lon", _shift_pairs(nlon, 1, True))
    from_east = lax.ppermute(edges, "lon", _shift_pairs(nlon, -1, True))

    step_flops = 60 * nf * nlev * tall * w
    first = lambda i: jnp.minimum(i, nlev - 1)
    second = lambda i: jnp.maximum(i - nlev, 0)
    raw = pl.pallas_call(
        _main_kernel,
        out_shape=(
            jax.ShapeDtypeStruct(thickness.shape, jnp.float32),
            jax.ShapeDtypeStruct(winds.shape, jnp.float32),
            jax.ShapeDtypeStruct(tracer_mass.shape, jnp.float32),
        ),
        grid=(2 * nlev,),
        in_specs=[
            pl.BlockSpec((nf, 1, HALO, w), lambda i: (0, first(i), 0, 0)),
            pl.BlockSpec((1, rows, w), lambda i: (first(i), 0, 0)),
            pl.BlockSpec((2, 1, rows, w), lambda i: (0, first(i), 0, 0)),
            pl.BlockSpec((nf - 3, 1, rows, w), lambda i: (0, first(i), 0, 0)),
            pl.BlockSpec((nf, 1, HALO, w), lambda i: (0, first(i), 0, 0)),
            pl.BlockSpec((nlev, rows, w), lambda i: (0, 0, 0)),
            pl.BlockSpec((1, nlev, HALO, w), lambda i: (0, 0, 0, 0)),
            pl.BlockSpec((1, nlev, HALO, w), lambda i: (0, 0, 0, 0)),
            pl.BlockSpec((3, tall, w), lambda i: (0, 0, 0)),
        ],
        out_specs=(
            pl.BlockSpec((1, rows, w), lambda i: (second(i), 0, 0)),
            pl.BlockSpec((2, 1, rows, w), lambda i: (0, second(i), 0, 0)),
            pl.BlockSpec((nf - 3, 1, rows, w), lambda i: (0, second(i), 0, 0)),
        ),
        scratch_shapes=[
            pltpu.VMEM((nlev, deep, w), jnp.float32),
            pltpu.VMEM((nf, deep, w), jnp.float32),
            pltpu.VMEM((nf, deep, w), jnp.float32),
            pltpu.VMEM((nf, nlev, deep, w), jnp.float32),
        ],
        compiler_params=pltpu.CompilerParams(dimension_semantics=("arbitrary",)),
        cost_estimate=pl.CostEstimate(flops=2 * step_flops, bytes_accessed=2 * slab * nlev, transcendentals=0),
    )(south, thickness, winds, tracer_mass, north, thickness, south, north, rowvec)

    vmem = pl.BlockSpec(memory_space=pltpu.VMEM)
    anywhere = pl.BlockSpec(memory_space=pl.ANY)
    return pl.pallas_call(
        _final_kernel,
        out_shape=(
            jax.ShapeDtypeStruct(thickness.shape, jnp.float32),
            jax.ShapeDtypeStruct(winds.shape, jnp.float32),
            jax.ShapeDtypeStruct(tracer_mass.shape, jnp.float32),
        ),
        in_specs=[vmem] * 4 + [anywhere] * 3,
        out_specs=(anywhere, anywhere, anywhere),
        input_output_aliases={4: 0, 5: 1, 6: 2},
        scratch_shapes=[
            pltpu.VMEM((nslab, nf, deep, w), jnp.float32),
            pltpu.VMEM((nslab, nf, deep, w), jnp.float32),
            pltpu.VMEM((nslab, deep, w), jnp.float32),
            pltpu.VMEM((nf, deep, w), jnp.float32),
            pltpu.VMEM(thickness.shape, jnp.float32),
            pltpu.VMEM(winds.shape, jnp.float32),
            pltpu.VMEM(tracer_mass.shape, jnp.float32),
            pltpu.SemaphoreType.DMA((6,)),
        ],
        cost_estimate=pl.CostEstimate(flops=4 * step_flops // nlev, bytes_accessed=4 * slab * nslab, transcendentals=0),
    )(edges, from_west, from_east, rowvec, *raw)


def solution(mesh):
    return jax.shard_map(
        shards,
        mesh=mesh,
        in_specs=(P(None, "lat", "lon"), P(None, None, "lat", "lon"), P(None, None, "lat", "lon")),
        out_specs=(P(None, "lat", "lon"), P(None, None, "lat", "lon"), P(None, None, "lat", "lon")),
        check_vma=False,
    )
```
